32 devices in a mesh: pages: 8 (over y, x, core), mp: 4 (over z).
Axes of the slice: x: 2, y: 2, z: 4, core: 2. Of those that a mesh axis runs over, the one named last changes fastest.
Arguments:
- hidden_in: bfloat16 [2048, 1280], P('pages'), may hold values from -240 to 240
- w_qkv: bfloat16 [3, 1280, 1280], P(None, None, 'mp'), may hold values from -0.15625 to 0.15625
- w_out: bfloat16 [1280, 1280], replicated, may hold values from -0.15625 to 0.15625
- w_gate_up: bfloat16 [2, 1280, 5120], P(None, None, 'mp'), may hold values from -0.15625 to 0.15625
- w_down: bfloat16 [5120, 1280], P('mp'), may hold values from -0.078125 to 0.078125
- scale_qk: float32 [1280], replicated, may hold values from 0.4 to 1.6
- scale_gate_up: float32 [2, 5120], P(None, 'mp'), may hold values from 0.5 to 2
- eigen_rates: float32 [2, 1280], replicated, may hold values from 0.1 to 1
- cache_keys: bfloat16 [32, 128, 1280], P('pages'), may hold values from -6 to 6
- cache_values: bfloat16 [32, 128, 1280], P('pages'), may hold values from -6 to 6
- page_table: int32 [32], replicated, may hold values from 0 to 31, as said below
- request_group: int32 [8, 4], replicated, may hold values from 0 to 7
- suffix_len: int32 [8, 4], replicated, may hold values from 1 to 253, as said below
Outputs:
- hidden_out: bfloat16 [2048, 1280], P(('pages', 'mp'))
The draws below stay inside these ranges and needn't reach their ends.
Inputs may be any that keep to these rules, and one draw needn't show every extreme that they name: `suffix_len`: the 4 lengths of one index of pages sum to at least 153 and at most 256, and to exactly 256 for at least one index. `page_table`: A permutation of the pool pages; the 4 pool pages of one index of pages hold prefix pages of 4 different groups.
All inputs are finite; a program needn't handle non-finite values.
Results may differ from the reference program's by a relative error of at most 0.013.
Values may be sent and summed in bfloat16 or wider, within the bound.
No kernel may reach another device: no remote copies, remote signals or barrier semaphores. Data moves between devices by JAX's collectives and lax.ppermute only.
A program may use at most 128 MiB of HBM per device.

```python
import math
import jax
import jax.numpy as jnp
from jax import lax

D = 1280
HEADS = 20
FF = 5120
GROUPS = 8
PAGE = 128
REQ_DEV = 4
PAGES_DEV = 4
SLOTS = 256
SHARDS = 8
POOL = 32
PREFIX_PAGES = 4
TOKENS = 2048


def draw_hidden_in(key, part):
    key_base, key_cols, key_rows = jax.random.split(key, 3)
    column_scale = jnp.exp(jax.random.uniform(key_cols, (D,), jnp.float32, 0.0, math.log(10.0)))
    row_scale = jnp.exp(jax.random.uniform(key_rows, (TOKENS, 1), jnp.float32, 0.0, math.log(4.0)))
    base = jax.random.truncated_normal(key_base, -6.0, 6.0, (TOKENS, D), jnp.float32)
    return (base * column_scale[None, :] * row_scale).astype(jnp.bfloat16)


def draw_page_table(key, part):
    key_groups, key_within, key_devices = jax.random.split(jax.random.fold_in(key, 17), 3)
    group_perm = jax.random.permutation(key_groups, GROUPS).astype(jnp.int32)
    within_keys = jax.random.split(key_within, GROUPS)
    within = jax.vmap(lambda one_key: jax.random.permutation(one_key, PREFIX_PAGES))(within_keys).astype(jnp.int32)
    device_perm = jax.random.permutation(key_devices, SHARDS).astype(jnp.int32)
    ordering = within * GROUPS + group_perm[:, None]
    physical = device_perm[ordering // PAGES_DEV] * PAGES_DEV + ordering % PAGES_DEV
    return physical.reshape(POOL).astype(jnp.int32)


def draw_suffix_len(key, part):
    key_totals, key_full, key_shares = jax.random.split(key, 3)
    totals = jax.random.randint(key_totals, (SHARDS,), 3 * SLOTS // 5, SLOTS + 1)
    full_index = jax.random.randint(key_full, (), 0, SHARDS)
    totals = jnp.where(jnp.arange(SHARDS, dtype=jnp.int32) == full_index, SLOTS, totals)
    shares = jax.random.randint(key_shares, (SHARDS, REQ_DEV), 1, 9)
    spare = totals - REQ_DEV
    portion = 1 + spare[:, None] * shares // jnp.sum(shares, axis=1, keepdims=True)
    leading = portion[:, :-1]
    closing = totals - jnp.sum(leading, axis=1)
    lengths = jnp.concatenate([leading, closing[:, None]], axis=1).astype(jnp.int32)
    request_ids = jnp.arange(REQ_DEV, dtype=jnp.int32)
    extreme = jnp.where(request_ids == REQ_DEV - 1, SLOTS - REQ_DEV + 1, 1).astype(jnp.int32)
    is_full = (jnp.arange(SHARDS, dtype=jnp.int32) == full_index)[:, None]
    return jnp.where(is_full, extreme[None, :], lengths).astype(jnp.int32)


def with_ends(entries, stream_key, smallest, top_value):
    index_at = [jax.random.randint(jax.random.fold_in(stream_key, axis), (), 0, length) for axis, length in enumerate(entries.shape)]
    longest = entries.shape.index(max(entries.shape))
    next_to = index_at[:longest] + [(index_at[longest] + 1) % entries.shape[longest]] + index_at[longest + 1:]
    return entries.at[tuple(index_at)].set(smallest).at[tuple(next_to)].set(top_value)


def level_of(stream_key, dims, cuts, least, top_value):
    gain = 1.0
    for dim, parts in cuts:
        steps = jax.random.uniform(jax.random.fold_in(jax.random.fold_in(stream_key, 6), dim), (parts,), jnp.float32, least / len(cuts), top_value / len(cuts))
        gain = gain * jnp.repeat(jnp.exp(steps), dims[dim] // parts).reshape((-1,) + (1,) * (len(dims) - 1 - dim))
    return gain


def noise(rng, dims, deviation, reach, cuts=(), kind=jnp.bfloat16):
    level = level_of(rng, dims, cuts, -0.22, 0.18) if cuts else 1.0
    values = jax.random.normal(rng, dims, jnp.float32) * deviation * level
    return jnp.minimum(jnp.maximum(values, -reach), reach).astype(kind)


def setup_inputs(seed: int = 0) -> dict:
    splits = jax.random.split(jax.random.key(seed), 14)
    return {
        "hidden_in": draw_hidden_in(jax.random.fold_in(splits[13], 71), 0),
        "w_qkv": noise(splits[1], (3, D, D), D ** -0.5, 0.15625, ((2, 4),)),
        "w_out": noise(splits[2], (D, D), D ** -0.5, 0.15625),
        "w_gate_up": noise(splits[3], (2, D, FF), D ** -0.5, 0.15625, ((2, 4),)),
        "w_down": noise(splits[4], (FF, D), FF ** -0.5, 0.078125, ((0, 4),)),
        "scale_qk": jnp.clip(jnp.exp(jax.random.uniform(splits[5], (D,), jnp.float32, math.log(0.4), math.log(1.6))), 0.4, 1.6),
        "scale_gate_up": jnp.clip(jnp.exp(math.log(2.0) - 1.3862944 * jax.random.uniform(splits[6], (2, FF), jnp.float32) ** level_of(splits[6], (2, FF), ((1, 4),), -0.2, 0.2)), 0.5, 2.0),
        "eigen_rates": jnp.clip(jnp.exp(jax.random.uniform(splits[7], (2, D), jnp.float32, math.log(0.1), math.log(1.0))), 0.1, 1.0),
        "cache_keys": noise(splits[8], (POOL, PAGE, D), 1.0, 6.0, ((0, 8),)),
        "cache_values": noise(splits[9], (POOL, PAGE, D), 1.0, 6.0, ((0, 8),)),
        "page_table": draw_page_table(jax.random.fold_in(splits[13], 71), 0),
        "request_group": with_ends(jax.random.randint(splits[11], (SHARDS, REQ_DEV), 0, GROUPS), jax.random.fold_in(splits[11], 1), 0, GROUPS - 1).astype(jnp.int32),
        "suffix_len": draw_suffix_len(jax.random.fold_in(splits[13], 71), 0),
    }


EPSILON = 1e-06

def rms_rows(values_in):
    return values_in * lax.rsqrt(lax.optimization_barrier(jnp.mean(values_in * values_in, axis=-1, keepdims=True)) + EPSILON)

def head_norm(values_in, scale_vec, head_count):
    row_count, model_width = values_in.shape
    per_head = values_in.reshape(row_count, head_count, model_width // head_count)
    normed = per_head * lax.rsqrt(lax.optimization_barrier(jnp.mean(per_head * per_head, axis=-1, keepdims=True)) + EPSILON)
    return normed.reshape(row_count, model_width) * scale_vec[None, :]

def rotate(values_in, position, head_count):
    row_count, model_width = values_in.shape
    head_dim = model_width // head_count
    half_dim = head_dim // 2
    frequency = jnp.exp(jnp.arange(half_dim).astype(jnp.float32) * (-2.0 * math.log(10000.0) / head_dim))
    rotation = position.astype(jnp.float32)[:, None] * frequency[None, :]
    cosine_table = jnp.cos(rotation)[:, None, :]
    sine_table = jnp.sin(rotation)[:, None, :]
    per_head = values_in.reshape(row_count, head_count, head_dim)
    lower_half = per_head[:, :, :half_dim]
    upper_half = per_head[:, :, half_dim:]
    turned = jnp.concatenate([lower_half * cosine_table - upper_half * sine_table, upper_half * cosine_table + lower_half * sine_table], axis=-1)
    return turned.reshape(row_count, model_width)

def slot_tables(suffix_len, request_group, slot_count):
    end_slots = jnp.cumsum(suffix_len, axis=1).astype(jnp.int32)
    start_slots = (end_slots - suffix_len).astype(jnp.int32)
    slot_ids = jnp.arange(slot_count).astype(jnp.int32)
    inside = (slot_ids[None, None, :] >= start_slots[:, :, None]) & (slot_ids[None, None, :] < end_slots[:, :, None])
    request_ids = jnp.arange(suffix_len.shape[1]).astype(jnp.int32)
    slot_valid = jnp.any(inside, axis=1)
    request = lax.optimization_barrier(jnp.sum(jnp.where(inside, request_ids[None, :, None], 0), axis=1)).astype(jnp.int32)
    offset = (slot_ids[None, :] - lax.optimization_barrier(jnp.sum(jnp.where(inside, start_slots[:, :, None], 0), axis=1))).astype(jnp.int32)
    group_id = jnp.where(slot_valid, lax.optimization_barrier(jnp.sum(jnp.where(inside, request_group[:, :, None], 0), axis=1)), -1).astype(jnp.int32)
    return (slot_valid, request, offset, group_id)

def reference(hidden_in, w_qkv, w_out, w_gate_up, w_down, scale_qk, scale_gate_up, eigen_rates, cache_keys, cache_values, page_table, request_group, suffix_len):
    model_width = hidden_in.shape[1]
    head_dim = model_width // HEADS
    score_scale = 1.0 / math.sqrt(head_dim)
    pool_pages, page_len = (cache_keys.shape[0], cache_keys.shape[1])
    prefix_pages = pool_pages // GROUPS
    prefix_len = prefix_pages * page_len
    slot_valid, request, offset, group_id = slot_tables(suffix_len, request_group, SLOTS)
    position = (prefix_len + offset).astype(jnp.int32).reshape(TOKENS)
    state_in = rms_rows(hidden_in.astype(jnp.float32)).astype(jnp.bfloat16)
    projected = [jnp.dot(state_in, w_qkv[which], preferred_element_type=jnp.float32).astype(jnp.bfloat16) for which in range(3)]
    queries = head_norm(rotate(projected[0].astype(jnp.float32), position, HEADS), scale_qk, HEADS).astype(jnp.bfloat16)
    keys_new = head_norm(rotate(projected[1].astype(jnp.float32), position, HEADS), scale_qk, HEADS).astype(jnp.bfloat16)
    values_new = projected[2]
    cache_norm = head_norm(cache_keys.reshape(pool_pages * page_len, model_width).astype(jnp.float32), scale_qk, HEADS).astype(jnp.bfloat16).reshape(pool_pages, page_len, model_width)
    page_rows = page_table.reshape(GROUPS, prefix_pages)

    def shard_attention(shard_items):
        query_rows, key_rows, value_rows, live_row, request_row, offset_row, groups_row = shard_items
        query_heads = query_rows.astype(jnp.float32).reshape(SLOTS, HEADS, head_dim)
        key_heads = key_rows.astype(jnp.float32).reshape(SLOTS, HEADS, head_dim)
        value_heads = value_rows.astype(jnp.float32).reshape(SLOTS, HEADS, head_dim)
        scores = jnp.einsum('qhd,khd->hqk', query_heads, key_heads) * score_scale
        allowed = (request_row[:, None] == request_row[None, :]) & (offset_row[None, :] <= offset_row[:, None]) & live_row[:, None] & live_row[None, :]
        weights = jnp.where(allowed[None], jnp.exp(scores), 0.0)
        suffix_total = lax.optimization_barrier(jnp.sum(weights, axis=-1))
        suffix_sum = jnp.einsum('hqk,khd->qhd', weights.astype(jnp.bfloat16).astype(jnp.float32), value_heads)
        pages_used = page_rows[groups_row]
        prefix_keys = cache_norm[pages_used].astype(jnp.float32).reshape(REQ_DEV, prefix_len, HEADS, head_dim)
        prefix_values = cache_values[pages_used].astype(jnp.float32).reshape(REQ_DEV, prefix_len, HEADS, head_dim)
        prefix_scores = jnp.einsum('qhd,rkhd->hqrk', query_heads, prefix_keys) * score_scale
        owner_mask = (request_row[:, None] == jnp.arange(REQ_DEV).astype(jnp.int32)[None, :]) & live_row[:, None]
        prefix_weights = jnp.where(owner_mask[None, :, :, None], jnp.exp(prefix_scores), 0.0)
        prefix_total = lax.optimization_barrier(jnp.sum(prefix_weights, axis=(2, 3)))
        prefix_sum = jnp.einsum('hqrk,rkhd->qhd', prefix_weights.astype(jnp.bfloat16).astype(jnp.float32), prefix_values)
        denominator = (suffix_total + prefix_total).T + (1.0 - live_row.astype(jnp.float32))[:, None]
        mixed = (suffix_sum + prefix_sum) / denominator[:, :, None]
        return mixed.reshape(SLOTS, model_width).astype(jnp.bfloat16)
    attention = lax.map(shard_attention, (queries.reshape(SHARDS, SLOTS, model_width), keys_new.reshape(SHARDS, SLOTS, model_width), values_new.reshape(SHARDS, SLOTS, model_width), slot_valid, request, offset, request_group))
    attention = attention.reshape(TOKENS, model_width)
    projected_out = jnp.dot(attention, w_out, preferred_element_type=jnp.float32)
    residual_in = state_in.astype(jnp.float32)
    state_mid = rms_rows(residual_in + eigen_rates[0][None, :] * (rms_rows(projected_out) - residual_in)).astype(jnp.bfloat16)
    gate_part = jnp.dot(state_mid, w_gate_up[0], preferred_element_type=jnp.float32)
    up_part = jnp.dot(state_mid, w_gate_up[1], preferred_element_type=jnp.float32)
    hidden = (jax.nn.silu(scale_gate_up[0][None, :] * gate_part) * (scale_gate_up[1][None, :] * up_part)).astype(jnp.bfloat16)
    feed_sum = jnp.dot(hidden, w_down, preferred_element_type=jnp.float32)
    middle = state_mid.astype(jnp.float32)
    result = rms_rows(middle + eigen_rates[1][None, :] * (rms_rows(feed_sum) - middle))
    live_rows = slot_valid.reshape(TOKENS).astype(jnp.float32)
    return (live_rows[:, None] * result).astype(jnp.bfloat16)
```

```python
import math

import jax
import jax.numpy as jnp
from jax import lax
from jax.sharding import PartitionSpec as P

HEADS = 20
GROUPS = 8


EPSILON = 1e-06


def rms_rows(values_in):
    return values_in * lax.rsqrt(jnp.mean(values_in * values_in, axis=-1, keepdims=True) + EPSILON)


def head_norm(values_in, scale_vec, head_count):
    row_count, model_width = values_in.shape
    per_head = values_in.reshape(row_count, head_count, model_width // head_count)
    normed = per_head * lax.rsqrt(jnp.mean(per_head * per_head, axis=-1, keepdims=True) + EPSILON)
    return normed.reshape(row_count, model_width) * scale_vec[None, :]


def rotate(values_in, position, head_count):
    row_count, model_width = values_in.shape
    head_dim = model_width // head_count
    half_dim = head_dim // 2
    frequency = jnp.exp(
        jnp.arange(half_dim).astype(jnp.float32) * (-2.0 * math.log(10000.0) / head_dim)
    )
    rotation = position.astype(jnp.float32)[:, None] * frequency[None, :]
    cosine_table = jnp.cos(rotation)[:, None, :]
    sine_table = jnp.sin(rotation)[:, None, :]
    per_head = values_in.reshape(row_count, head_count, head_dim)
    lower_half = per_head[:, :, :half_dim]
    upper_half = per_head[:, :, half_dim:]
    turned = jnp.concatenate(
        [
            lower_half * cosine_table - upper_half * sine_table,
            upper_half * cosine_table + lower_half * sine_table,
        ],
        axis=-1,
    )
    return turned.reshape(row_count, model_width)


def slot_tables(suffix_len, request_group, slot_count):
    end_slots = jnp.cumsum(suffix_len, axis=1)
    start_slots = end_slots - suffix_len
    slot_ids = jnp.arange(slot_count)
    inside = (slot_ids[None, None, :] >= start_slots[:, :, None]) & (
        slot_ids[None, None, :] < end_slots[:, :, None]
    )
    request_ids = jnp.arange(suffix_len.shape[1])
    slot_valid = jnp.any(inside, axis=1)
    request = jnp.sum(jnp.where(inside, request_ids[None, :, None], 0), axis=1)
    offset = slot_ids[None, :] - jnp.sum(jnp.where(inside, start_slots[:, :, None], 0), axis=1)
    group_id = jnp.where(
        slot_valid, jnp.sum(jnp.where(inside, request_group[:, :, None], 0), axis=1), -1
    )
    return (slot_valid, request, offset, group_id)


def prefix_block(query_block, group_block, prefix_keys, prefix_values, key_group, score_scale):
    row_count, model_width = query_block.shape
    head_dim = model_width // HEADS
    query_heads = query_block.reshape(row_count, HEADS, head_dim)
    key_heads = prefix_keys.reshape(-1, HEADS, head_dim)
    value_heads = prefix_values.reshape(-1, HEADS, head_dim)
    scores = (
        jnp.einsum("qhd,khd->qhk", query_heads, key_heads, preferred_element_type=jnp.float32)
        * score_scale
    )
    allowed = group_block[:, None] == key_group[None, :]
    weights = jnp.where(allowed[:, None, :], jnp.exp(scores), 0.0)
    weight_sum = jnp.sum(weights, axis=-1)
    summed = jnp.einsum(
        "qhk,khd->qhd",
        weights.astype(jnp.bfloat16),
        value_heads,
        preferred_element_type=jnp.float32,
    )
    return (summed.reshape(row_count, model_width), weight_sum)


def shards_columns(
    hidden_in,
    w_qkv,
    w_out,
    w_gate_up,
    w_down,
    scale_qk,
    scale_gate_up,
    eigen_rates,
    cache_keys,
    cache_values,
    page_table,
    request_group,
    suffix_len,
):
    slot_count, model_width = hidden_in.shape
    head_dim = model_width // HEADS
    score_scale = 1.0 / math.sqrt(head_dim)
    mp_count = lax.axis_size("mp")
    mp_index = lax.axis_index("mp")
    own_rows = slot_count // mp_count
    row_first = mp_index * own_rows
    shard_index = lax.axis_index("pages")
    pages_here, page_len = (cache_keys.shape[0], cache_keys.shape[1])
    pool_pages = page_table.shape[0]
    prefix_pages = pool_pages // GROUPS
    slot_valid, request, offset, group_id = slot_tables(suffix_len, request_group, slot_count)
    live_shard = lax.dynamic_index_in_dim(slot_valid, shard_index, 0, keepdims=False)
    request_shard = lax.dynamic_index_in_dim(request, shard_index, 0, keepdims=False)
    offset_shard = lax.dynamic_index_in_dim(offset, shard_index, 0, keepdims=False)
    position_shard = prefix_pages * page_len + offset_shard
    live_own = lax.dynamic_slice_in_dim(live_shard, row_first, own_rows, 0)
    request_own = lax.dynamic_slice_in_dim(request_shard, row_first, own_rows, 0)
    offset_own = lax.dynamic_slice_in_dim(offset_shard, row_first, own_rows, 0)
    position_own = lax.dynamic_slice_in_dim(position_shard, row_first, own_rows, 0)
    state_in = rms_rows(hidden_in.astype(jnp.float32)).astype(jnp.bfloat16)
    projected = jnp.einsum(
        "sd,jdc->jsc", state_in, w_qkv, preferred_element_type=jnp.float32
    ).astype(jnp.bfloat16)
    columns = lax.all_gather(projected, "mp", axis=2, tiled=True)
    query_raw = lax.dynamic_slice_in_dim(columns[0], row_first, own_rows, 0)
    key_raw, value_rows = (columns[1], columns[2])
    queries = head_norm(
        rotate(query_raw.astype(jnp.float32), position_own, HEADS), scale_qk, HEADS
    ).astype(jnp.bfloat16)
    keys_new = head_norm(
        rotate(key_raw.astype(jnp.float32), position_shard, HEADS), scale_qk, HEADS
    ).astype(jnp.bfloat16)
    query_heads = queries.reshape(own_rows, HEADS, head_dim)
    scores = (
        jnp.einsum(
            "qhd,khd->hqk",
            query_heads,
            keys_new.reshape(slot_count, HEADS, head_dim),
            preferred_element_type=jnp.float32,
        )
        * score_scale
    )
    allowed = (
        (request_own[:, None] == request_shard[None, :])
        & (offset_shard[None, :] <= offset_own[:, None])
        & live_own[:, None]
        & live_shard[None, :]
    )
    weights = jnp.where(allowed[None], jnp.exp(scores), 0.0)
    suffix_total = jnp.sum(weights, axis=-1)
    suffix_sum = jnp.einsum(
        "hqk,khd->qhd",
        weights.astype(jnp.bfloat16),
        value_rows.reshape(slot_count, HEADS, head_dim),
        preferred_element_type=jnp.float32,
    )
    physical = shard_index * pages_here + jnp.arange(pages_here, dtype=jnp.int32)
    matches = page_table[:, None] == physical[None, :]
    logical = jnp.sum(
        jnp.where(matches, jnp.arange(pool_pages, dtype=jnp.int32)[:, None], 0), axis=0
    )
    key_group = jnp.repeat(logical // prefix_pages, page_len)
    prefix_keys = head_norm(
        cache_keys.reshape(pages_here * page_len, model_width).astype(jnp.float32), scale_qk, HEADS
    ).astype(jnp.bfloat16)
    prefix_values = cache_values.reshape(pages_here * page_len, model_width)
    gathered = lax.all_gather(queries, "pages", axis=0, tiled=True)
    gathered_group = lax.dynamic_slice_in_dim(group_id, row_first, own_rows, 1).reshape(-1)
    row_count = own_rows * lax.axis_size("pages")
    block_rows = row_count if row_count <= 512 else math.gcd(row_count, 512)

    def attend_block(block_first):
        query_block = lax.dynamic_slice_in_dim(gathered, block_first, block_rows, 0)
        group_block = lax.dynamic_slice_in_dim(gathered_group, block_first, block_rows, 0)
        return prefix_block(
            query_block, group_block, prefix_keys, prefix_values, key_group, score_scale
        )

    block_starts = jnp.arange(row_count // block_rows, dtype=jnp.int32) * block_rows
    summed, weight_sum = lax.map(attend_block, block_starts)
    prefix_sum, prefix_total = lax.psum_scatter(
        (summed.reshape(row_count, model_width), weight_sum.reshape(row_count, HEADS)),
        "pages",
        scatter_dimension=0,
        tiled=True,
    )
    denominator = suffix_total.T + prefix_total + (1.0 - live_own.astype(jnp.float32))[:, None]
    mixed = (suffix_sum + prefix_sum.reshape(own_rows, HEADS, head_dim)) / denominator[:, :, None]
    attention = mixed.reshape(own_rows, model_width).astype(jnp.bfloat16)
    projected_out = jnp.dot(
        lax.all_gather(attention, "mp", axis=0, tiled=True),
        w_out,
        preferred_element_type=jnp.float32,
    )
    residual_in = state_in.astype(jnp.float32)
    state_mid = rms_rows(
        residual_in + eigen_rates[0][None, :] * (rms_rows(projected_out) - residual_in)
    ).astype(jnp.bfloat16)
    state_own = lax.dynamic_slice_in_dim(state_mid, row_first, own_rows, 0)
    gate_up = jnp.einsum("sd,jdf->jsf", state_mid, w_gate_up, preferred_element_type=jnp.float32)
    hidden = (
        jax.nn.silu(scale_gate_up[0][None, :] * gate_up[0])
        * (scale_gate_up[1][None, :] * gate_up[1])
    ).astype(jnp.bfloat16)
    feed_sum = lax.psum_scatter(
        jnp.dot(hidden, w_down, preferred_element_type=jnp.float32),
        "mp",
        scatter_dimension=0,
        tiled=True,
    )
    middle = state_own.astype(jnp.float32)
    result = rms_rows(middle + eigen_rates[1][None, :] * (rms_rows(feed_sum) - middle))
    return (live_own.astype(jnp.float32)[:, None] * result).astype(jnp.bfloat16)


def shards_heads(
    hidden_in,
    w_qkv,
    w_out,
    w_gate_up,
    w_down,
    scale_qk,
    scale_gate_up,
    eigen_rates,
    cache_keys,
    cache_values,
    page_table,
    request_group,
    suffix_len,
):
    slot_count, model_width = hidden_in.shape
    head_dim = model_width // HEADS
    score_scale = 1.0 / math.sqrt(head_dim)
    mp_count = lax.axis_size("mp")
    mp_index = lax.axis_index("mp")
    local_heads = HEADS // mp_count
    local_width = local_heads * head_dim
    own_rows = slot_count // mp_count
    row_first = mp_index * own_rows
    shard_index = lax.axis_index("pages")
    pages_here, page_len = (cache_keys.shape[0], cache_keys.shape[1])
    pool_pages = page_table.shape[0]
    prefix_pages = pool_pages // GROUPS
    slot_valid, request, offset, group_id = slot_tables(suffix_len, request_group, slot_count)
    live_shard = lax.dynamic_index_in_dim(slot_valid, shard_index, 0, keepdims=False)
    request_shard = lax.dynamic_index_in_dim(request, shard_index, 0, keepdims=False)
    offset_shard = lax.dynamic_index_in_dim(offset, shard_index, 0, keepdims=False)
    position_shard = prefix_pages * page_len + offset_shard
    live_own = lax.dynamic_slice_in_dim(live_shard, row_first, own_rows, 0)
    scale_local = lax.dynamic_slice_in_dim(scale_qk, mp_index * local_width, local_width, 0)
    state_in = rms_rows(hidden_in.astype(jnp.float32)).astype(jnp.bfloat16)
    projected = jnp.einsum(
        "sd,jdc->jsc", state_in, w_qkv, preferred_element_type=jnp.float32
    ).astype(jnp.bfloat16)
    queries = head_norm(
        rotate(projected[0].astype(jnp.float32), position_shard, local_heads), scale_local, local_heads
    ).astype(jnp.bfloat16)
    keys_new = head_norm(
        rotate(projected[1].astype(jnp.float32), position_shard, local_heads), scale_local, local_heads
    ).astype(jnp.bfloat16)
    value_rows = projected[2]
    gathered = lax.all_gather(queries, "pages", axis=0, tiled=True)
    scores = (
        jnp.einsum(
            "qhd,khd->hqk",
            queries.reshape(slot_count, local_heads, head_dim),
            keys_new.reshape(slot_count, local_heads, head_dim),
            preferred_element_type=jnp.float32,
        )
        * score_scale
    )
    allowed = (
        (request_shard[:, None] == request_shard[None, :])
        & (offset_shard[None, :] <= offset_shard[:, None])
        & live_shard[:, None]
        & live_shard[None, :]
    )
    weights = jnp.where(allowed[None], jnp.exp(scores), 0.0)
    suffix_total = jnp.sum(weights, axis=-1)
    suffix_sum = jnp.einsum(
        "hqk,khd->qhd",
        weights.astype(jnp.bfloat16),
        value_rows.reshape(slot_count, local_heads, head_dim),
        preferred_element_type=jnp.float32,
    )
    physical = shard_index * pages_here + jnp.arange(pages_here, dtype=jnp.int32)
    matches = page_table[:, None] == physical[None, :]
    logical = jnp.sum(
        jnp.where(matches, jnp.arange(pool_pages, dtype=jnp.int32)[:, None], 0), axis=0
    )
    key_group = jnp.repeat(logical // prefix_pages, page_len)
    cache_local = lax.dynamic_slice_in_dim(cache_keys, mp_index * local_width, local_width, 2)
    prefix_keys = head_norm(
        cache_local.reshape(pages_here * page_len, local_width).astype(jnp.float32),
        scale_local,
        local_heads,
    ).astype(jnp.bfloat16)
    prefix_values = lax.dynamic_slice_in_dim(
        cache_values, mp_index * local_width, local_width, 2
    ).reshape(pages_here * page_len, local_width)
    gathered_group = group_id.reshape(-1)
    row_count = gathered.shape[0]
    query_heads = gathered.reshape(row_count, local_heads, head_dim)
    key_heads = prefix_keys.reshape(-1, local_heads, head_dim)
    value_heads = prefix_values.reshape(-1, local_heads, head_dim)
    prefix_scores = (
        jnp.einsum("qhd,khd->qhk", query_heads, key_heads, preferred_element_type=jnp.float32)
        * score_scale
    )
    prefix_allowed = gathered_group[:, None] == key_group[None, :]
    prefix_weights = jnp.where(prefix_allowed[:, None, :], jnp.exp(prefix_scores), 0.0)
    weight_sum = jnp.sum(prefix_weights, axis=-1)
    summed = jnp.einsum(
        "qhk,khd->qhd",
        prefix_weights.astype(jnp.bfloat16),
        value_heads,
        preferred_element_type=jnp.float32,
    )
    prefix_sum, prefix_total = lax.psum_scatter(
        (summed.reshape(row_count, local_width), weight_sum),
        "pages",
        scatter_dimension=0,
        tiled=True,
    )
    denominator = suffix_total.T + prefix_total + (1.0 - live_shard.astype(jnp.float32))[:, None]
    mixed = (suffix_sum + prefix_sum.reshape(slot_count, local_heads, head_dim)) / denominator[
        :, :, None
    ]
    attention_local = mixed.reshape(slot_count, local_width).astype(jnp.bfloat16)
    attention = lax.all_gather(attention_local, "mp", axis=1, tiled=True)
    projected_out = jnp.dot(attention, w_out, preferred_element_type=jnp.float32)
    residual_in = state_in.astype(jnp.float32)
    state_mid = rms_rows(
        residual_in + eigen_rates[0][None, :] * (rms_rows(projected_out) - residual_in)
    ).astype(jnp.bfloat16)
    state_own = lax.dynamic_slice_in_dim(state_mid, row_first, own_rows, 0)
    gate_up = jnp.einsum("sd,jdf->jsf", state_mid, w_gate_up, preferred_element_type=jnp.float32)
    hidden = (
        jax.nn.silu(scale_gate_up[0][None, :] * gate_up[0])
        * (scale_gate_up[1][None, :] * gate_up[1])
    ).astype(jnp.bfloat16)
    feed_sum = lax.psum_scatter(
        jnp.dot(hidden, w_down, preferred_element_type=jnp.float32),
        "mp",
        scatter_dimension=0,
        tiled=True,
    )
    middle = state_own.astype(jnp.float32)
    result = rms_rows(middle + eigen_rates[1][None, :] * (rms_rows(feed_sum) - middle))
    return (live_own.astype(jnp.float32)[:, None] * result).astype(jnp.bfloat16)


def solution(mesh):
    shards = shards_heads if HEADS % mesh.shape["mp"] == 0 else shards_columns
    return jax.shard_map(
        shards,
        mesh=mesh,
        in_specs=(
            P("pages", None),
            P(None, None, "mp"),
            P(),
            P(None, None, "mp"),
            P("mp", None),
            P(),
            P(None, "mp"),
            P(),
            P("pages", None, None),
            P("pages", None, None),
            P(),
            P(),
            P(),
        ),
        out_specs=P(("pages", "mp"), None),
        check_vma=False,
    )
```

```python
import math

import jax
import jax.numpy as jnp
from jax import lax
from jax.sharding import PartitionSpec as P

HEADS = 20
GROUPS = 8


EPSILON = 1e-06


def rms_rows(values_in):
    return values_in * lax.rsqrt(jnp.mean(values_in * values_in, axis=-1, keepdims=True) + EPSILON)


def head_norm(values_in, scale_vec, head_count):
    row_count, model_width = values_in.shape
    per_head = values_in.reshape(row_count, head_count, model_width // head_count)
    normed = per_head * lax.rsqrt(jnp.mean(per_head * per_head, axis=-1, keepdims=True) + EPSILON)
    return normed.reshape(row_count, model_width) * scale_vec[None, :]


def rotate(values_in, position, head_count):
    row_count, model_width = values_in.shape
    head_dim = model_width // head_count
    half_dim = head_dim // 2
    frequency = jnp.exp(
        jnp.arange(half_dim).astype(jnp.float32) * (-2.0 * math.log(10000.0) / head_dim)
    )
    rotation = position.astype(jnp.float32)[:, None] * frequency[None, :]
    cosine_table = jnp.cos(rotation)[:, None, :]
    sine_table = jnp.sin(rotation)[:, None, :]
    per_head = values_in.reshape(row_count, head_count, head_dim)
    lower_half = per_head[:, :, :half_dim]
    upper_half = per_head[:, :, half_dim:]
    turned = jnp.concatenate(
        [
            lower_half * cosine_table - upper_half * sine_table,
            upper_half * cosine_table + lower_half * sine_table,
        ],
        axis=-1,
    )
    return turned.reshape(row_count, model_width)


def slot_tables(suffix_len, request_group, slot_count):
    end_slots = jnp.cumsum(suffix_len, axis=1)
    start_slots = end_slots - suffix_len
    slot_ids = jnp.arange(slot_count)
    inside = (slot_ids[None, None, :] >= start_slots[:, :, None]) & (
        slot_ids[None, None, :] < end_slots[:, :, None]
    )
    request_ids = jnp.arange(suffix_len.shape[1])
    slot_valid = jnp.any(inside, axis=1)
    request = jnp.sum(jnp.where(inside, request_ids[None, :, None], 0), axis=1)
    offset = slot_ids[None, :] - jnp.sum(jnp.where(inside, start_slots[:, :, None], 0), axis=1)
    group_id = jnp.where(
        slot_valid, jnp.sum(jnp.where(inside, request_group[:, :, None], 0), axis=1), -1
    )
    return (slot_valid, request, offset, group_id)


def prefix_block(query_block, group_block, prefix_keys, prefix_values, key_group, score_scale):
    row_count, model_width = query_block.shape
    head_dim = model_width // HEADS
    query_heads = query_block.reshape(row_count, HEADS, head_dim)
    key_heads = prefix_keys.reshape(-1, HEADS, head_dim)
    value_heads = prefix_values.reshape(-1, HEADS, head_dim)
    scores = (
        jnp.einsum("qhd,khd->qhk", query_heads, key_heads, preferred_element_type=jnp.float32)
        * score_scale
    )
    allowed = group_block[:, None] == key_group[None, :]
    weights = jnp.where(allowed[:, None, :], jnp.exp(scores), 0.0)
    weight_sum = jnp.sum(weights, axis=-1)
    summed = jnp.einsum(
        "qhk,khd->qhd",
        weights.astype(jnp.bfloat16),
        value_heads,
        preferred_element_type=jnp.float32,
    )
    return (summed.reshape(row_count, model_width), weight_sum)


def shards_columns(
    hidden_in,
    w_qkv,
    w_out,
    w_gate_up,
    w_down,
    scale_qk,
    scale_gate_up,
    eigen_rates,
    cache_keys,
    cache_values,
    page_table,
    request_group,
    suffix_len,
):
    slot_count, model_width = hidden_in.shape
    head_dim = model_width // HEADS
    score_scale = 1.0 / math.sqrt(head_dim)
    mp_count = lax.axis_size("mp")
    mp_index = lax.axis_index("mp")
    own_rows = slot_count // mp_count
    row_first = mp_index * own_rows
    shard_index = lax.axis_index("pages")
    pages_here, page_len = (cache_keys.shape[0], cache_keys.shape[1])
    pool_pages = page_table.shape[0]
    prefix_pages = pool_pages // GROUPS
    slot_valid, request, offset, group_id = slot_tables(suffix_len, request_group, slot_count)
    live_shard = lax.dynamic_index_in_dim(slot_valid, shard_index, 0, keepdims=False)
    request_shard = lax.dynamic_index_in_dim(request, shard_index, 0, keepdims=False)
    offset_shard = lax.dynamic_index_in_dim(offset, shard_index, 0, keepdims=False)
    position_shard = prefix_pages * page_len + offset_shard
    live_own = lax.dynamic_slice_in_dim(live_shard, row_first, own_rows, 0)
    request_own = lax.dynamic_slice_in_dim(request_shard, row_first, own_rows, 0)
    offset_own = lax.dynamic_slice_in_dim(offset_shard, row_first, own_rows, 0)
    position_own = lax.dynamic_slice_in_dim(position_shard, row_first, own_rows, 0)
    state_in = rms_rows(hidden_in.astype(jnp.float32)).astype(jnp.bfloat16)
    projected = jnp.einsum(
        "sd,jdc->jsc", state_in, w_qkv, preferred_element_type=jnp.float32
    ).astype(jnp.bfloat16)
    columns = lax.all_gather(projected, "mp", axis=2, tiled=True)
    query_raw = lax.dynamic_slice_in_dim(columns[0], row_first, own_rows, 0)
    key_raw, value_rows = (columns[1], columns[2])
    queries = head_norm(
        rotate(query_raw.astype(jnp.float32), position_own, HEADS), scale_qk, HEADS
    ).astype(jnp.bfloat16)
    keys_new = head_norm(
        rotate(key_raw.astype(jnp.float32), position_shard, HEADS), scale_qk, HEADS
    ).astype(jnp.bfloat16)
    query_heads = queries.reshape(own_rows, HEADS, head_dim)
    scores = (
        jnp.einsum(
            "qhd,khd->hqk",
            query_heads,
            keys_new.reshape(slot_count, HEADS, head_dim),
            preferred_element_type=jnp.float32,
        )
        * score_scale
    )
    allowed = (
        (request_own[:, None] == request_shard[None, :])
        & (offset_shard[None, :] <= offset_own[:, None])
        & live_own[:, None]
        & live_shard[None, :]
    )
    weights = jnp.where(allowed[None], jnp.exp(scores), 0.0)
    suffix_total = jnp.sum(weights, axis=-1)
    suffix_sum = jnp.einsum(
        "hqk,khd->qhd",
        weights.astype(jnp.bfloat16),
        value_rows.reshape(slot_count, HEADS, head_dim),
        preferred_element_type=jnp.float32,
    )
    physical = shard_index * pages_here + jnp.arange(pages_here, dtype=jnp.int32)
    matches = page_table[:, None] == physical[None, :]
    logical = jnp.sum(
        jnp.where(matches, jnp.arange(pool_pages, dtype=jnp.int32)[:, None], 0), axis=0
    )
    key_group = jnp.repeat(logical // prefix_pages, page_len)
    prefix_keys = head_norm(
        cache_keys.reshape(pages_here * page_len, model_width).astype(jnp.float32), scale_qk, HEADS
    ).astype(jnp.bfloat16)
    prefix_values = cache_values.reshape(pages_here * page_len, model_width)
    gathered = lax.all_gather(queries, "pages", axis=0, tiled=True)
    gathered_group = lax.dynamic_slice_in_dim(group_id, row_first, own_rows, 1).reshape(-1)
    row_count = own_rows * lax.axis_size("pages")
    block_rows = row_count if row_count <= 512 else math.gcd(row_count, 512)

    def attend_block(block_first):
        query_block = lax.dynamic_slice_in_dim(gathered, block_first, block_rows, 0)
        group_block = lax.dynamic_slice_in_dim(gathered_group, block_first, block_rows, 0)
        return prefix_block(
            query_block, group_block, prefix_keys, prefix_values, key_group, score_scale
        )

    block_starts = jnp.arange(row_count // block_rows, dtype=jnp.int32) * block_rows
    summed, weight_sum = lax.map(attend_block, block_starts)
    prefix_sum, prefix_total = lax.psum_scatter(
        (summed.reshape(row_count, model_width), weight_sum.reshape(row_count, HEADS)),
        "pages",
        scatter_dimension=0,
        tiled=True,
    )
    denominator = suffix_total.T + prefix_total + (1.0 - live_own.astype(jnp.float32))[:, None]
    mixed = (suffix_sum + prefix_sum.reshape(own_rows, HEADS, head_dim)) / denominator[:, :, None]
    attention = mixed.reshape(own_rows, model_width).astype(jnp.bfloat16)
    projected_out = jnp.dot(
        lax.all_gather(attention, "mp", axis=0, tiled=True),
        w_out,
        preferred_element_type=jnp.float32,
    )
    residual_in = state_in.astype(jnp.float32)
    state_mid = rms_rows(
        residual_in + eigen_rates[0][None, :] * (rms_rows(projected_out) - residual_in)
    ).astype(jnp.bfloat16)
    state_own = lax.dynamic_slice_in_dim(state_mid, row_first, own_rows, 0)
    gate_up = jnp.einsum("sd,jdf->jsf", state_mid, w_gate_up, preferred_element_type=jnp.float32)
    hidden = (
        jax.nn.silu(scale_gate_up[0][None, :] * gate_up[0])
        * (scale_gate_up[1][None, :] * gate_up[1])
    ).astype(jnp.bfloat16)
    feed_sum = lax.psum_scatter(
        jnp.dot(hidden, w_down, preferred_element_type=jnp.float32),
        "mp",
        scatter_dimension=0,
        tiled=True,
    )
    middle = state_own.astype(jnp.float32)
    result = rms_rows(middle + eigen_rates[1][None, :] * (rms_rows(feed_sum) - middle))
    return (live_own.astype(jnp.float32)[:, None] * result).astype(jnp.bfloat16)


def shards_heads(
    hidden_in,
    w_qkv,
    w_out,
    w_gate_up,
    w_down,
    scale_qk,
    scale_gate_up,
    eigen_rates,
    cache_keys,
    cache_values,
    page_table,
    request_group,
    suffix_len,
):
    slot_count, model_width = hidden_in.shape
    head_dim = model_width // HEADS
    score_scale = 1.0 / math.sqrt(head_dim)
    mp_count = lax.axis_size("mp")
    mp_index = lax.axis_index("mp")
    local_heads = HEADS // mp_count
    local_width = local_heads * head_dim
    own_rows = slot_count // mp_count
    row_first = mp_index * own_rows
    shard_index = lax.axis_index("pages")
    pages_here, page_len = (cache_keys.shape[0], cache_keys.shape[1])
    pool_pages = page_table.shape[0]
    prefix_pages = pool_pages // GROUPS
    slot_valid, request, offset, group_id = slot_tables(suffix_len, request_group, slot_count)
    live_shard = lax.dynamic_index_in_dim(slot_valid, shard_index, 0, keepdims=False)
    request_shard = lax.dynamic_index_in_dim(request, shard_index, 0, keepdims=False)
    offset_shard = lax.dynamic_index_in_dim(offset, shard_index, 0, keepdims=False)
    position_shard = prefix_pages * page_len + offset_shard
    live_own = lax.dynamic_slice_in_dim(live_shard, row_first, own_rows, 0)
    scale_local = lax.dynamic_slice_in_dim(scale_qk, mp_index * local_width, local_width, 0)
    state_in = rms_rows(hidden_in.astype(jnp.float32)).astype(jnp.bfloat16)
    projected = jnp.einsum(
        "sd,jdc->jsc", state_in, w_qkv, preferred_element_type=jnp.float32
    ).astype(jnp.bfloat16)
    queries = head_norm(
        rotate(projected[0].astype(jnp.float32), position_shard, local_heads), scale_local, local_heads
    ).astype(jnp.bfloat16)
    keys_new = head_norm(
        rotate(projected[1].astype(jnp.float32), position_shard, local_heads), scale_local, local_heads
    ).astype(jnp.bfloat16)
    value_rows = projected[2]
    gathered = lax.all_gather(queries, "pages", axis=0, tiled=True)
    scores = (
        jnp.einsum(
            "qhd,khd->hqk",
            queries.reshape(slot_count, local_heads, head_dim),
            keys_new.reshape(slot_count, local_heads, head_dim),
            preferred_element_type=jnp.float32,
        )
        * score_scale
    )
    allowed = (
        (request_shard[:, None] == request_shard[None, :])
        & (offset_shard[None, :] <= offset_shard[:, None])
        & live_shard[:, None]
        & live_shard[None, :]
    )
    weights = jnp.where(allowed[None], jnp.exp(scores), 0.0)
    suffix_total = jnp.sum(weights, axis=-1)
    suffix_sum = jnp.einsum(
        "hqk,khd->qhd",
        weights.astype(jnp.bfloat16),
        value_rows.reshape(slot_count, local_heads, head_dim),
        preferred_element_type=jnp.float32,
    )
    physical = shard_index * pages_here + jnp.arange(pages_here, dtype=jnp.int32)
    matches = page_table[:, None] == physical[None, :]
    logical = jnp.sum(
        jnp.where(matches, jnp.arange(pool_pages, dtype=jnp.int32)[:, None], 0), axis=0
    )
    key_group = jnp.repeat(logical // prefix_pages, page_len)
    cache_local = lax.dynamic_slice_in_dim(cache_keys, mp_index * local_width, local_width, 2)
    prefix_keys = head_norm(
        cache_local.reshape(pages_here * page_len, local_width).astype(jnp.float32),
        scale_local,
        local_heads,
    ).astype(jnp.bfloat16)
    prefix_values = lax.dynamic_slice_in_dim(
        cache_values, mp_index * local_width, local_width, 2
    ).reshape(pages_here * page_len, local_width)
    gathered_group = group_id.reshape(-1)
    row_count = gathered.shape[0]
    query_heads = gathered.reshape(row_count, local_heads, head_dim)
    key_heads = prefix_keys.reshape(-1, local_heads, head_dim)
    value_heads = prefix_values.reshape(-1, local_heads, head_dim)
    prefix_scores = (
        jnp.einsum("qhd,khd->qhk", query_heads, key_heads, preferred_element_type=jnp.float32)
        * score_scale
    )
    prefix_allowed = gathered_group[:, None] == key_group[None, :]
    prefix_weights = jnp.where(prefix_allowed[:, None, :], jnp.exp(prefix_scores), 0.0)
    weight_sum = jnp.sum(prefix_weights, axis=-1)
    summed = jnp.einsum(
        "qhk,khd->qhd",
        prefix_weights.astype(jnp.bfloat16),
        value_heads,
        preferred_element_type=jnp.float32,
    )
    prefix_both = lax.psum_scatter(
        jnp.concatenate([summed.reshape(row_count, local_width), weight_sum], axis=1),
        "pages",
        scatter_dimension=0,
        tiled=True,
    )
    prefix_sum = prefix_both[:, :local_width]
    prefix_total = prefix_both[:, local_width:]
    denominator = suffix_total.T + prefix_total + (1.0 - live_shard.astype(jnp.float32))[:, None]
    mixed = (suffix_sum + prefix_sum.reshape(slot_count, local_heads, head_dim)) / denominator[
        :, :, None
    ]
    attention_local = mixed.reshape(slot_count, local_width).astype(jnp.bfloat16)
    attention = lax.all_gather(attention_local, "mp", axis=1, tiled=True)
    projected_out = jnp.dot(attention, w_out, preferred_element_type=jnp.float32)
    residual_in = state_in.astype(jnp.float32)
    state_mid = rms_rows(
        residual_in + eigen_rates[0][None, :] * (rms_rows(projected_out) - residual_in)
    ).astype(jnp.bfloat16)
    state_own = lax.dynamic_slice_in_dim(state_mid, row_first, own_rows, 0)
    gate_up = jnp.einsum("sd,jdf->jsf", state_mid, w_gate_up, preferred_element_type=jnp.float32)
    hidden = (
        jax.nn.silu(scale_gate_up[0][None, :] * gate_up[0])
        * (scale_gate_up[1][None, :] * gate_up[1])
    ).astype(jnp.bfloat16)
    feed_sum = lax.psum_scatter(
        jnp.dot(hidden, w_down, preferred_element_type=jnp.float32),
        "mp",
        scatter_dimension=0,
        tiled=True,
    )
    middle = state_own.astype(jnp.float32)
    result = rms_rows(middle + eigen_rates[1][None, :] * (rms_rows(feed_sum) - middle))
    return (live_own.astype(jnp.float32)[:, None] * result).astype(jnp.bfloat16)


def solution(mesh):
    shards = shards_heads if HEADS % mesh.shape["mp"] == 0 else shards_columns
    return jax.shard_map(
        shards,
        mesh=mesh,
        in_specs=(
            P("pages", None),
            P(None, None, "mp"),
            P(),
            P(None, None, "mp"),
            P("mp", None),
            P(),
            P(None, "mp"),
            P(),
            P("pages", None, None),
            P("pages", None, None),
            P(),
            P(),
            P(),
        ),
        out_specs=P(("pages", "mp"), None),
        check_vma=False,
    )
```

```python
import math

import jax
import jax.numpy as jnp
from jax import lax
from jax.sharding import PartitionSpec as P

HEADS = 20
GROUPS = 8


EPSILON = 1e-06


def rms_rows(values_in):
    return values_in * lax.rsqrt(jnp.mean(values_in * values_in, axis=-1, keepdims=True) + EPSILON)


def head_norm(values_in, scale_vec, head_count):
    row_count, model_width = values_in.shape
    per_head = values_in.reshape(row_count, head_count, model_width // head_count)
    normed = per_head * lax.rsqrt(jnp.mean(per_head * per_head, axis=-1, keepdims=True) + EPSILON)
    return normed.reshape(row_count, model_width) * scale_vec[None, :]


def rotate(values_in, position, head_count):
    row_count, model_width = values_in.shape
    head_dim = model_width // head_count
    half_dim = head_dim // 2
    frequency = jnp.exp(
        jnp.arange(half_dim).astype(jnp.float32) * (-2.0 * math.log(10000.0) / head_dim)
    )
    rotation = position.astype(jnp.float32)[:, None] * frequency[None, :]
    cosine_table = jnp.cos(rotation)[:, None, :]
    sine_table = jnp.sin(rotation)[:, None, :]
    per_head = values_in.reshape(row_count, head_count, head_dim)
    lower_half = per_head[:, :, :half_dim]
    upper_half = per_head[:, :, half_dim:]
    turned = jnp.concatenate(
        [
            lower_half * cosine_table - upper_half * sine_table,
            upper_half * cosine_table + lower_half * sine_table,
        ],
        axis=-1,
    )
    return turned.reshape(row_count, model_width)


def slot_tables(suffix_len, request_group, slot_count):
    end_slots = jnp.cumsum(suffix_len, axis=1)
    start_slots = end_slots - suffix_len
    slot_ids = jnp.arange(slot_count)
    inside = (slot_ids[None, None, :] >= start_slots[:, :, None]) & (
        slot_ids[None, None, :] < end_slots[:, :, None]
    )
    request_ids = jnp.arange(suffix_len.shape[1])
    slot_valid = jnp.any(inside, axis=1)
    request = jnp.sum(jnp.where(inside, request_ids[None, :, None], 0), axis=1)
    offset = slot_ids[None, :] - jnp.sum(jnp.where(inside, start_slots[:, :, None], 0), axis=1)
    group_id = jnp.where(
        slot_valid, jnp.sum(jnp.where(inside, request_group[:, :, None], 0), axis=1), -1
    )
    return (slot_valid, request, offset, group_id)


def prefix_block(query_block, group_block, prefix_keys, prefix_values, key_group, score_scale):
    row_count, model_width = query_block.shape
    head_dim = model_width // HEADS
    query_heads = query_block.reshape(row_count, HEADS, head_dim)
    key_heads = prefix_keys.reshape(-1, HEADS, head_dim)
    value_heads = prefix_values.reshape(-1, HEADS, head_dim)
    scores = (
        jnp.einsum("qhd,khd->qhk", query_heads, key_heads, preferred_element_type=jnp.float32)
        * score_scale
    )
    allowed = group_block[:, None] == key_group[None, :]
    weights = jnp.where(allowed[:, None, :], jnp.exp(scores), 0.0)
    weight_sum = jnp.sum(weights, axis=-1)
    summed = jnp.einsum(
        "qhk,khd->qhd",
        weights.astype(jnp.bfloat16),
        value_heads,
        preferred_element_type=jnp.float32,
    )
    return (summed.reshape(row_count, model_width), weight_sum)


def shards_columns(
    hidden_in,
    w_qkv,
    w_out,
    w_gate_up,
    w_down,
    scale_qk,
    scale_gate_up,
    eigen_rates,
    cache_keys,
    cache_values,
    page_table,
    request_group,
    suffix_len,
):
    slot_count, model_width = hidden_in.shape
    head_dim = model_width // HEADS
    score_scale = 1.0 / math.sqrt(head_dim)
    mp_count = lax.axis_size("mp")
    mp_index = lax.axis_index("mp")
    own_rows = slot_count // mp_count
    row_first = mp_index * own_rows
    shard_index = lax.axis_index("pages")
    pages_here, page_len = (cache_keys.shape[0], cache_keys.shape[1])
    pool_pages = page_table.shape[0]
    prefix_pages = pool_pages // GROUPS
    slot_valid, request, offset, group_id = slot_tables(suffix_len, request_group, slot_count)
    live_shard = lax.dynamic_index_in_dim(slot_valid, shard_index, 0, keepdims=False)
    request_shard = lax.dynamic_index_in_dim(request, shard_index, 0, keepdims=False)
    offset_shard = lax.dynamic_index_in_dim(offset, shard_index, 0, keepdims=False)
    position_shard = prefix_pages * page_len + offset_shard
    live_own = lax.dynamic_slice_in_dim(live_shard, row_first, own_rows, 0)
    request_own = lax.dynamic_slice_in_dim(request_shard, row_first, own_rows, 0)
    offset_own = lax.dynamic_slice_in_dim(offset_shard, row_first, own_rows, 0)
    position_own = lax.dynamic_slice_in_dim(position_shard, row_first, own_rows, 0)
    state_in = rms_rows(hidden_in.astype(jnp.float32)).astype(jnp.bfloat16)
    projected = jnp.einsum(
        "sd,jdc->jsc", state_in, w_qkv, preferred_element_type=jnp.float32
    ).astype(jnp.bfloat16)
    columns = lax.all_gather(projected, "mp", axis=2, tiled=True)
    query_raw = lax.dynamic_slice_in_dim(columns[0], row_first, own_rows, 0)
    key_raw, value_rows = (columns[1], columns[2])
    queries = head_norm(
        rotate(query_raw.astype(jnp.float32), position_own, HEADS), scale_qk, HEADS
    ).astype(jnp.bfloat16)
    keys_new = head_norm(
        rotate(key_raw.astype(jnp.float32), position_shard, HEADS), scale_qk, HEADS
    ).astype(jnp.bfloat16)
    query_heads = queries.reshape(own_rows, HEADS, head_dim)
    scores = (
        jnp.einsum(
            "qhd,khd->hqk",
            query_heads,
            keys_new.reshape(slot_count, HEADS, head_dim),
            preferred_element_type=jnp.float32,
        )
        * score_scale
    )
    allowed = (
        (request_own[:, None] == request_shard[None, :])
        & (offset_shard[None, :] <= offset_own[:, None])
        & live_own[:, None]
        & live_shard[None, :]
    )
    weights = jnp.where(allowed[None], jnp.exp(scores), 0.0)
    suffix_total = jnp.sum(weights, axis=-1)
    suffix_sum = jnp.einsum(
        "hqk,khd->qhd",
        weights.astype(jnp.bfloat16),
        value_rows.reshape(slot_count, HEADS, head_dim),
        preferred_element_type=jnp.float32,
    )
    physical = shard_index * pages_here + jnp.arange(pages_here, dtype=jnp.int32)
    matches = page_table[:, None] == physical[None, :]
    logical = jnp.sum(
        jnp.where(matches, jnp.arange(pool_pages, dtype=jnp.int32)[:, None], 0), axis=0
    )
    key_group = jnp.repeat(logical // prefix_pages, page_len)
    prefix_keys = head_norm(
        cache_keys.reshape(pages_here * page_len, model_width).astype(jnp.float32), scale_qk, HEADS
    ).astype(jnp.bfloat16)
    prefix_values = cache_values.reshape(pages_here * page_len, model_width)
    gathered = lax.all_gather(queries, "pages", axis=0, tiled=True)
    gathered_group = lax.dynamic_slice_in_dim(group_id, row_first, own_rows, 1).reshape(-1)
    row_count = own_rows * lax.axis_size("pages")
    block_rows = row_count if row_count <= 512 else math.gcd(row_count, 512)

    def attend_block(block_first):
        query_block = lax.dynamic_slice_in_dim(gathered, block_first, block_rows, 0)
        group_block = lax.dynamic_slice_in_dim(gathered_group, block_first, block_rows, 0)
        return prefix_block(
            query_block, group_block, prefix_keys, prefix_values, key_group, score_scale
        )

    block_starts = jnp.arange(row_count // block_rows, dtype=jnp.int32) * block_rows
    summed, weight_sum = lax.map(attend_block, block_starts)
    prefix_sum, prefix_total = lax.psum_scatter(
        (summed.reshape(row_count, model_width), weight_sum.reshape(row_count, HEADS)),
        "pages",
        scatter_dimension=0,
        tiled=True,
    )
    denominator = suffix_total.T + prefix_total + (1.0 - live_own.astype(jnp.float32))[:, None]
    mixed = (suffix_sum + prefix_sum.reshape(own_rows, HEADS, head_dim)) / denominator[:, :, None]
    attention = mixed.reshape(own_rows, model_width).astype(jnp.bfloat16)
    projected_out = jnp.dot(
        lax.all_gather(attention, "mp", axis=0, tiled=True),
        w_out,
        preferred_element_type=jnp.float32,
    )
    residual_in = state_in.astype(jnp.float32)
    state_mid = rms_rows(
        residual_in + eigen_rates[0][None, :] * (rms_rows(projected_out) - residual_in)
    ).astype(jnp.bfloat16)
    state_own = lax.dynamic_slice_in_dim(state_mid, row_first, own_rows, 0)
    gate_up = jnp.einsum("sd,jdf->jsf", state_mid, w_gate_up, preferred_element_type=jnp.float32)
    hidden = (
        jax.nn.silu(scale_gate_up[0][None, :] * gate_up[0])
        * (scale_gate_up[1][None, :] * gate_up[1])
    ).astype(jnp.bfloat16)
    feed_sum = lax.psum_scatter(
        jnp.dot(hidden, w_down, preferred_element_type=jnp.float32),
        "mp",
        scatter_dimension=0,
        tiled=True,
    )
    middle = state_own.astype(jnp.float32)
    result = rms_rows(middle + eigen_rates[1][None, :] * (rms_rows(feed_sum) - middle))
    return (live_own.astype(jnp.float32)[:, None] * result).astype(jnp.bfloat16)


def shards_heads(
    hidden_in,
    w_qkv,
    w_out,
    w_gate_up,
    w_down,
    scale_qk,
    scale_gate_up,
    eigen_rates,
    cache_keys,
    cache_values,
    page_table,
    request_group,
    suffix_len,
):
    slot_count, model_width = hidden_in.shape
    head_dim = model_width // HEADS
    score_scale = 1.0 / math.sqrt(head_dim)
    mp_count = lax.axis_size("mp")
    mp_index = lax.axis_index("mp")
    local_heads = HEADS // mp_count
    local_width = local_heads * head_dim
    own_rows = slot_count // mp_count
    row_first = mp_index * own_rows
    shard_index = lax.axis_index("pages")
    pages_here, page_len = (cache_keys.shape[0], cache_keys.shape[1])
    pool_pages = page_table.shape[0]
    prefix_pages = pool_pages // GROUPS
    slot_valid, request, offset, group_id = slot_tables(suffix_len, request_group, slot_count)
    live_shard = lax.dynamic_index_in_dim(slot_valid, shard_index, 0, keepdims=False)
    request_shard = lax.dynamic_index_in_dim(request, shard_index, 0, keepdims=False)
    offset_shard = lax.dynamic_index_in_dim(offset, shard_index, 0, keepdims=False)
    position_shard = prefix_pages * page_len + offset_shard
    live_own = lax.dynamic_slice_in_dim(live_shard, row_first, own_rows, 0)
    scale_local = lax.dynamic_slice_in_dim(scale_qk, mp_index * local_width, local_width, 0)
    state_in = rms_rows(hidden_in.astype(jnp.float32)).astype(jnp.bfloat16)
    projected = jnp.einsum(
        "sd,jdc->jsc", state_in, w_qkv, preferred_element_type=jnp.float32
    ).astype(jnp.bfloat16)
    queries = head_norm(
        rotate(projected[0].astype(jnp.float32), position_shard, local_heads), scale_local, local_heads
    ).astype(jnp.bfloat16)
    keys_new = head_norm(
        rotate(projected[1].astype(jnp.float32), position_shard, local_heads), scale_local, local_heads
    ).astype(jnp.bfloat16)
    value_rows = projected[2]
    gathered = lax.all_gather(queries, "pages", axis=0, tiled=True)
    scores = (
        jnp.einsum(
            "qhd,khd->hqk",
            queries.reshape(slot_count, local_heads, head_dim),
            keys_new.reshape(slot_count, local_heads, head_dim),
            preferred_element_type=jnp.float32,
        )
        * score_scale
    )
    allowed = (
        (request_shard[:, None] == request_shard[None, :])
        & (offset_shard[None, :] <= offset_shard[:, None])
        & live_shard[:, None]
        & live_shard[None, :]
    )
    weights = jnp.where(allowed[None], jnp.exp(scores), 0.0)
    suffix_total = jnp.sum(weights, axis=-1)
    suffix_sum = jnp.einsum(
        "hqk,khd->qhd",
        weights.astype(jnp.bfloat16),
        value_rows.reshape(slot_count, local_heads, head_dim),
        preferred_element_type=jnp.float32,
    )
    physical = shard_index * pages_here + jnp.arange(pages_here, dtype=jnp.int32)
    matches = page_table[:, None] == physical[None, :]
    logical = jnp.sum(
        jnp.where(matches, jnp.arange(pool_pages, dtype=jnp.int32)[:, None], 0), axis=0
    )
    key_group = jnp.repeat(logical // prefix_pages, page_len)
    cache_local = lax.dynamic_slice_in_dim(cache_keys, mp_index * local_width, local_width, 2)
    prefix_keys = head_norm(
        cache_local.reshape(pages_here * page_len, local_width).astype(jnp.float32),
        scale_local,
        local_heads,
    ).astype(jnp.bfloat16)
    prefix_values = lax.dynamic_slice_in_dim(
        cache_values, mp_index * local_width, local_width, 2
    ).reshape(pages_here * page_len, local_width)
    gathered_group = group_id.reshape(-1)
    row_count = gathered.shape[0]
    query_heads = gathered.reshape(row_count, local_heads, head_dim)
    key_heads = prefix_keys.reshape(-1, local_heads, head_dim)
    value_heads = prefix_values.reshape(-1, local_heads, head_dim)
    prefix_scores = (
        jnp.einsum("qhd,khd->qhk", query_heads, key_heads, preferred_element_type=jnp.float32)
        * score_scale
    )
    prefix_allowed = gathered_group[:, None] == key_group[None, :]
    prefix_weights = jnp.where(prefix_allowed[:, None, :], jnp.exp(prefix_scores), 0.0)
    weight_sum = jnp.sum(prefix_weights, axis=-1)
    summed = jnp.einsum(
        "qhk,khd->qhd",
        prefix_weights.astype(jnp.bfloat16),
        value_heads,
        preferred_element_type=jnp.float32,
    )
    prefix_both = lax.psum_scatter(
        jnp.concatenate([summed.reshape(row_count, local_width), weight_sum], axis=1).astype(
            jnp.bfloat16
        ),
        "pages",
        scatter_dimension=0,
        tiled=True,
    ).astype(jnp.float32)
    prefix_sum = prefix_both[:, :local_width]
    prefix_total = prefix_both[:, local_width:]
    denominator = suffix_total.T + prefix_total + (1.0 - live_shard.astype(jnp.float32))[:, None]
    mixed = (suffix_sum + prefix_sum.reshape(slot_count, local_heads, head_dim)) / denominator[
        :, :, None
    ]
    attention_local = mixed.reshape(slot_count, local_width).astype(jnp.bfloat16)
    attention = lax.all_gather(attention_local, "mp", axis=1, tiled=True)
    projected_out = jnp.dot(attention, w_out, preferred_element_type=jnp.float32)
    residual_in = state_in.astype(jnp.float32)
    state_mid = rms_rows(
        residual_in + eigen_rates[0][None, :] * (rms_rows(projected_out) - residual_in)
    ).astype(jnp.bfloat16)
    state_own = lax.dynamic_slice_in_dim(state_mid, row_first, own_rows, 0)
    gate_up = jnp.einsum("sd,jdf->jsf", state_mid, w_gate_up, preferred_element_type=jnp.float32)
    hidden = (
        jax.nn.silu(scale_gate_up[0][None, :] * gate_up[0])
        * (scale_gate_up[1][None, :] * gate_up[1])
    ).astype(jnp.bfloat16)
    feed_sum = lax.psum_scatter(
        jnp.dot(hidden, w_down, preferred_element_type=jnp.float32).astype(jnp.bfloat16),
        "mp",
        scatter_dimension=0,
        tiled=True,
    ).astype(jnp.float32)
    middle = state_own.astype(jnp.float32)
    result = rms_rows(middle + eigen_rates[1][None, :] * (rms_rows(feed_sum) - middle))
    return (live_own.astype(jnp.float32)[:, None] * result).astype(jnp.bfloat16)


def solution(mesh):
    shards = shards_heads if HEADS % mesh.shape["mp"] == 0 else shards_columns
    return jax.shard_map(
        shards,
        mesh=mesh,
        in_specs=(
            P("pages", None),
            P(None, None, "mp"),
            P(),
            P(None, None, "mp"),
            P("mp", None),
            P(),
            P(None, "mp"),
            P(),
            P("pages", None, None),
            P("pages", None, None),
            P(),
            P(),
            P(),
        ),
        out_specs=P(("pages", "mp"), None),
        check_vma=False,
    )
```

```python
import functools
import math

import jax
import jax.numpy as jnp
from jax import lax
from jax.experimental import pallas as pl
from jax.sharding import PartitionSpec as P

HEADS = 20
GROUPS = 8


EPSILON = 1e-06


def rms_rows(values_in):
    return values_in * lax.rsqrt(jnp.mean(values_in * values_in, axis=-1, keepdims=True) + EPSILON)


def head_norm(values_in, scale_vec, head_count):
    row_count, model_width = values_in.shape
    per_head = values_in.reshape(row_count, head_count, model_width // head_count)
    normed = per_head * lax.rsqrt(jnp.mean(per_head * per_head, axis=-1, keepdims=True) + EPSILON)
    return normed.reshape(row_count, model_width) * scale_vec[None, :]


def rotate(values_in, position, head_count):
    row_count, model_width = values_in.shape
    head_dim = model_width // head_count
    half_dim = head_dim // 2
    frequency = jnp.exp(
        jnp.arange(half_dim).astype(jnp.float32) * (-2.0 * math.log(10000.0) / head_dim)
    )
    rotation = position.astype(jnp.float32)[:, None] * frequency[None, :]
    cosine_table = jnp.cos(rotation)[:, None, :]
    sine_table = jnp.sin(rotation)[:, None, :]
    per_head = values_in.reshape(row_count, head_count, head_dim)
    lower_half = per_head[:, :, :half_dim]
    upper_half = per_head[:, :, half_dim:]
    turned = jnp.concatenate(
        [
            lower_half * cosine_table - upper_half * sine_table,
            upper_half * cosine_table + lower_half * sine_table,
        ],
        axis=-1,
    )
    return turned.reshape(row_count, model_width)


def slot_tables(suffix_len, request_group, slot_count):
    end_slots = jnp.cumsum(suffix_len, axis=1)
    start_slots = end_slots - suffix_len
    slot_ids = jnp.arange(slot_count)
    inside = (slot_ids[None, None, :] >= start_slots[:, :, None]) & (
        slot_ids[None, None, :] < end_slots[:, :, None]
    )
    request_ids = jnp.arange(suffix_len.shape[1])
    slot_valid = jnp.any(inside, axis=1)
    request = jnp.sum(jnp.where(inside, request_ids[None, :, None], 0), axis=1)
    offset = slot_ids[None, :] - jnp.sum(jnp.where(inside, start_slots[:, :, None], 0), axis=1)
    group_id = jnp.where(
        slot_valid, jnp.sum(jnp.where(inside, request_group[:, :, None], 0), axis=1), -1
    )
    return (slot_valid, request, offset, group_id)


def prefix_block(query_block, group_block, prefix_keys, prefix_values, key_group, score_scale):
    row_count, model_width = query_block.shape
    head_dim = model_width // HEADS
    query_heads = query_block.reshape(row_count, HEADS, head_dim)
    key_heads = prefix_keys.reshape(-1, HEADS, head_dim)
    value_heads = prefix_values.reshape(-1, HEADS, head_dim)
    scores = (
        jnp.einsum("qhd,khd->qhk", query_heads, key_heads, preferred_element_type=jnp.float32)
        * score_scale
    )
    allowed = group_block[:, None] == key_group[None, :]
    weights = jnp.where(allowed[:, None, :], jnp.exp(scores), 0.0)
    weight_sum = jnp.sum(weights, axis=-1)
    summed = jnp.einsum(
        "qhk,khd->qhd",
        weights.astype(jnp.bfloat16),
        value_heads,
        preferred_element_type=jnp.float32,
    )
    return (summed.reshape(row_count, model_width), weight_sum)


def prefix_kernel(q_ref, k_ref, v_ref, rg_ref, kg_ref, num_ref, den_ref, *, heads, head_dim, scale):
    queries = q_ref[...]
    keys = k_ref[...]
    values = v_ref[...]
    row_count, width = queries.shape
    allowed = rg_ref[...] == kg_ref[...]
    column = lax.broadcasted_iota(jnp.int32, (1, width), 1)
    lane = lax.broadcasted_iota(jnp.int32, (1, den_ref.shape[1]), 1)
    numerator = jnp.zeros((row_count, width), jnp.float32)
    denominator = jnp.zeros((row_count, den_ref.shape[1]), jnp.float32)
    for head in range(heads):
        in_head = (column >= head * head_dim) & (column < (head + 1) * head_dim)
        head_keys = jnp.where(in_head, keys, jnp.zeros_like(keys))
        scores = (
            lax.dot_general(
                queries,
                head_keys,
                (((1,), (1,)), ((), ())),
                preferred_element_type=jnp.float32,
            )
            * scale
        )
        weights = jnp.where(allowed, jnp.exp(scores), 0.0)
        denominator = jnp.where(lane == head, jnp.sum(weights, axis=1, keepdims=True), denominator)
        summed = jnp.dot(weights.astype(jnp.bfloat16), values, preferred_element_type=jnp.float32)
        numerator = jnp.where(in_head, summed, numerator)
    num_ref[...] = numerator.astype(num_ref.dtype)
    den_ref[...] = denominator.astype(den_ref.dtype)


def prefix_attention(queries, keys, values, row_group, key_group, heads, head_dim, scale):
    row_count, width = queries.shape
    key_count = keys.shape[0]
    block = math.gcd(row_count, 256)
    den_width = 128
    flops = 4 * row_count * key_count * width * heads
    return pl.pallas_call(
        functools.partial(prefix_kernel, heads=heads, head_dim=head_dim, scale=scale),
        grid=(row_count // block,),
        in_specs=[
            pl.BlockSpec((block, width), lambda i: (i, 0)),
            pl.BlockSpec((key_count, width), lambda i: (0, 0)),
            pl.BlockSpec((key_count, width), lambda i: (0, 0)),
            pl.BlockSpec((block, 1), lambda i: (i, 0)),
            pl.BlockSpec((1, key_count), lambda i: (0, 0)),
        ],
        out_specs=[
            pl.BlockSpec((block, width), lambda i: (i, 0)),
            pl.BlockSpec((block, den_width), lambda i: (i, 0)),
        ],
        out_shape=[
            jax.ShapeDtypeStruct((row_count, width), jnp.bfloat16),
            jax.ShapeDtypeStruct((row_count, den_width), jnp.bfloat16),
        ],
        cost_estimate=pl.CostEstimate(
            flops=flops,
            transcendentals=row_count * key_count * heads,
            bytes_accessed=2 * (row_count * width * 2 + 2 * key_count * width + row_count * den_width),
        ),
    )(queries, keys, values, row_group.reshape(row_count, 1), key_group.reshape(1, key_count))


def shards_columns(
    hidden_in,
    w_qkv,
    w_out,
    w_gate_up,
    w_down,
    scale_qk,
    scale_gate_up,
    eigen_rates,
    cache_keys,
    cache_values,
    page_table,
    request_group,
    suffix_len,
):
    slot_count, model_width = hidden_in.shape
    head_dim = model_width // HEADS
    score_scale = 1.0 / math.sqrt(head_dim)
    mp_count = lax.axis_size("mp")
    mp_index = lax.axis_index("mp")
    own_rows = slot_count // mp_count
    row_first = mp_index * own_rows
    shard_index = lax.axis_index("pages")
    pages_here, page_len = (cache_keys.shape[0], cache_keys.shape[1])
    pool_pages = page_table.shape[0]
    prefix_pages = pool_pages // GROUPS
    slot_valid, request, offset, group_id = slot_tables(suffix_len, request_group, slot_count)
    live_shard = lax.dynamic_index_in_dim(slot_valid, shard_index, 0, keepdims=False)
    request_shard = lax.dynamic_index_in_dim(request, shard_index, 0, keepdims=False)
    offset_shard = lax.dynamic_index_in_dim(offset, shard_index, 0, keepdims=False)
    position_shard = prefix_pages * page_len + offset_shard
    live_own = lax.dynamic_slice_in_dim(live_shard, row_first, own_rows, 0)
    request_own = lax.dynamic_slice_in_dim(request_shard, row_first, own_rows, 0)
    offset_own = lax.dynamic_slice_in_dim(offset_shard, row_first, own_rows, 0)
    position_own = lax.dynamic_slice_in_dim(position_shard, row_first, own_rows, 0)
    state_in = rms_rows(hidden_in.astype(jnp.float32)).astype(jnp.bfloat16)
    projected = jnp.einsum(
        "sd,jdc->jsc", state_in, w_qkv, preferred_element_type=jnp.float32
    ).astype(jnp.bfloat16)
    columns = lax.all_gather(projected, "mp", axis=2, tiled=True)
    query_raw = lax.dynamic_slice_in_dim(columns[0], row_first, own_rows, 0)
    key_raw, value_rows = (columns[1], columns[2])
    queries = head_norm(
        rotate(query_raw.astype(jnp.float32), position_own, HEADS), scale_qk, HEADS
    ).astype(jnp.bfloat16)
    keys_new = head_norm(
        rotate(key_raw.astype(jnp.float32), position_shard, HEADS), scale_qk, HEADS
    ).astype(jnp.bfloat16)
    query_heads = queries.reshape(own_rows, HEADS, head_dim)
    scores = (
        jnp.einsum(
            "qhd,khd->hqk",
            query_heads,
            keys_new.reshape(slot_count, HEADS, head_dim),
            preferred_element_type=jnp.float32,
        )
        * score_scale
    )
    allowed = (
        (request_own[:, None] == request_shard[None, :])
        & (offset_shard[None, :] <= offset_own[:, None])
        & live_own[:, None]
        & live_shard[None, :]
    )
    weights = jnp.where(allowed[None], jnp.exp(scores), 0.0)
    suffix_total = jnp.sum(weights, axis=-1)
    suffix_sum = jnp.einsum(
        "hqk,khd->qhd",
        weights.astype(jnp.bfloat16),
        value_rows.reshape(slot_count, HEADS, head_dim),
        preferred_element_type=jnp.float32,
    )
    physical = shard_index * pages_here + jnp.arange(pages_here, dtype=jnp.int32)
    matches = page_table[:, None] == physical[None, :]
    logical = jnp.sum(
        jnp.where(matches, jnp.arange(pool_pages, dtype=jnp.int32)[:, None], 0), axis=0
    )
    key_group = jnp.repeat(logical // prefix_pages, page_len)
    prefix_keys = head_norm(
        cache_keys.reshape(pages_here * page_len, model_width).astype(jnp.float32), scale_qk, HEADS
    ).astype(jnp.bfloat16)
    prefix_values = cache_values.reshape(pages_here * page_len, model_width)
    gathered = lax.all_gather(queries, "pages", axis=0, tiled=True)
    gathered_group = lax.dynamic_slice_in_dim(group_id, row_first, own_rows, 1).reshape(-1)
    row_count = own_rows * lax.axis_size("pages")
    block_rows = row_count if row_count <= 512 else math.gcd(row_count, 512)

    def attend_block(block_first):
        query_block = lax.dynamic_slice_in_dim(gathered, block_first, block_rows, 0)
        group_block = lax.dynamic_slice_in_dim(gathered_group, block_first, block_rows, 0)
        return prefix_block(
            query_block, group_block, prefix_keys, prefix_values, key_group, score_scale
        )

    block_starts = jnp.arange(row_count // block_rows, dtype=jnp.int32) * block_rows
    summed, weight_sum = lax.map(attend_block, block_starts)
    prefix_sum, prefix_total = lax.psum_scatter(
        (summed.reshape(row_count, model_width), weight_sum.reshape(row_count, HEADS)),
        "pages",
        scatter_dimension=0,
        tiled=True,
    )
    denominator = suffix_total.T + prefix_total + (1.0 - live_own.astype(jnp.float32))[:, None]
    mixed = (suffix_sum + prefix_sum.reshape(own_rows, HEADS, head_dim)) / denominator[:, :, None]
    attention = mixed.reshape(own_rows, model_width).astype(jnp.bfloat16)
    projected_out = jnp.dot(
        lax.all_gather(attention, "mp", axis=0, tiled=True),
        w_out,
        preferred_element_type=jnp.float32,
    )
    residual_in = state_in.astype(jnp.float32)
    state_mid = rms_rows(
        residual_in + eigen_rates[0][None, :] * (rms_rows(projected_out) - residual_in)
    ).astype(jnp.bfloat16)
    state_own = lax.dynamic_slice_in_dim(state_mid, row_first, own_rows, 0)
    gate_up = jnp.einsum("sd,jdf->jsf", state_mid, w_gate_up, preferred_element_type=jnp.float32)
    hidden = (
        jax.nn.silu(scale_gate_up[0][None, :] * gate_up[0])
        * (scale_gate_up[1][None, :] * gate_up[1])
    ).astype(jnp.bfloat16)
    feed_sum = lax.psum_scatter(
        jnp.dot(hidden, w_down, preferred_element_type=jnp.float32),
        "mp",
        scatter_dimension=0,
        tiled=True,
    )
    middle = state_own.astype(jnp.float32)
    result = rms_rows(middle + eigen_rates[1][None, :] * (rms_rows(feed_sum) - middle))
    return (live_own.astype(jnp.float32)[:, None] * result).astype(jnp.bfloat16)


def shards_heads(
    hidden_in,
    w_qkv,
    w_out,
    w_gate_up,
    w_down,
    scale_qk,
    scale_gate_up,
    eigen_rates,
    cache_keys,
    cache_values,
    page_table,
    request_group,
    suffix_len,
):
    slot_count, model_width = hidden_in.shape
    head_dim = model_width // HEADS
    score_scale = 1.0 / math.sqrt(head_dim)
    mp_count = lax.axis_size("mp")
    mp_index = lax.axis_index("mp")
    local_heads = HEADS // mp_count
    local_width = local_heads * head_dim
    own_rows = slot_count // mp_count
    row_first = mp_index * own_rows
    shard_index = lax.axis_index("pages")
    pages_here, page_len = (cache_keys.shape[0], cache_keys.shape[1])
    pool_pages = page_table.shape[0]
    prefix_pages = pool_pages // GROUPS
    slot_valid, request, offset, group_id = slot_tables(suffix_len, request_group, slot_count)
    live_shard = lax.dynamic_index_in_dim(slot_valid, shard_index, 0, keepdims=False)
    request_shard = lax.dynamic_index_in_dim(request, shard_index, 0, keepdims=False)
    offset_shard = lax.dynamic_index_in_dim(offset, shard_index, 0, keepdims=False)
    position_shard = prefix_pages * page_len + offset_shard
    live_own = lax.dynamic_slice_in_dim(live_shard, row_first, own_rows, 0)
    scale_local = lax.dynamic_slice_in_dim(scale_qk, mp_index * local_width, local_width, 0)
    state_in = rms_rows(hidden_in.astype(jnp.float32)).astype(jnp.bfloat16)
    projected = jnp.einsum(
        "sd,jdc->jsc", state_in, w_qkv, preferred_element_type=jnp.float32
    ).astype(jnp.bfloat16)
    queries = head_norm(
        rotate(projected[0].astype(jnp.float32), position_shard, local_heads), scale_local, local_heads
    ).astype(jnp.bfloat16)
    keys_new = head_norm(
        rotate(projected[1].astype(jnp.float32), position_shard, local_heads), scale_local, local_heads
    ).astype(jnp.bfloat16)
    value_rows = projected[2]
    gathered = lax.all_gather(queries, "pages", axis=0, tiled=True)
    scores = (
        jnp.einsum(
            "qhd,khd->hqk",
            queries.reshape(slot_count, local_heads, head_dim),
            keys_new.reshape(slot_count, local_heads, head_dim),
            preferred_element_type=jnp.float32,
        )
        * score_scale
    )
    allowed = (
        (request_shard[:, None] == request_shard[None, :])
        & (offset_shard[None, :] <= offset_shard[:, None])
        & live_shard[:, None]
        & live_shard[None, :]
    )
    weights = jnp.where(allowed[None], jnp.exp(scores), 0.0)
    suffix_total = jnp.sum(weights, axis=-1)
    suffix_sum = jnp.einsum(
        "hqk,khd->qhd",
        weights.astype(jnp.bfloat16),
        value_rows.reshape(slot_count, local_heads, head_dim),
        preferred_element_type=jnp.float32,
    )
    physical = shard_index * pages_here + jnp.arange(pages_here, dtype=jnp.int32)
    matches = page_table[:, None] == physical[None, :]
    logical = jnp.sum(
        jnp.where(matches, jnp.arange(pool_pages, dtype=jnp.int32)[:, None], 0), axis=0
    )
    key_group = jnp.repeat(logical // prefix_pages, page_len)
    cache_local = lax.dynamic_slice_in_dim(cache_keys, mp_index * local_width, local_width, 2)
    prefix_keys = head_norm(
        cache_local.reshape(pages_here * page_len, local_width).astype(jnp.float32),
        scale_local,
        local_heads,
    ).astype(jnp.bfloat16)
    prefix_values = lax.dynamic_slice_in_dim(
        cache_values, mp_index * local_width, local_width, 2
    ).reshape(pages_here * page_len, local_width)
    gathered_group = group_id.reshape(-1)
    row_count = gathered.shape[0]
    prefix_num, prefix_den = prefix_attention(
        gathered,
        prefix_keys,
        prefix_values,
        gathered_group,
        key_group,
        local_heads,
        head_dim,
        score_scale,
    )
    prefix_both = lax.psum_scatter(
        jnp.concatenate([prefix_num, prefix_den[:, :local_heads]], axis=1),
        "pages",
        scatter_dimension=0,
        tiled=True,
    ).astype(jnp.float32)
    prefix_sum = prefix_both[:, :local_width]
    prefix_total = prefix_both[:, local_width:]
    denominator = suffix_total.T + prefix_total + (1.0 - live_shard.astype(jnp.float32))[:, None]
    mixed = (suffix_sum + prefix_sum.reshape(slot_count, local_heads, head_dim)) / denominator[
        :, :, None
    ]
    attention_local = mixed.reshape(slot_count, local_width).astype(jnp.bfloat16)
    attention = lax.all_gather(attention_local, "mp", axis=1, tiled=True)
    projected_out = jnp.dot(attention, w_out, preferred_element_type=jnp.float32)
    residual_in = state_in.astype(jnp.float32)
    state_mid = rms_rows(
        residual_in + eigen_rates[0][None, :] * (rms_rows(projected_out) - residual_in)
    ).astype(jnp.bfloat16)
    state_own = lax.dynamic_slice_in_dim(state_mid, row_first, own_rows, 0)
    gate_up = jnp.einsum("sd,jdf->jsf", state_mid, w_gate_up, preferred_element_type=jnp.float32)
    hidden = (
        jax.nn.silu(scale_gate_up[0][None, :] * gate_up[0])
        * (scale_gate_up[1][None, :] * gate_up[1])
    ).astype(jnp.bfloat16)
    feed_sum = lax.psum_scatter(
        jnp.dot(hidden, w_down, preferred_element_type=jnp.float32).astype(jnp.bfloat16),
        "mp",
        scatter_dimension=0,
        tiled=True,
    ).astype(jnp.float32)
    middle = state_own.astype(jnp.float32)
    result = rms_rows(middle + eigen_rates[1][None, :] * (rms_rows(feed_sum) - middle))
    return (live_own.astype(jnp.float32)[:, None] * result).astype(jnp.bfloat16)


def solution(mesh):
    shards = shards_heads if HEADS % mesh.shape["mp"] == 0 else shards_columns
    return jax.shard_map(
        shards,
        mesh=mesh,
        in_specs=(
            P("pages", None),
            P(None, None, "mp"),
            P(),
            P(None, None, "mp"),
            P("mp", None),
            P(),
            P(None, "mp"),
            P(),
            P("pages", None, None),
            P("pages", None, None),
            P(),
            P(),
            P(),
        ),
        out_specs=P(("pages", "mp"), None),
        check_vma=False,
    )
```

```python
import math

import jax
import jax.numpy as jnp
from jax import lax
from jax.sharding import PartitionSpec as P

HEADS = 20
GROUPS = 8


EPSILON = 1e-06


def rms_rows(values_in):
    return values_in * lax.rsqrt(jnp.mean(values_in * values_in, axis=-1, keepdims=True) + EPSILON)


def head_norm(values_in, scale_vec, head_count):
    row_count, model_width = values_in.shape
    per_head = values_in.reshape(row_count, head_count, model_width // head_count)
    normed = per_head * lax.rsqrt(jnp.mean(per_head * per_head, axis=-1, keepdims=True) + EPSILON)
    return normed.reshape(row_count, model_width) * scale_vec[None, :]


def rotate(values_in, position, head_count):
    row_count, model_width = values_in.shape
    head_dim = model_width // head_count
    half_dim = head_dim // 2
    frequency = jnp.exp(
        jnp.arange(half_dim).astype(jnp.float32) * (-2.0 * math.log(10000.0) / head_dim)
    )
    rotation = position.astype(jnp.float32)[:, None] * frequency[None, :]
    cosine_table = jnp.cos(rotation)[:, None, :]
    sine_table = jnp.sin(rotation)[:, None, :]
    per_head = values_in.reshape(row_count, head_count, head_dim)
    lower_half = per_head[:, :, :half_dim]
    upper_half = per_head[:, :, half_dim:]
    turned = jnp.concatenate(
        [
            lower_half * cosine_table - upper_half * sine_table,
            upper_half * cosine_table + lower_half * sine_table,
        ],
        axis=-1,
    )
    return turned.reshape(row_count, model_width)


def slot_tables(suffix_len, request_group, slot_count):
    end_slots = jnp.cumsum(suffix_len, axis=1)
    start_slots = end_slots - suffix_len
    slot_ids = jnp.arange(slot_count)
    inside = (slot_ids[None, None, :] >= start_slots[:, :, None]) & (
        slot_ids[None, None, :] < end_slots[:, :, None]
    )
    request_ids = jnp.arange(suffix_len.shape[1])
    slot_valid = jnp.any(inside, axis=1)
    request = jnp.sum(jnp.where(inside, request_ids[None, :, None], 0), axis=1)
    offset = slot_ids[None, :] - jnp.sum(jnp.where(inside, start_slots[:, :, None], 0), axis=1)
    group_id = jnp.where(
        slot_valid, jnp.sum(jnp.where(inside, request_group[:, :, None], 0), axis=1), -1
    )
    return (slot_valid, request, offset, group_id)


def prefix_block(query_block, group_block, prefix_keys, prefix_values, key_group, score_scale):
    row_count, model_width = query_block.shape
    head_dim = model_width // HEADS
    query_heads = query_block.reshape(row_count, HEADS, head_dim)
    key_heads = prefix_keys.reshape(-1, HEADS, head_dim)
    value_heads = prefix_values.reshape(-1, HEADS, head_dim)
    scores = (
        jnp.einsum("qhd,khd->qhk", query_heads, key_heads, preferred_element_type=jnp.float32)
        * score_scale
    )
    allowed = group_block[:, None] == key_group[None, :]
    weights = jnp.where(allowed[:, None, :], jnp.exp(scores), 0.0)
    weight_sum = jnp.sum(weights, axis=-1)
    summed = jnp.einsum(
        "qhk,khd->qhd",
        weights.astype(jnp.bfloat16),
        value_heads,
        preferred_element_type=jnp.float32,
    )
    return (summed.reshape(row_count, model_width), weight_sum)


def shards_columns(
    hidden_in,
    w_qkv,
    w_out,
    w_gate_up,
    w_down,
    scale_qk,
    scale_gate_up,
    eigen_rates,
    cache_keys,
    cache_values,
    page_table,
    request_group,
    suffix_len,
):
    slot_count, model_width = hidden_in.shape
    head_dim = model_width // HEADS
    score_scale = 1.0 / math.sqrt(head_dim)
    mp_count = lax.axis_size("mp")
    mp_index = lax.axis_index("mp")
    own_rows = slot_count // mp_count
    row_first = mp_index * own_rows
    shard_index = lax.axis_index("pages")
    pages_here, page_len = (cache_keys.shape[0], cache_keys.shape[1])
    pool_pages = page_table.shape[0]
    prefix_pages = pool_pages // GROUPS
    slot_valid, request, offset, group_id = slot_tables(suffix_len, request_group, slot_count)
    live_shard = lax.dynamic_index_in_dim(slot_valid, shard_index, 0, keepdims=False)
    request_shard = lax.dynamic_index_in_dim(request, shard_index, 0, keepdims=False)
    offset_shard = lax.dynamic_index_in_dim(offset, shard_index, 0, keepdims=False)
    position_shard = prefix_pages * page_len + offset_shard
    live_own = lax.dynamic_slice_in_dim(live_shard, row_first, own_rows, 0)
    request_own = lax.dynamic_slice_in_dim(request_shard, row_first, own_rows, 0)
    offset_own = lax.dynamic_slice_in_dim(offset_shard, row_first, own_rows, 0)
    position_own = lax.dynamic_slice_in_dim(position_shard, row_first, own_rows, 0)
    state_in = rms_rows(hidden_in.astype(jnp.float32)).astype(jnp.bfloat16)
    projected = jnp.einsum(
        "sd,jdc->jsc", state_in, w_qkv, preferred_element_type=jnp.float32
    ).astype(jnp.bfloat16)
    columns = lax.all_gather(projected, "mp", axis=2, tiled=True)
    query_raw = lax.dynamic_slice_in_dim(columns[0], row_first, own_rows, 0)
    key_raw, value_rows = (columns[1], columns[2])
    queries = head_norm(
        rotate(query_raw.astype(jnp.float32), position_own, HEADS), scale_qk, HEADS
    ).astype(jnp.bfloat16)
    keys_new = head_norm(
        rotate(key_raw.astype(jnp.float32), position_shard, HEADS), scale_qk, HEADS
    ).astype(jnp.bfloat16)
    query_heads = queries.reshape(own_rows, HEADS, head_dim)
    scores = (
        jnp.einsum(
            "qhd,khd->hqk",
            query_heads,
            keys_new.reshape(slot_count, HEADS, head_dim),
            preferred_element_type=jnp.float32,
        )
        * score_scale
    )
    allowed = (
        (request_own[:, None] == request_shard[None, :])
        & (offset_shard[None, :] <= offset_own[:, None])
        & live_own[:, None]
        & live_shard[None, :]
    )
    weights = jnp.where(allowed[None], jnp.exp(scores), 0.0)
    suffix_total = jnp.sum(weights, axis=-1)
    suffix_sum = jnp.einsum(
        "hqk,khd->qhd",
        weights.astype(jnp.bfloat16),
        value_rows.reshape(slot_count, HEADS, head_dim),
        preferred_element_type=jnp.float32,
    )
    physical = shard_index * pages_here + jnp.arange(pages_here, dtype=jnp.int32)
    matches = page_table[:, None] == physical[None, :]
    logical = jnp.sum(
        jnp.where(matches, jnp.arange(pool_pages, dtype=jnp.int32)[:, None], 0), axis=0
    )
    key_group = jnp.repeat(logical // prefix_pages, page_len)
    prefix_keys = head_norm(
        cache_keys.reshape(pages_here * page_len, model_width).astype(jnp.float32), scale_qk, HEADS
    ).astype(jnp.bfloat16)
    prefix_values = cache_values.reshape(pages_here * page_len, model_width)
    gathered = lax.all_gather(queries, "pages", axis=0, tiled=True)
    gathered_group = lax.dynamic_slice_in_dim(group_id, row_first, own_rows, 1).reshape(-1)
    row_count = own_rows * lax.axis_size("pages")
    block_rows = row_count if row_count <= 512 else math.gcd(row_count, 512)

    def attend_block(block_first):
        query_block = lax.dynamic_slice_in_dim(gathered, block_first, block_rows, 0)
        group_block = lax.dynamic_slice_in_dim(gathered_group, block_first, block_rows, 0)
        return prefix_block(
            query_block, group_block, prefix_keys, prefix_values, key_group, score_scale
        )

    block_starts = jnp.arange(row_count // block_rows, dtype=jnp.int32) * block_rows
    summed, weight_sum = lax.map(attend_block, block_starts)
    prefix_sum, prefix_total = lax.psum_scatter(
        (summed.reshape(row_count, model_width), weight_sum.reshape(row_count, HEADS)),
        "pages",
        scatter_dimension=0,
        tiled=True,
    )
    denominator = suffix_total.T + prefix_total + (1.0 - live_own.astype(jnp.float32))[:, None]
    mixed = (suffix_sum + prefix_sum.reshape(own_rows, HEADS, head_dim)) / denominator[:, :, None]
    attention = mixed.reshape(own_rows, model_width).astype(jnp.bfloat16)
    projected_out = jnp.dot(
        lax.all_gather(attention, "mp", axis=0, tiled=True),
        w_out,
        preferred_element_type=jnp.float32,
    )
    residual_in = state_in.astype(jnp.float32)
    state_mid = rms_rows(
        residual_in + eigen_rates[0][None, :] * (rms_rows(projected_out) - residual_in)
    ).astype(jnp.bfloat16)
    state_own = lax.dynamic_slice_in_dim(state_mid, row_first, own_rows, 0)
    gate_up = jnp.einsum("sd,jdf->jsf", state_mid, w_gate_up, preferred_element_type=jnp.float32)
    hidden = (
        jax.nn.silu(scale_gate_up[0][None, :] * gate_up[0])
        * (scale_gate_up[1][None, :] * gate_up[1])
    ).astype(jnp.bfloat16)
    feed_sum = lax.psum_scatter(
        jnp.dot(hidden, w_down, preferred_element_type=jnp.float32),
        "mp",
        scatter_dimension=0,
        tiled=True,
    )
    middle = state_own.astype(jnp.float32)
    result = rms_rows(middle + eigen_rates[1][None, :] * (rms_rows(feed_sum) - middle))
    return (live_own.astype(jnp.float32)[:, None] * result).astype(jnp.bfloat16)


def shards_heads(
    hidden_in,
    w_qkv,
    w_out,
    w_gate_up,
    w_down,
    scale_qk,
    scale_gate_up,
    eigen_rates,
    cache_keys,
    cache_values,
    page_table,
    request_group,
    suffix_len,
):
    slot_count, model_width = hidden_in.shape
    head_dim = model_width // HEADS
    score_scale = 1.0 / math.sqrt(head_dim)
    mp_count = lax.axis_size("mp")
    mp_index = lax.axis_index("mp")
    local_heads = HEADS // mp_count
    local_width = local_heads * head_dim
    own_rows = slot_count // mp_count
    row_first = mp_index * own_rows
    shard_index = lax.axis_index("pages")
    pages_here, page_len = (cache_keys.shape[0], cache_keys.shape[1])
    pool_pages = page_table.shape[0]
    prefix_pages = pool_pages // GROUPS
    slot_valid, request, offset, group_id = slot_tables(suffix_len, request_group, slot_count)
    live_shard = lax.dynamic_index_in_dim(slot_valid, shard_index, 0, keepdims=False)
    request_shard = lax.dynamic_index_in_dim(request, shard_index, 0, keepdims=False)
    offset_shard = lax.dynamic_index_in_dim(offset, shard_index, 0, keepdims=False)
    position_shard = prefix_pages * page_len + offset_shard
    live_own = lax.dynamic_slice_in_dim(live_shard, row_first, own_rows, 0)
    scale_local = lax.dynamic_slice_in_dim(scale_qk, mp_index * local_width, local_width, 0)
    state_in = rms_rows(hidden_in.astype(jnp.float32)).astype(jnp.bfloat16)
    projected = jnp.einsum(
        "sd,jdc->jsc", state_in, w_qkv, preferred_element_type=jnp.float32
    ).astype(jnp.bfloat16)
    queries = head_norm(
        rotate(projected[0].astype(jnp.float32), position_shard, local_heads), scale_local, local_heads
    ).astype(jnp.bfloat16)
    keys_new = head_norm(
        rotate(projected[1].astype(jnp.float32), position_shard, local_heads), scale_local, local_heads
    ).astype(jnp.bfloat16)
    value_rows = projected[2]
    scores = (
        jnp.einsum(
            "qhd,khd->hqk",
            queries.reshape(slot_count, local_heads, head_dim),
            keys_new.reshape(slot_count, local_heads, head_dim),
            preferred_element_type=jnp.float32,
        )
        * score_scale
    )
    allowed = (
        (request_shard[:, None] == request_shard[None, :])
        & (offset_shard[None, :] <= offset_shard[:, None])
        & live_shard[:, None]
        & live_shard[None, :]
    )
    weights = jnp.where(allowed[None], jnp.exp(scores), 0.0)
    suffix_total = jnp.sum(weights, axis=-1)
    suffix_sum = jnp.einsum(
        "hqk,khd->qhd",
        weights.astype(jnp.bfloat16),
        value_rows.reshape(slot_count, local_heads, head_dim),
        preferred_element_type=jnp.float32,
    )
    physical = shard_index * pages_here + jnp.arange(pages_here, dtype=jnp.int32)
    matches = page_table[:, None] == physical[None, :]
    logical = jnp.sum(
        jnp.where(matches, jnp.arange(pool_pages, dtype=jnp.int32)[:, None], 0), axis=0
    )
    key_group = jnp.repeat(logical // prefix_pages, page_len)
    cache_local = lax.dynamic_slice_in_dim(cache_keys, mp_index * local_width, local_width, 2)
    prefix_keys = head_norm(
        cache_local.reshape(pages_here * page_len, local_width).astype(jnp.float32),
        scale_local,
        local_heads,
    ).astype(jnp.bfloat16)
    prefix_values = lax.dynamic_slice_in_dim(
        cache_values, mp_index * local_width, local_width, 2
    ).reshape(pages_here * page_len, local_width)
    key_heads = prefix_keys.reshape(-1, local_heads, head_dim)
    value_heads = prefix_values.reshape(-1, local_heads, head_dim)
    chunk_count = 2 if slot_count % 16 == 0 else 1
    chunk_rows = slot_count // chunk_count
    pages_count = lax.axis_size("pages")
    gathered_all = lax.all_gather(queries, "pages", axis=0, tiled=True).reshape(
        pages_count, slot_count, local_width
    )
    pieces = []
    for chunk in range(chunk_count):
        gathered = lax.slice_in_dim(
            gathered_all, chunk * chunk_rows, (chunk + 1) * chunk_rows, axis=1
        ).reshape(pages_count * chunk_rows, local_width)
        gathered_group = lax.slice_in_dim(
            group_id, chunk * chunk_rows, (chunk + 1) * chunk_rows, axis=1
        ).reshape(-1)
        row_count = gathered.shape[0]
        query_heads = gathered.reshape(row_count, local_heads, head_dim)
        prefix_scores = (
            jnp.einsum("qhd,khd->qhk", query_heads, key_heads, preferred_element_type=jnp.float32)
            * score_scale
        )
        prefix_allowed = gathered_group[:, None] == key_group[None, :]
        prefix_weights = jnp.where(prefix_allowed[:, None, :], jnp.exp(prefix_scores), 0.0)
        weight_sum = jnp.sum(prefix_weights, axis=-1)
        summed = jnp.einsum(
            "qhk,khd->qhd",
            prefix_weights.astype(jnp.bfloat16),
            value_heads,
            preferred_element_type=jnp.float32,
        )
        pieces.append(
            lax.psum_scatter(
                jnp.concatenate([summed.reshape(row_count, local_width), weight_sum], axis=1).astype(
                    jnp.bfloat16
                ),
                "pages",
                scatter_dimension=0,
                tiled=True,
            )
        )
    prefix_both = jnp.concatenate(pieces, axis=0).astype(jnp.float32)
    prefix_sum = prefix_both[:, :local_width]
    prefix_total = prefix_both[:, local_width:]
    denominator = suffix_total.T + prefix_total + (1.0 - live_shard.astype(jnp.float32))[:, None]
    mixed = (suffix_sum + prefix_sum.reshape(slot_count, local_heads, head_dim)) / denominator[
        :, :, None
    ]
    attention_local = mixed.reshape(slot_count, local_width).astype(jnp.bfloat16)
    attention = lax.all_gather(attention_local, "mp", axis=1, tiled=True)
    projected_out = jnp.dot(attention, w_out, preferred_element_type=jnp.float32)
    residual_in = state_in.astype(jnp.float32)
    state_mid = rms_rows(
        residual_in + eigen_rates[0][None, :] * (rms_rows(projected_out) - residual_in)
    ).astype(jnp.bfloat16)
    state_own = lax.dynamic_slice_in_dim(state_mid, row_first, own_rows, 0)
    gate_up = jnp.einsum("sd,jdf->jsf", state_mid, w_gate_up, preferred_element_type=jnp.float32)
    hidden = (
        jax.nn.silu(scale_gate_up[0][None, :] * gate_up[0])
        * (scale_gate_up[1][None, :] * gate_up[1])
    ).astype(jnp.bfloat16)
    feed_sum = lax.psum_scatter(
        jnp.dot(hidden, w_down, preferred_element_type=jnp.float32).astype(jnp.bfloat16),
        "mp",
        scatter_dimension=0,
        tiled=True,
    ).astype(jnp.float32)
    middle = state_own.astype(jnp.float32)
    result = rms_rows(middle + eigen_rates[1][None, :] * (rms_rows(feed_sum) - middle))
    return (live_own.astype(jnp.float32)[:, None] * result).astype(jnp.bfloat16)


def solution(mesh):
    shards = shards_heads if HEADS % mesh.shape["mp"] == 0 else shards_columns
    return jax.shard_map(
        shards,
        mesh=mesh,
        in_specs=(
            P("pages", None),
            P(None, None, "mp"),
            P(),
            P(None, None, "mp"),
            P("mp", None),
            P(),
            P(None, "mp"),
            P(),
            P("pages", None, None),
            P("pages", None, None),
            P(),
            P(),
            P(),
        ),
        out_specs=P(("pages", "mp"), None),
        check_vma=False,
    )
```

```python
import math

import jax
import jax.numpy as jnp
from jax import lax
from jax.sharding import PartitionSpec as P

HEADS = 20
GROUPS = 8


EPSILON = 1e-06


def rms_rows(values_in):
    return values_in * lax.rsqrt(jnp.mean(values_in * values_in, axis=-1, keepdims=True) + EPSILON)


def head_norm(values_in, scale_vec, head_count):
    row_count, model_width = values_in.shape
    per_head = values_in.reshape(row_count, head_count, model_width // head_count)
    normed = per_head * lax.rsqrt(jnp.mean(per_head * per_head, axis=-1, keepdims=True) + EPSILON)
    return normed.reshape(row_count, model_width) * scale_vec[None, :]


def rotate(values_in, position, head_count):
    row_count, model_width = values_in.shape
    head_dim = model_width // head_count
    half_dim = head_dim // 2
    frequency = jnp.exp(
        jnp.arange(half_dim).astype(jnp.float32) * (-2.0 * math.log(10000.0) / head_dim)
    )
    rotation = position.astype(jnp.float32)[:, None] * frequency[None, :]
    cosine_table = jnp.cos(rotation)[:, None, :]
    sine_table = jnp.sin(rotation)[:, None, :]
    per_head = values_in.reshape(row_count, head_count, head_dim)
    lower_half = per_head[:, :, :half_dim]
    upper_half = per_head[:, :, half_dim:]
    turned = jnp.concatenate(
        [
            lower_half * cosine_table - upper_half * sine_table,
            upper_half * cosine_table + lower_half * sine_table,
        ],
        axis=-1,
    )
    return turned.reshape(row_count, model_width)


def slot_tables(suffix_len, request_group, slot_count):
    end_slots = jnp.cumsum(suffix_len, axis=1)
    start_slots = end_slots - suffix_len
    slot_ids = jnp.arange(slot_count)
    inside = (slot_ids[None, None, :] >= start_slots[:, :, None]) & (
        slot_ids[None, None, :] < end_slots[:, :, None]
    )
    request_ids = jnp.arange(suffix_len.shape[1])
    slot_valid = jnp.any(inside, axis=1)
    request = jnp.sum(jnp.where(inside, request_ids[None, :, None], 0), axis=1)
    offset = slot_ids[None, :] - jnp.sum(jnp.where(inside, start_slots[:, :, None], 0), axis=1)
    group_id = jnp.where(
        slot_valid, jnp.sum(jnp.where(inside, request_group[:, :, None], 0), axis=1), -1
    )
    return (slot_valid, request, offset, group_id)


def prefix_block(query_block, group_block, prefix_keys, prefix_values, key_group, score_scale):
    row_count, model_width = query_block.shape
    head_dim = model_width // HEADS
    query_heads = query_block.reshape(row_count, HEADS, head_dim)
    key_heads = prefix_keys.reshape(-1, HEADS, head_dim)
    value_heads = prefix_values.reshape(-1, HEADS, head_dim)
    scores = (
        jnp.einsum("qhd,khd->qhk", query_heads, key_heads, preferred_element_type=jnp.float32)
        * score_scale
    )
    allowed = group_block[:, None] == key_group[None, :]
    weights = jnp.where(allowed[:, None, :], jnp.exp(scores), 0.0)
    weight_sum = jnp.sum(weights, axis=-1)
    summed = jnp.einsum(
        "qhk,khd->qhd",
        weights.astype(jnp.bfloat16),
        value_heads,
        preferred_element_type=jnp.float32,
    )
    return (summed.reshape(row_count, model_width), weight_sum)


def shards_columns(
    hidden_in,
    w_qkv,
    w_out,
    w_gate_up,
    w_down,
    scale_qk,
    scale_gate_up,
    eigen_rates,
    cache_keys,
    cache_values,
    page_table,
    request_group,
    suffix_len,
):
    slot_count, model_width = hidden_in.shape
    head_dim = model_width // HEADS
    score_scale = 1.0 / math.sqrt(head_dim)
    mp_count = lax.axis_size("mp")
    mp_index = lax.axis_index("mp")
    own_rows = slot_count // mp_count
    row_first = mp_index * own_rows
    shard_index = lax.axis_index("pages")
    pages_here, page_len = (cache_keys.shape[0], cache_keys.shape[1])
    pool_pages = page_table.shape[0]
    prefix_pages = pool_pages // GROUPS
    slot_valid, request, offset, group_id = slot_tables(suffix_len, request_group, slot_count)
    live_shard = lax.dynamic_index_in_dim(slot_valid, shard_index, 0, keepdims=False)
    request_shard = lax.dynamic_index_in_dim(request, shard_index, 0, keepdims=False)
    offset_shard = lax.dynamic_index_in_dim(offset, shard_index, 0, keepdims=False)
    position_shard = prefix_pages * page_len + offset_shard
    live_own = lax.dynamic_slice_in_dim(live_shard, row_first, own_rows, 0)
    request_own = lax.dynamic_slice_in_dim(request_shard, row_first, own_rows, 0)
    offset_own = lax.dynamic_slice_in_dim(offset_shard, row_first, own_rows, 0)
    position_own = lax.dynamic_slice_in_dim(position_shard, row_first, own_rows, 0)
    state_in = rms_rows(hidden_in.astype(jnp.float32)).astype(jnp.bfloat16)
    projected = jnp.einsum(
        "sd,jdc->jsc", state_in, w_qkv, preferred_element_type=jnp.float32
    ).astype(jnp.bfloat16)
    columns = lax.all_gather(projected, "mp", axis=2, tiled=True)
    query_raw = lax.dynamic_slice_in_dim(columns[0], row_first, own_rows, 0)
    key_raw, value_rows = (columns[1], columns[2])
    queries = head_norm(
        rotate(query_raw.astype(jnp.float32), position_own, HEADS), scale_qk, HEADS
    ).astype(jnp.bfloat16)
    keys_new = head_norm(
        rotate(key_raw.astype(jnp.float32), position_shard, HEADS), scale_qk, HEADS
    ).astype(jnp.bfloat16)
    query_heads = queries.reshape(own_rows, HEADS, head_dim)
    scores = (
        jnp.einsum(
            "qhd,khd->hqk",
            query_heads,
            keys_new.reshape(slot_count, HEADS, head_dim),
            preferred_element_type=jnp.float32,
        )
        * score_scale
    )
    allowed = (
        (request_own[:, None] == request_shard[None, :])
        & (offset_shard[None, :] <= offset_own[:, None])
        & live_own[:, None]
        & live_shard[None, :]
    )
    weights = jnp.where(allowed[None], jnp.exp(scores), 0.0)
    suffix_total = jnp.sum(weights, axis=-1)
    suffix_sum = jnp.einsum(
        "hqk,khd->qhd",
        weights.astype(jnp.bfloat16),
        value_rows.reshape(slot_count, HEADS, head_dim),
        preferred_element_type=jnp.float32,
    )
    physical = shard_index * pages_here + jnp.arange(pages_here, dtype=jnp.int32)
    matches = page_table[:, None] == physical[None, :]
    logical = jnp.sum(
        jnp.where(matches, jnp.arange(pool_pages, dtype=jnp.int32)[:, None], 0), axis=0
    )
    key_group = jnp.repeat(logical // prefix_pages, page_len)
    prefix_keys = head_norm(
        cache_keys.reshape(pages_here * page_len, model_width).astype(jnp.float32), scale_qk, HEADS
    ).astype(jnp.bfloat16)
    prefix_values = cache_values.reshape(pages_here * page_len, model_width)
    gathered = lax.all_gather(queries, "pages", axis=0, tiled=True)
    gathered_group = lax.dynamic_slice_in_dim(group_id, row_first, own_rows, 1).reshape(-1)
    row_count = own_rows * lax.axis_size("pages")
    block_rows = row_count if row_count <= 512 else math.gcd(row_count, 512)

    def attend_block(block_first):
        query_block = lax.dynamic_slice_in_dim(gathered, block_first, block_rows, 0)
        group_block = lax.dynamic_slice_in_dim(gathered_group, block_first, block_rows, 0)
        return prefix_block(
            query_block, group_block, prefix_keys, prefix_values, key_group, score_scale
        )

    block_starts = jnp.arange(row_count // block_rows, dtype=jnp.int32) * block_rows
    summed, weight_sum = lax.map(attend_block, block_starts)
    prefix_sum, prefix_total = lax.psum_scatter(
        (summed.reshape(row_count, model_width), weight_sum.reshape(row_count, HEADS)),
        "pages",
        scatter_dimension=0,
        tiled=True,
    )
    denominator = suffix_total.T + prefix_total + (1.0 - live_own.astype(jnp.float32))[:, None]
    mixed = (suffix_sum + prefix_sum.reshape(own_rows, HEADS, head_dim)) / denominator[:, :, None]
    attention = mixed.reshape(own_rows, model_width).astype(jnp.bfloat16)
    projected_out = jnp.dot(
        lax.all_gather(attention, "mp", axis=0, tiled=True),
        w_out,
        preferred_element_type=jnp.float32,
    )
    residual_in = state_in.astype(jnp.float32)
    state_mid = rms_rows(
        residual_in + eigen_rates[0][None, :] * (rms_rows(projected_out) - residual_in)
    ).astype(jnp.bfloat16)
    state_own = lax.dynamic_slice_in_dim(state_mid, row_first, own_rows, 0)
    gate_up = jnp.einsum("sd,jdf->jsf", state_mid, w_gate_up, preferred_element_type=jnp.float32)
    hidden = (
        jax.nn.silu(scale_gate_up[0][None, :] * gate_up[0])
        * (scale_gate_up[1][None, :] * gate_up[1])
    ).astype(jnp.bfloat16)
    feed_sum = lax.psum_scatter(
        jnp.dot(hidden, w_down, preferred_element_type=jnp.float32),
        "mp",
        scatter_dimension=0,
        tiled=True,
    )
    middle = state_own.astype(jnp.float32)
    result = rms_rows(middle + eigen_rates[1][None, :] * (rms_rows(feed_sum) - middle))
    return (live_own.astype(jnp.float32)[:, None] * result).astype(jnp.bfloat16)


def shards_heads(
    hidden_in,
    w_qkv,
    w_out,
    w_gate_up,
    w_down,
    scale_qk,
    scale_gate_up,
    eigen_rates,
    cache_keys,
    cache_values,
    page_table,
    request_group,
    suffix_len,
):
    slot_count, model_width = hidden_in.shape
    head_dim = model_width // HEADS
    score_scale = 1.0 / math.sqrt(head_dim)
    mp_count = lax.axis_size("mp")
    mp_index = lax.axis_index("mp")
    local_heads = HEADS // mp_count
    local_width = local_heads * head_dim
    own_rows = slot_count // mp_count
    row_first = mp_index * own_rows
    shard_index = lax.axis_index("pages")
    pages_here, page_len = (cache_keys.shape[0], cache_keys.shape[1])
    pool_pages = page_table.shape[0]
    prefix_pages = pool_pages // GROUPS
    slot_valid, request, offset, group_id = slot_tables(suffix_len, request_group, slot_count)
    live_shard = lax.dynamic_index_in_dim(slot_valid, shard_index, 0, keepdims=False)
    request_shard = lax.dynamic_index_in_dim(request, shard_index, 0, keepdims=False)
    offset_shard = lax.dynamic_index_in_dim(offset, shard_index, 0, keepdims=False)
    position_shard = prefix_pages * page_len + offset_shard
    live_own = lax.dynamic_slice_in_dim(live_shard, row_first, own_rows, 0)
    scale_local = lax.dynamic_slice_in_dim(scale_qk, mp_index * local_width, local_width, 0)
    state_in = rms_rows(hidden_in.astype(jnp.float32)).astype(jnp.bfloat16)
    projected = jnp.einsum(
        "sd,jdc->jsc", state_in, w_qkv, preferred_element_type=jnp.float32
    ).astype(jnp.bfloat16)
    queries = head_norm(
        rotate(projected[0].astype(jnp.float32), position_shard, local_heads), scale_local, local_heads
    ).astype(jnp.bfloat16)
    keys_new = head_norm(
        rotate(projected[1].astype(jnp.float32), position_shard, local_heads), scale_local, local_heads
    ).astype(jnp.bfloat16)
    value_rows = projected[2]
    gathered = lax.all_gather(queries, "pages", axis=0, tiled=True)
    scores = (
        jnp.einsum(
            "qhd,khd->hqk",
            queries.reshape(slot_count, local_heads, head_dim),
            keys_new.reshape(slot_count, local_heads, head_dim),
            preferred_element_type=jnp.float32,
        )
        * score_scale
    )
    allowed = (
        (request_shard[:, None] == request_shard[None, :])
        & (offset_shard[None, :] <= offset_shard[:, None])
        & live_shard[:, None]
        & live_shard[None, :]
    )
    weights = jnp.where(allowed[None], jnp.exp(scores), 0.0)
    suffix_total = jnp.sum(weights, axis=-1)
    suffix_sum = jnp.einsum(
        "hqk,khd->qhd",
        weights.astype(jnp.bfloat16),
        value_rows.reshape(slot_count, local_heads, head_dim),
        preferred_element_type=jnp.float32,
    )
    physical = shard_index * pages_here + jnp.arange(pages_here, dtype=jnp.int32)
    matches = page_table[:, None] == physical[None, :]
    logical = jnp.sum(
        jnp.where(matches, jnp.arange(pool_pages, dtype=jnp.int32)[:, None], 0), axis=0
    )
    key_group = jnp.repeat(logical // prefix_pages, page_len)
    cache_local = lax.dynamic_slice_in_dim(cache_keys, mp_index * local_width, local_width, 2)
    prefix_keys = head_norm(
        cache_local.reshape(pages_here * page_len, local_width).astype(jnp.float32),
        scale_local,
        local_heads,
    ).astype(jnp.bfloat16)
    prefix_values = lax.dynamic_slice_in_dim(
        cache_values, mp_index * local_width, local_width, 2
    ).reshape(pages_here * page_len, local_width)
    gathered_group = group_id.reshape(-1)
    row_count = gathered.shape[0]
    query_heads = gathered.reshape(row_count, local_heads, head_dim)
    key_heads = prefix_keys.reshape(-1, local_heads, head_dim)
    value_heads = prefix_values.reshape(-1, local_heads, head_dim)
    prefix_scores = (
        jnp.einsum("qhd,khd->qhk", query_heads, key_heads, preferred_element_type=jnp.float32)
        * score_scale
    )
    prefix_allowed = gathered_group[:, None] == key_group[None, :]
    prefix_weights = jnp.where(prefix_allowed[:, None, :], jnp.exp(prefix_scores), 0.0)
    weight_sum = jnp.sum(prefix_weights, axis=-1)
    summed = jnp.einsum(
        "qhk,khd->qhd",
        prefix_weights.astype(jnp.bfloat16),
        value_heads,
        preferred_element_type=jnp.float32,
    )
    pages_count = lax.axis_size("pages")
    prefix_parts = lax.all_to_all(
        jnp.concatenate([summed.reshape(row_count, local_width), weight_sum], axis=1).astype(
            jnp.bfloat16
        ),
        "pages",
        0,
        0,
        tiled=True,
    )
    prefix_both = jnp.sum(
        prefix_parts.reshape(pages_count, slot_count, local_width + local_heads).astype(jnp.float32),
        axis=0,
    )
    prefix_sum = prefix_both[:, :local_width]
    prefix_total = prefix_both[:, local_width:]
    denominator = suffix_total.T + prefix_total + (1.0 - live_shard.astype(jnp.float32))[:, None]
    mixed = (suffix_sum + prefix_sum.reshape(slot_count, local_heads, head_dim)) / denominator[
        :, :, None
    ]
    attention_local = mixed.reshape(slot_count, local_width).astype(jnp.bfloat16)
    attention = lax.all_gather(attention_local, "mp", axis=1, tiled=True)
    projected_out = jnp.dot(attention, w_out, preferred_element_type=jnp.float32)
    residual_in = state_in.astype(jnp.float32)
    state_mid = rms_rows(
        residual_in + eigen_rates[0][None, :] * (rms_rows(projected_out) - residual_in)
    ).astype(jnp.bfloat16)
    state_own = lax.dynamic_slice_in_dim(state_mid, row_first, own_rows, 0)
    gate_up = jnp.einsum("sd,jdf->jsf", state_mid, w_gate_up, preferred_element_type=jnp.float32)
    hidden = (
        jax.nn.silu(scale_gate_up[0][None, :] * gate_up[0])
        * (scale_gate_up[1][None, :] * gate_up[1])
    ).astype(jnp.bfloat16)
    feed_sum = lax.psum_scatter(
        jnp.dot(hidden, w_down, preferred_element_type=jnp.float32).astype(jnp.bfloat16),
        "mp",
        scatter_dimension=0,
        tiled=True,
    ).astype(jnp.float32)
    middle = state_own.astype(jnp.float32)
    result = rms_rows(middle + eigen_rates[1][None, :] * (rms_rows(feed_sum) - middle))
    return (live_own.astype(jnp.float32)[:, None] * result).astype(jnp.bfloat16)


def solution(mesh):
    shards = shards_heads if HEADS % mesh.shape["mp"] == 0 else shards_columns
    return jax.shard_map(
        shards,
        mesh=mesh,
        in_specs=(
            P("pages", None),
            P(None, None, "mp"),
            P(),
            P(None, None, "mp"),
            P("mp", None),
            P(),
            P(None, "mp"),
            P(),
            P("pages", None, None),
            P("pages", None, None),
            P(),
            P(),
            P(),
        ),
        out_specs=P(("pages", "mp"), None),
        check_vma=False,
    )
```

```python
import math

import jax
import jax.numpy as jnp
from jax import lax
from jax.sharding import PartitionSpec as P

HEADS = 20
GROUPS = 8


EPSILON = 1e-06


def rms_rows(values_in):
    return values_in * lax.rsqrt(jnp.mean(values_in * values_in, axis=-1, keepdims=True) + EPSILON)


def head_norm(values_in, scale_vec, head_count):
    row_count, model_width = values_in.shape
    per_head = values_in.reshape(row_count, head_count, model_width // head_count)
    normed = per_head * lax.rsqrt(jnp.mean(per_head * per_head, axis=-1, keepdims=True) + EPSILON)
    return normed.reshape(row_count, model_width) * scale_vec[None, :]


def rotate(values_in, position, head_count):
    row_count, model_width = values_in.shape
    head_dim = model_width // head_count
    half_dim = head_dim // 2
    frequency = jnp.exp(
        jnp.arange(half_dim).astype(jnp.float32) * (-2.0 * math.log(10000.0) / head_dim)
    )
    rotation = position.astype(jnp.float32)[:, None] * frequency[None, :]
    cosine_table = jnp.cos(rotation)[:, None, :]
    sine_table = jnp.sin(rotation)[:, None, :]
    per_head = values_in.reshape(row_count, head_count, head_dim)
    lower_half = per_head[:, :, :half_dim]
    upper_half = per_head[:, :, half_dim:]
    turned = jnp.concatenate(
        [
            lower_half * cosine_table - upper_half * sine_table,
            upper_half * cosine_table + lower_half * sine_table,
        ],
        axis=-1,
    )
    return turned.reshape(row_count, model_width)


def slot_tables(suffix_len, request_group, slot_count):
    end_slots = jnp.cumsum(suffix_len, axis=1)
    start_slots = end_slots - suffix_len
    slot_ids = jnp.arange(slot_count)
    inside = (slot_ids[None, None, :] >= start_slots[:, :, None]) & (
        slot_ids[None, None, :] < end_slots[:, :, None]
    )
    request_ids = jnp.arange(suffix_len.shape[1])
    slot_valid = jnp.any(inside, axis=1)
    request = jnp.sum(jnp.where(inside, request_ids[None, :, None], 0), axis=1)
    offset = slot_ids[None, :] - jnp.sum(jnp.where(inside, start_slots[:, :, None], 0), axis=1)
    group_id = jnp.where(
        slot_valid, jnp.sum(jnp.where(inside, request_group[:, :, None], 0), axis=1), -1
    )
    return (slot_valid, request, offset, group_id)


def prefix_block(query_block, group_block, prefix_keys, prefix_values, key_group, score_scale):
    row_count, model_width = query_block.shape
    head_dim = model_width // HEADS
    query_heads = query_block.reshape(row_count, HEADS, head_dim)
    key_heads = prefix_keys.reshape(-1, HEADS, head_dim)
    value_heads = prefix_values.reshape(-1, HEADS, head_dim)
    scores = (
        jnp.einsum("qhd,khd->qhk", query_heads, key_heads, preferred_element_type=jnp.float32)
        * score_scale
    )
    allowed = group_block[:, None] == key_group[None, :]
    weights = jnp.where(allowed[:, None, :], jnp.exp(scores), 0.0)
    weight_sum = jnp.sum(weights, axis=-1)
    summed = jnp.einsum(
        "qhk,khd->qhd",
        weights.astype(jnp.bfloat16),
        value_heads,
        preferred_element_type=jnp.float32,
    )
    return (summed.reshape(row_count, model_width), weight_sum)


def shards_columns(
    hidden_in,
    w_qkv,
    w_out,
    w_gate_up,
    w_down,
    scale_qk,
    scale_gate_up,
    eigen_rates,
    cache_keys,
    cache_values,
    page_table,
    request_group,
    suffix_len,
):
    slot_count, model_width = hidden_in.shape
    head_dim = model_width // HEADS
    score_scale = 1.0 / math.sqrt(head_dim)
    mp_count = lax.axis_size("mp")
    mp_index = lax.axis_index("mp")
    own_rows = slot_count // mp_count
    row_first = mp_index * own_rows
    shard_index = lax.axis_index("pages")
    pages_here, page_len = (cache_keys.shape[0], cache_keys.shape[1])
    pool_pages = page_table.shape[0]
    prefix_pages = pool_pages // GROUPS
    slot_valid, request, offset, group_id = slot_tables(suffix_len, request_group, slot_count)
    live_shard = lax.dynamic_index_in_dim(slot_valid, shard_index, 0, keepdims=False)
    request_shard = lax.dynamic_index_in_dim(request, shard_index, 0, keepdims=False)
    offset_shard = lax.dynamic_index_in_dim(offset, shard_index, 0, keepdims=False)
    position_shard = prefix_pages * page_len + offset_shard
    live_own = lax.dynamic_slice_in_dim(live_shard, row_first, own_rows, 0)
    request_own = lax.dynamic_slice_in_dim(request_shard, row_first, own_rows, 0)
    offset_own = lax.dynamic_slice_in_dim(offset_shard, row_first, own_rows, 0)
    position_own = lax.dynamic_slice_in_dim(position_shard, row_first, own_rows, 0)
    state_in = rms_rows(hidden_in.astype(jnp.float32)).astype(jnp.bfloat16)
    projected = jnp.einsum(
        "sd,jdc->jsc", state_in, w_qkv, preferred_element_type=jnp.float32
    ).astype(jnp.bfloat16)
    columns = lax.all_gather(projected, "mp", axis=2, tiled=True)
    query_raw = lax.dynamic_slice_in_dim(columns[0], row_first, own_rows, 0)
    key_raw, value_rows = (columns[1], columns[2])
    queries = head_norm(
        rotate(query_raw.astype(jnp.float32), position_own, HEADS), scale_qk, HEADS
    ).astype(jnp.bfloat16)
    keys_new = head_norm(
        rotate(key_raw.astype(jnp.float32), position_shard, HEADS), scale_qk, HEADS
    ).astype(jnp.bfloat16)
    query_heads = queries.reshape(own_rows, HEADS, head_dim)
    scores = (
        jnp.einsum(
            "qhd,khd->hqk",
            query_heads,
            keys_new.reshape(slot_count, HEADS, head_dim),
            preferred_element_type=jnp.float32,
        )
        * score_scale
    )
    allowed = (
        (request_own[:, None] == request_shard[None, :])
        & (offset_shard[None, :] <= offset_own[:, None])
        & live_own[:, None]
        & live_shard[None, :]
    )
    weights = jnp.where(allowed[None], jnp.exp(scores), 0.0)
    suffix_total = jnp.sum(weights, axis=-1)
    suffix_sum = jnp.einsum(
        "hqk,khd->qhd",
        weights.astype(jnp.bfloat16),
        value_rows.reshape(slot_count, HEADS, head_dim),
        preferred_element_type=jnp.float32,
    )
    physical = shard_index * pages_here + jnp.arange(pages_here, dtype=jnp.int32)
    matches = page_table[:, None] == physical[None, :]
    logical = jnp.sum(
        jnp.where(matches, jnp.arange(pool_pages, dtype=jnp.int32)[:, None], 0), axis=0
    )
    key_group = jnp.repeat(logical // prefix_pages, page_len)
    prefix_keys = head_norm(
        cache_keys.reshape(pages_here * page_len, model_width).astype(jnp.float32), scale_qk, HEADS
    ).astype(jnp.bfloat16)
    prefix_values = cache_values.reshape(pages_here * page_len, model_width)
    gathered = lax.all_gather(queries, "pages", axis=0, tiled=True)
    gathered_group = lax.dynamic_slice_in_dim(group_id, row_first, own_rows, 1).reshape(-1)
    row_count = own_rows * lax.axis_size("pages")
    block_rows = row_count if row_count <= 512 else math.gcd(row_count, 512)

    def attend_block(block_first):
        query_block = lax.dynamic_slice_in_dim(gathered, block_first, block_rows, 0)
        group_block = lax.dynamic_slice_in_dim(gathered_group, block_first, block_rows, 0)
        return prefix_block(
            query_block, group_block, prefix_keys, prefix_values, key_group, score_scale
        )

    block_starts = jnp.arange(row_count // block_rows, dtype=jnp.int32) * block_rows
    summed, weight_sum = lax.map(attend_block, block_starts)
    prefix_sum, prefix_total = lax.psum_scatter(
        (summed.reshape(row_count, model_width), weight_sum.reshape(row_count, HEADS)),
        "pages",
        scatter_dimension=0,
        tiled=True,
    )
    denominator = suffix_total.T + prefix_total + (1.0 - live_own.astype(jnp.float32))[:, None]
    mixed = (suffix_sum + prefix_sum.reshape(own_rows, HEADS, head_dim)) / denominator[:, :, None]
    attention = mixed.reshape(own_rows, model_width).astype(jnp.bfloat16)
    projected_out = jnp.dot(
        lax.all_gather(attention, "mp", axis=0, tiled=True),
        w_out,
        preferred_element_type=jnp.float32,
    )
    residual_in = state_in.astype(jnp.float32)
    state_mid = rms_rows(
        residual_in + eigen_rates[0][None, :] * (rms_rows(projected_out) - residual_in)
    ).astype(jnp.bfloat16)
    state_own = lax.dynamic_slice_in_dim(state_mid, row_first, own_rows, 0)
    gate_up = jnp.einsum("sd,jdf->jsf", state_mid, w_gate_up, preferred_element_type=jnp.float32)
    hidden = (
        jax.nn.silu(scale_gate_up[0][None, :] * gate_up[0])
        * (scale_gate_up[1][None, :] * gate_up[1])
    ).astype(jnp.bfloat16)
    feed_sum = lax.psum_scatter(
        jnp.dot(hidden, w_down, preferred_element_type=jnp.float32),
        "mp",
        scatter_dimension=0,
        tiled=True,
    )
    middle = state_own.astype(jnp.float32)
    result = rms_rows(middle + eigen_rates[1][None, :] * (rms_rows(feed_sum) - middle))
    return (live_own.astype(jnp.float32)[:, None] * result).astype(jnp.bfloat16)


def shards_heads(
    hidden_in,
    w_qkv,
    w_out,
    w_gate_up,
    w_down,
    scale_qk,
    scale_gate_up,
    eigen_rates,
    cache_keys,
    cache_values,
    page_table,
    request_group,
    suffix_len,
):
    slot_count, model_width = hidden_in.shape
    head_dim = model_width // HEADS
    score_scale = 1.0 / math.sqrt(head_dim)
    mp_count = lax.axis_size("mp")
    mp_index = lax.axis_index("mp")
    local_heads = HEADS // mp_count
    local_width = local_heads * head_dim
    own_rows = slot_count // mp_count
    row_first = mp_index * own_rows
    shard_index = lax.axis_index("pages")
    pages_here, page_len = (cache_keys.shape[0], cache_keys.shape[1])
    pool_pages = page_table.shape[0]
    prefix_pages = pool_pages // GROUPS
    slot_valid, request, offset, group_id = slot_tables(suffix_len, request_group, slot_count)
    live_shard = lax.dynamic_index_in_dim(slot_valid, shard_index, 0, keepdims=False)
    request_shard = lax.dynamic_index_in_dim(request, shard_index, 0, keepdims=False)
    offset_shard = lax.dynamic_index_in_dim(offset, shard_index, 0, keepdims=False)
    position_shard = prefix_pages * page_len + offset_shard
    live_own = lax.dynamic_slice_in_dim(live_shard, row_first, own_rows, 0)
    scale_local = lax.dynamic_slice_in_dim(scale_qk, mp_index * local_width, local_width, 0)
    state_in = rms_rows(hidden_in.astype(jnp.float32)).astype(jnp.bfloat16)
    projected = jnp.einsum(
        "sd,jdc->jsc", state_in, w_qkv, preferred_element_type=jnp.float32
    ).astype(jnp.bfloat16)
    queries = head_norm(
        rotate(projected[0].astype(jnp.float32), position_shard, local_heads), scale_local, local_heads
    ).astype(jnp.bfloat16)
    keys_new = head_norm(
        rotate(projected[1].astype(jnp.float32), position_shard, local_heads), scale_local, local_heads
    ).astype(jnp.bfloat16)
    value_rows = projected[2]
    gathered = lax.all_gather(queries, "pages", axis=0, tiled=True)
    scores = (
        jnp.einsum(
            "qhd,khd->hqk",
            queries.reshape(slot_count, local_heads, head_dim),
            keys_new.reshape(slot_count, local_heads, head_dim),
            preferred_element_type=jnp.float32,
        )
        * score_scale
    )
    allowed = (
        (request_shard[:, None] == request_shard[None, :])
        & (offset_shard[None, :] <= offset_shard[:, None])
        & live_shard[:, None]
        & live_shard[None, :]
    )
    weights = jnp.where(allowed[None], jnp.exp(scores), 0.0)
    suffix_total = jnp.sum(weights, axis=-1)
    suffix_sum = jnp.einsum(
        "hqk,khd->qhd",
        weights.astype(jnp.bfloat16),
        value_rows.reshape(slot_count, local_heads, head_dim),
        preferred_element_type=jnp.float32,
    )
    physical = shard_index * pages_here + jnp.arange(pages_here, dtype=jnp.int32)
    matches = page_table[:, None] == physical[None, :]
    logical = jnp.sum(
        jnp.where(matches, jnp.arange(pool_pages, dtype=jnp.int32)[:, None], 0), axis=0
    )
    key_group = jnp.repeat(logical // prefix_pages, page_len)
    cache_local = lax.dynamic_slice_in_dim(cache_keys, mp_index * local_width, local_width, 2)
    prefix_keys = head_norm(
        cache_local.reshape(pages_here * page_len, local_width).astype(jnp.float32),
        scale_local,
        local_heads,
    ).astype(jnp.bfloat16)
    prefix_values = lax.dynamic_slice_in_dim(
        cache_values, mp_index * local_width, local_width, 2
    ).reshape(pages_here * page_len, local_width)
    gathered_group = group_id.reshape(-1)
    row_count = gathered.shape[0]
    query_heads = gathered.reshape(row_count, local_heads, head_dim)
    key_heads = prefix_keys.reshape(-1, local_heads, head_dim)
    value_heads = prefix_values.reshape(-1, local_heads, head_dim)
    prefix_scores = (
        jnp.einsum("qhd,khd->qhk", query_heads, key_heads, preferred_element_type=jnp.float32)
        * score_scale
    )
    prefix_allowed = gathered_group[:, None] == key_group[None, :]
    prefix_weights = jnp.where(prefix_allowed[:, None, :], jnp.exp(prefix_scores), 0.0)
    weight_sum = jnp.sum(prefix_weights, axis=-1)
    summed = jnp.einsum(
        "qhk,khd->qhd",
        prefix_weights.astype(jnp.bfloat16),
        value_heads,
        preferred_element_type=jnp.float32,
    )
    pages_count = lax.axis_size("pages")
    prefix_parts = lax.all_to_all(
        jnp.concatenate([summed.reshape(row_count, local_width), weight_sum], axis=1).astype(
            jnp.bfloat16
        ),
        "pages",
        0,
        0,
        tiled=True,
    )
    prefix_both = jnp.sum(
        prefix_parts.reshape(pages_count, slot_count, local_width + local_heads).astype(jnp.float32),
        axis=0,
    )
    prefix_sum = prefix_both[:, :local_width]
    prefix_total = prefix_both[:, local_width:]
    denominator = suffix_total.T + prefix_total + (1.0 - live_shard.astype(jnp.float32))[:, None]
    mixed = (suffix_sum + prefix_sum.reshape(slot_count, local_heads, head_dim)) / denominator[
        :, :, None
    ]
    attention_local = mixed.reshape(slot_count, local_width).astype(jnp.bfloat16)
    attention_parts = lax.all_to_all(
        jnp.tile(attention_local, (mp_count, 1)), "mp", 0, 0, tiled=True
    ).reshape(mp_count, slot_count, local_width)
    attention = jnp.transpose(attention_parts, (1, 0, 2)).reshape(slot_count, model_width)
    projected_out = jnp.dot(attention, w_out, preferred_element_type=jnp.float32)
    residual_in = state_in.astype(jnp.float32)
    state_mid = rms_rows(
        residual_in + eigen_rates[0][None, :] * (rms_rows(projected_out) - residual_in)
    ).astype(jnp.bfloat16)
    state_own = lax.dynamic_slice_in_dim(state_mid, row_first, own_rows, 0)
    gate_up = jnp.einsum("sd,jdf->jsf", state_mid, w_gate_up, preferred_element_type=jnp.float32)
    hidden = (
        jax.nn.silu(scale_gate_up[0][None, :] * gate_up[0])
        * (scale_gate_up[1][None, :] * gate_up[1])
    ).astype(jnp.bfloat16)
    feed_parts = lax.all_to_all(
        jnp.dot(hidden, w_down, preferred_element_type=jnp.float32).astype(jnp.bfloat16),
        "mp",
        0,
        0,
        tiled=True,
    )
    feed_sum = jnp.sum(
        feed_parts.reshape(mp_count, own_rows, model_width).astype(jnp.float32), axis=0
    )
    middle = state_own.astype(jnp.float32)
    result = rms_rows(middle + eigen_rates[1][None, :] * (rms_rows(feed_sum) - middle))
    return (live_own.astype(jnp.float32)[:, None] * result).astype(jnp.bfloat16)


def solution(mesh):
    shards = shards_heads if HEADS % mesh.shape["mp"] == 0 else shards_columns
    return jax.shard_map(
        shards,
        mesh=mesh,
        in_specs=(
            P("pages", None),
            P(None, None, "mp"),
            P(),
            P(None, None, "mp"),
            P("mp", None),
            P(),
            P(None, "mp"),
            P(),
            P("pages", None, None),
            P("pages", None, None),
            P(),
            P(),
            P(),
        ),
        out_specs=P(("pages", "mp"), None),
        check_vma=False,
    )
```

```python
import math

import jax
import jax.numpy as jnp
from jax import lax
from jax.sharding import PartitionSpec as P

HEADS = 20
GROUPS = 8


EPSILON = 1e-06


def rms_rows(values_in):
    return values_in * lax.rsqrt(jnp.mean(values_in * values_in, axis=-1, keepdims=True) + EPSILON)


def head_norm(values_in, scale_vec, head_count):
    row_count, model_width = values_in.shape
    per_head = values_in.reshape(row_count, head_count, model_width // head_count)
    normed = per_head * lax.rsqrt(jnp.mean(per_head * per_head, axis=-1, keepdims=True) + EPSILON)
    return normed.reshape(row_count, model_width) * scale_vec[None, :]


def rotate(values_in, position, head_count):
    row_count, model_width = values_in.shape
    head_dim = model_width // head_count
    half_dim = head_dim // 2
    frequency = jnp.exp(
        jnp.arange(half_dim).astype(jnp.float32) * (-2.0 * math.log(10000.0) / head_dim)
    )
    rotation = position.astype(jnp.float32)[:, None] * frequency[None, :]
    cosine_table = jnp.cos(rotation)[:, None, :]
    sine_table = jnp.sin(rotation)[:, None, :]
    per_head = values_in.reshape(row_count, head_count, head_dim)
    lower_half = per_head[:, :, :half_dim]
    upper_half = per_head[:, :, half_dim:]
    turned = jnp.concatenate(
        [
            lower_half * cosine_table - upper_half * sine_table,
            upper_half * cosine_table + lower_half * sine_table,
        ],
        axis=-1,
    )
    return turned.reshape(row_count, model_width)


def slot_tables(suffix_len, request_group, slot_count):
    end_slots = jnp.cumsum(suffix_len, axis=1)
    start_slots = end_slots - suffix_len
    slot_ids = jnp.arange(slot_count)
    inside = (slot_ids[None, None, :] >= start_slots[:, :, None]) & (
        slot_ids[None, None, :] < end_slots[:, :, None]
    )
    request_ids = jnp.arange(suffix_len.shape[1])
    slot_valid = jnp.any(inside, axis=1)
    request = jnp.sum(jnp.where(inside, request_ids[None, :, None], 0), axis=1)
    offset = slot_ids[None, :] - jnp.sum(jnp.where(inside, start_slots[:, :, None], 0), axis=1)
    group_id = jnp.where(
        slot_valid, jnp.sum(jnp.where(inside, request_group[:, :, None], 0), axis=1), -1
    )
    return (slot_valid, request, offset, group_id)


def prefix_block(query_block, group_block, prefix_keys, prefix_values, key_group, score_scale):
    row_count, model_width = query_block.shape
    head_dim = model_width // HEADS
    query_heads = query_block.reshape(row_count, HEADS, head_dim)
    key_heads = prefix_keys.reshape(-1, HEADS, head_dim)
    value_heads = prefix_values.reshape(-1, HEADS, head_dim)
    scores = (
        jnp.einsum("qhd,khd->qhk", query_heads, key_heads, preferred_element_type=jnp.float32)
        * score_scale
    )
    allowed = group_block[:, None] == key_group[None, :]
    weights = jnp.where(allowed[:, None, :], jnp.exp(scores), 0.0)
    weight_sum = jnp.sum(weights, axis=-1)
    summed = jnp.einsum(
        "qhk,khd->qhd",
        weights.astype(jnp.bfloat16),
        value_heads,
        preferred_element_type=jnp.float32,
    )
    return (summed.reshape(row_count, model_width), weight_sum)


def shards_columns(
    hidden_in,
    w_qkv,
    w_out,
    w_gate_up,
    w_down,
    scale_qk,
    scale_gate_up,
    eigen_rates,
    cache_keys,
    cache_values,
    page_table,
    request_group,
    suffix_len,
):
    slot_count, model_width = hidden_in.shape
    head_dim = model_width // HEADS
    score_scale = 1.0 / math.sqrt(head_dim)
    mp_count = lax.axis_size("mp")
    mp_index = lax.axis_index("mp")
    own_rows = slot_count // mp_count
    row_first = mp_index * own_rows
    shard_index = lax.axis_index("pages")
    pages_here, page_len = (cache_keys.shape[0], cache_keys.shape[1])
    pool_pages = page_table.shape[0]
    prefix_pages = pool_pages // GROUPS
    slot_valid, request, offset, group_id = slot_tables(suffix_len, request_group, slot_count)
    live_shard = lax.dynamic_index_in_dim(slot_valid, shard_index, 0, keepdims=False)
    request_shard = lax.dynamic_index_in_dim(request, shard_index, 0, keepdims=False)
    offset_shard = lax.dynamic_index_in_dim(offset, shard_index, 0, keepdims=False)
    position_shard = prefix_pages * page_len + offset_shard
    live_own = lax.dynamic_slice_in_dim(live_shard, row_first, own_rows, 0)
    request_own = lax.dynamic_slice_in_dim(request_shard, row_first, own_rows, 0)
    offset_own = lax.dynamic_slice_in_dim(offset_shard, row_first, own_rows, 0)
    position_own = lax.dynamic_slice_in_dim(position_shard, row_first, own_rows, 0)
    state_in = rms_rows(hidden_in.astype(jnp.float32)).astype(jnp.bfloat16)
    projected = jnp.einsum(
        "sd,jdc->jsc", state_in, w_qkv, preferred_element_type=jnp.float32
    ).astype(jnp.bfloat16)
    columns = lax.all_gather(projected, "mp", axis=2, tiled=True)
    query_raw = lax.dynamic_slice_in_dim(columns[0], row_first, own_rows, 0)
    key_raw, value_rows = (columns[1], columns[2])
    queries = head_norm(
        rotate(query_raw.astype(jnp.float32), position_own, HEADS), scale_qk, HEADS
    ).astype(jnp.bfloat16)
    keys_new = head_norm(
        rotate(key_raw.astype(jnp.float32), position_shard, HEADS), scale_qk, HEADS
    ).astype(jnp.bfloat16)
    query_heads = queries.reshape(own_rows, HEADS, head_dim)
    scores = (
        jnp.einsum(
            "qhd,khd->hqk",
            query_heads,
            keys_new.reshape(slot_count, HEADS, head_dim),
            preferred_element_type=jnp.float32,
        )
        * score_scale
    )
    allowed = (
        (request_own[:, None] == request_shard[None, :])
        & (offset_shard[None, :] <= offset_own[:, None])
        & live_own[:, None]
        & live_shard[None, :]
    )
    weights = jnp.where(allowed[None], jnp.exp(scores), 0.0)
    suffix_total = jnp.sum(weights, axis=-1)
    suffix_sum = jnp.einsum(
        "hqk,khd->qhd",
        weights.astype(jnp.bfloat16),
        value_rows.reshape(slot_count, HEADS, head_dim),
        preferred_element_type=jnp.float32,
    )
    physical = shard_index * pages_here + jnp.arange(pages_here, dtype=jnp.int32)
    matches = page_table[:, None] == physical[None, :]
    logical = jnp.sum(
        jnp.where(matches, jnp.arange(pool_pages, dtype=jnp.int32)[:, None], 0), axis=0
    )
    key_group = jnp.repeat(logical // prefix_pages, page_len)
    prefix_keys = head_norm(
        cache_keys.reshape(pages_here * page_len, model_width).astype(jnp.float32), scale_qk, HEADS
    ).astype(jnp.bfloat16)
    prefix_values = cache_values.reshape(pages_here * page_len, model_width)
    gathered = lax.all_gather(queries, "pages", axis=0, tiled=True)
    gathered_group = lax.dynamic_slice_in_dim(group_id, row_first, own_rows, 1).reshape(-1)
    row_count = own_rows * lax.axis_size("pages")
    block_rows = row_count if row_count <= 512 else math.gcd(row_count, 512)

    def attend_block(block_first):
        query_block = lax.dynamic_slice_in_dim(gathered, block_first, block_rows, 0)
        group_block = lax.dynamic_slice_in_dim(gathered_group, block_first, block_rows, 0)
        return prefix_block(
            query_block, group_block, prefix_keys, prefix_values, key_group, score_scale
        )

    block_starts = jnp.arange(row_count // block_rows, dtype=jnp.int32) * block_rows
    summed, weight_sum = lax.map(attend_block, block_starts)
    prefix_sum, prefix_total = lax.psum_scatter(
        (summed.reshape(row_count, model_width), weight_sum.reshape(row_count, HEADS)),
        "pages",
        scatter_dimension=0,
        tiled=True,
    )
    denominator = suffix_total.T + prefix_total + (1.0 - live_own.astype(jnp.float32))[:, None]
    mixed = (suffix_sum + prefix_sum.reshape(own_rows, HEADS, head_dim)) / denominator[:, :, None]
    attention = mixed.reshape(own_rows, model_width).astype(jnp.bfloat16)
    projected_out = jnp.dot(
        lax.all_gather(attention, "mp", axis=0, tiled=True),
        w_out,
        preferred_element_type=jnp.float32,
    )
    residual_in = state_in.astype(jnp.float32)
    state_mid = rms_rows(
        residual_in + eigen_rates[0][None, :] * (rms_rows(projected_out) - residual_in)
    ).astype(jnp.bfloat16)
    state_own = lax.dynamic_slice_in_dim(state_mid, row_first, own_rows, 0)
    gate_up = jnp.einsum("sd,jdf->jsf", state_mid, w_gate_up, preferred_element_type=jnp.float32)
    hidden = (
        jax.nn.silu(scale_gate_up[0][None, :] * gate_up[0])
        * (scale_gate_up[1][None, :] * gate_up[1])
    ).astype(jnp.bfloat16)
    feed_sum = lax.psum_scatter(
        jnp.dot(hidden, w_down, preferred_element_type=jnp.float32),
        "mp",
        scatter_dimension=0,
        tiled=True,
    )
    middle = state_own.astype(jnp.float32)
    result = rms_rows(middle + eigen_rates[1][None, :] * (rms_rows(feed_sum) - middle))
    return (live_own.astype(jnp.float32)[:, None] * result).astype(jnp.bfloat16)


def shards_heads(
    hidden_in,
    w_qkv,
    w_out,
    w_gate_up,
    w_down,
    scale_qk,
    scale_gate_up,
    eigen_rates,
    cache_keys,
    cache_values,
    page_table,
    request_group,
    suffix_len,
):
    slot_count, model_width = hidden_in.shape
    head_dim = model_width // HEADS
    score_scale = 1.0 / math.sqrt(head_dim)
    mp_count = lax.axis_size("mp")
    mp_index = lax.axis_index("mp")
    local_heads = HEADS // mp_count
    local_width = local_heads * head_dim
    own_rows = slot_count // mp_count
    row_first = mp_index * own_rows
    shard_index = lax.axis_index("pages")
    pages_here, page_len = (cache_keys.shape[0], cache_keys.shape[1])
    pool_pages = page_table.shape[0]
    prefix_pages = pool_pages // GROUPS
    slot_valid, request, offset, group_id = slot_tables(suffix_len, request_group, slot_count)
    live_shard = lax.dynamic_index_in_dim(slot_valid, shard_index, 0, keepdims=False)
    request_shard = lax.dynamic_index_in_dim(request, shard_index, 0, keepdims=False)
    offset_shard = lax.dynamic_index_in_dim(offset, shard_index, 0, keepdims=False)
    position_shard = prefix_pages * page_len + offset_shard
    live_own = lax.dynamic_slice_in_dim(live_shard, row_first, own_rows, 0)
    scale_local = lax.dynamic_slice_in_dim(scale_qk, mp_index * local_width, local_width, 0)
    state_in = rms_rows(hidden_in.astype(jnp.float32)).astype(jnp.bfloat16)
    projected = jnp.einsum(
        "sd,jdc->jsc", state_in, w_qkv, preferred_element_type=jnp.float32
    ).astype(jnp.bfloat16)
    queries = head_norm(
        rotate(projected[0].astype(jnp.float32), position_shard, local_heads), scale_local, local_heads
    ).astype(jnp.bfloat16)
    keys_new = head_norm(
        rotate(projected[1].astype(jnp.float32), position_shard, local_heads), scale_local, local_heads
    ).astype(jnp.bfloat16)
    value_rows = projected[2]
    gathered = lax.all_gather(queries, "pages", axis=0, tiled=True)
    scores = (
        jnp.einsum(
            "qhd,khd->hqk",
            queries.reshape(slot_count, local_heads, head_dim),
            keys_new.reshape(slot_count, local_heads, head_dim),
            preferred_element_type=jnp.float32,
        )
        * score_scale
    )
    allowed = (
        (request_shard[:, None] == request_shard[None, :])
        & (offset_shard[None, :] <= offset_shard[:, None])
        & live_shard[:, None]
        & live_shard[None, :]
    )
    weights = jnp.where(allowed[None], jnp.exp(scores), 0.0)
    suffix_total = jnp.sum(weights, axis=-1)
    suffix_sum = jnp.einsum(
        "hqk,khd->qhd",
        weights.astype(jnp.bfloat16),
        value_rows.reshape(slot_count, local_heads, head_dim),
        preferred_element_type=jnp.float32,
    )
    physical = shard_index * pages_here + jnp.arange(pages_here, dtype=jnp.int32)
    matches = page_table[:, None] == physical[None, :]
    logical = jnp.sum(
        jnp.where(matches, jnp.arange(pool_pages, dtype=jnp.int32)[:, None], 0), axis=0
    )
    key_group = jnp.repeat(logical // prefix_pages, page_len)
    cache_local = lax.dynamic_slice_in_dim(cache_keys, mp_index * local_width, local_width, 2)
    prefix_keys = head_norm(
        cache_local.reshape(pages_here * page_len, local_width).astype(jnp.float32),
        scale_local,
        local_heads,
    ).astype(jnp.bfloat16)
    prefix_values = lax.dynamic_slice_in_dim(
        cache_values, mp_index * local_width, local_width, 2
    ).reshape(pages_here * page_len, local_width)
    all_groups = group_id.reshape(-1)
    key_heads = prefix_keys.reshape(-1, local_heads, head_dim)
    value_heads = prefix_values.reshape(-1, local_heads, head_dim)
    total_rows = gathered.shape[0]
    chunk_count = 2 if total_rows % 16 == 0 else 1
    row_count = total_rows // chunk_count
    pieces = []
    for chunk in range(chunk_count):
        query_heads = lax.slice_in_dim(
            gathered, chunk * row_count, (chunk + 1) * row_count, axis=0
        ).reshape(row_count, local_heads, head_dim)
        gathered_group = lax.slice_in_dim(
            all_groups, chunk * row_count, (chunk + 1) * row_count, axis=0
        )
        prefix_scores = (
            jnp.einsum("qhd,khd->qhk", query_heads, key_heads, preferred_element_type=jnp.float32)
            * score_scale
        )
        prefix_allowed = gathered_group[:, None] == key_group[None, :]
        prefix_weights = jnp.where(prefix_allowed[:, None, :], jnp.exp(prefix_scores), 0.0)
        weight_sum = jnp.sum(prefix_weights, axis=-1)
        summed = jnp.einsum(
            "qhk,khd->qhd",
            prefix_weights.astype(jnp.bfloat16),
            value_heads,
            preferred_element_type=jnp.float32,
        )
        pieces.append(
            jnp.concatenate([summed.reshape(row_count, local_width), weight_sum], axis=1).astype(
                jnp.bfloat16
            )
        )
    pages_count = lax.axis_size("pages")
    prefix_parts = lax.all_to_all(
        jnp.concatenate(pieces, axis=0),
        "pages",
        0,
        0,
        tiled=True,
    )
    prefix_both = jnp.sum(
        prefix_parts.reshape(pages_count, slot_count, local_width + local_heads).astype(jnp.float32),
        axis=0,
    )
    prefix_sum = prefix_both[:, :local_width]
    prefix_total = prefix_both[:, local_width:]
    denominator = suffix_total.T + prefix_total + (1.0 - live_shard.astype(jnp.float32))[:, None]
    mixed = (suffix_sum + prefix_sum.reshape(slot_count, local_heads, head_dim)) / denominator[
        :, :, None
    ]
    attention_local = mixed.reshape(slot_count, local_width).astype(jnp.bfloat16)
    attention = lax.all_gather(attention_local, "mp", axis=1, tiled=True)
    projected_out = jnp.dot(attention, w_out, preferred_element_type=jnp.float32)
    residual_in = state_in.astype(jnp.float32)
    state_mid = rms_rows(
        residual_in + eigen_rates[0][None, :] * (rms_rows(projected_out) - residual_in)
    ).astype(jnp.bfloat16)
    state_own = lax.dynamic_slice_in_dim(state_mid, row_first, own_rows, 0)
    gate_up = jnp.einsum("sd,jdf->jsf", state_mid, w_gate_up, preferred_element_type=jnp.float32)
    hidden = (
        jax.nn.silu(scale_gate_up[0][None, :] * gate_up[0])
        * (scale_gate_up[1][None, :] * gate_up[1])
    ).astype(jnp.bfloat16)
    feed_parts = lax.all_to_all(
        jnp.dot(hidden, w_down, preferred_element_type=jnp.float32).astype(jnp.bfloat16),
        "mp",
        0,
        0,
        tiled=True,
    )
    feed_sum = jnp.sum(
        feed_parts.reshape(mp_count, own_rows, model_width).astype(jnp.float32), axis=0
    )
    middle = state_own.astype(jnp.float32)
    result = rms_rows(middle + eigen_rates[1][None, :] * (rms_rows(feed_sum) - middle))
    return (live_own.astype(jnp.float32)[:, None] * result).astype(jnp.bfloat16)


def solution(mesh):
    shards = shards_heads if HEADS % mesh.shape["mp"] == 0 else shards_columns
    return jax.shard_map(
        shards,
        mesh=mesh,
        in_specs=(
            P("pages", None),
            P(None, None, "mp"),
            P(),
            P(None, None, "mp"),
            P("mp", None),
            P(),
            P(None, "mp"),
            P(),
            P("pages", None, None),
            P("pages", None, None),
            P(),
            P(),
            P(),
        ),
        out_specs=P(("pages", "mp"), None),
        check_vma=False,
    )
```

```python
import math

import jax
import jax.numpy as jnp
from jax import lax
from jax.sharding import PartitionSpec as P

HEADS = 20
GROUPS = 8


EPSILON = 1e-06


def rms_rows(values_in):
    return values_in * lax.rsqrt(jnp.mean(values_in * values_in, axis=-1, keepdims=True) + EPSILON)


def head_norm(values_in, scale_vec, head_count):
    row_count, model_width = values_in.shape
    per_head = values_in.reshape(row_count, head_count, model_width // head_count)
    normed = per_head * lax.rsqrt(jnp.mean(per_head * per_head, axis=-1, keepdims=True) + EPSILON)
    return normed.reshape(row_count, model_width) * scale_vec[None, :]


def rotate(values_in, position, head_count):
    row_count, model_width = values_in.shape
    head_dim = model_width // head_count
    half_dim = head_dim // 2
    frequency = jnp.exp(
        jnp.arange(half_dim).astype(jnp.float32) * (-2.0 * math.log(10000.0) / head_dim)
    )
    rotation = position.astype(jnp.float32)[:, None] * frequency[None, :]
    cosine_table = jnp.cos(rotation)[:, None, :]
    sine_table = jnp.sin(rotation)[:, None, :]
    per_head = values_in.reshape(row_count, head_count, head_dim)
    lower_half = per_head[:, :, :half_dim]
    upper_half = per_head[:, :, half_dim:]
    turned = jnp.concatenate(
        [
            lower_half * cosine_table - upper_half * sine_table,
            upper_half * cosine_table + lower_half * sine_table,
        ],
        axis=-1,
    )
    return turned.reshape(row_count, model_width)


def slot_tables(suffix_len, request_group, slot_count):
    end_slots = jnp.cumsum(suffix_len, axis=1)
    start_slots = end_slots - suffix_len
    slot_ids = jnp.arange(slot_count)
    inside = (slot_ids[None, None, :] >= start_slots[:, :, None]) & (
        slot_ids[None, None, :] < end_slots[:, :, None]
    )
    request_ids = jnp.arange(suffix_len.shape[1])
    slot_valid = jnp.any(inside, axis=1)
    request = jnp.sum(jnp.where(inside, request_ids[None, :, None], 0), axis=1)
    offset = slot_ids[None, :] - jnp.sum(jnp.where(inside, start_slots[:, :, None], 0), axis=1)
    group_id = jnp.where(
        slot_valid, jnp.sum(jnp.where(inside, request_group[:, :, None], 0), axis=1), -1
    )
    return (slot_valid, request, offset, group_id)


def prefix_block(query_block, group_block, prefix_keys, prefix_values, key_group, score_scale):
    row_count, model_width = query_block.shape
    head_dim = model_width // HEADS
    query_heads = query_block.reshape(row_count, HEADS, head_dim)
    key_heads = prefix_keys.reshape(-1, HEADS, head_dim)
    value_heads = prefix_values.reshape(-1, HEADS, head_dim)
    scores = (
        jnp.einsum("qhd,khd->qhk", query_heads, key_heads, preferred_element_type=jnp.float32)
        * score_scale
    )
    allowed = group_block[:, None] == key_group[None, :]
    weights = jnp.where(allowed[:, None, :], jnp.exp(scores), 0.0)
    weight_sum = jnp.sum(weights, axis=-1)
    summed = jnp.einsum(
        "qhk,khd->qhd",
        weights.astype(jnp.bfloat16),
        value_heads,
        preferred_element_type=jnp.float32,
    )
    return (summed.reshape(row_count, model_width), weight_sum)


def shards_columns(
    hidden_in,
    w_qkv,
    w_out,
    w_gate_up,
    w_down,
    scale_qk,
    scale_gate_up,
    eigen_rates,
    cache_keys,
    cache_values,
    page_table,
    request_group,
    suffix_len,
):
    slot_count, model_width = hidden_in.shape
    head_dim = model_width // HEADS
    score_scale = 1.0 / math.sqrt(head_dim)
    mp_count = lax.axis_size("mp")
    mp_index = lax.axis_index("mp")
    own_rows = slot_count // mp_count
    row_first = mp_index * own_rows
    shard_index = lax.axis_index("pages")
    pages_here, page_len = (cache_keys.shape[0], cache_keys.shape[1])
    pool_pages = page_table.shape[0]
    prefix_pages = pool_pages // GROUPS
    slot_valid, request, offset, group_id = slot_tables(suffix_len, request_group, slot_count)
    live_shard = lax.dynamic_index_in_dim(slot_valid, shard_index, 0, keepdims=False)
    request_shard = lax.dynamic_index_in_dim(request, shard_index, 0, keepdims=False)
    offset_shard = lax.dynamic_index_in_dim(offset, shard_index, 0, keepdims=False)
    position_shard = prefix_pages * page_len + offset_shard
    live_own = lax.dynamic_slice_in_dim(live_shard, row_first, own_rows, 0)
    request_own = lax.dynamic_slice_in_dim(request_shard, row_first, own_rows, 0)
    offset_own = lax.dynamic_slice_in_dim(offset_shard, row_first, own_rows, 0)
    position_own = lax.dynamic_slice_in_dim(position_shard, row_first, own_rows, 0)
    state_in = rms_rows(hidden_in.astype(jnp.float32)).astype(jnp.bfloat16)
    projected = jnp.einsum(
        "sd,jdc->jsc", state_in, w_qkv, preferred_element_type=jnp.float32
    ).astype(jnp.bfloat16)
    columns = lax.all_gather(projected, "mp", axis=2, tiled=True)
    query_raw = lax.dynamic_slice_in_dim(columns[0], row_first, own_rows, 0)
    key_raw, value_rows = (columns[1], columns[2])
    queries = head_norm(
        rotate(query_raw.astype(jnp.float32), position_own, HEADS), scale_qk, HEADS
    ).astype(jnp.bfloat16)
    keys_new = head_norm(
        rotate(key_raw.astype(jnp.float32), position_shard, HEADS), scale_qk, HEADS
    ).astype(jnp.bfloat16)
    query_heads = queries.reshape(own_rows, HEADS, head_dim)
    scores = (
        jnp.einsum(
            "qhd,khd->hqk",
            query_heads,
            keys_new.reshape(slot_count, HEADS, head_dim),
            preferred_element_type=jnp.float32,
        )
        * score_scale
    )
    allowed = (
        (request_own[:, None] == request_shard[None, :])
        & (offset_shard[None, :] <= offset_own[:, None])
        & live_own[:, None]
        & live_shard[None, :]
    )
    weights = jnp.where(allowed[None], jnp.exp(scores), 0.0)
    suffix_total = jnp.sum(weights, axis=-1)
    suffix_sum = jnp.einsum(
        "hqk,khd->qhd",
        weights.astype(jnp.bfloat16),
        value_rows.reshape(slot_count, HEADS, head_dim),
        preferred_element_type=jnp.float32,
    )
    physical = shard_index * pages_here + jnp.arange(pages_here, dtype=jnp.int32)
    matches = page_table[:, None] == physical[None, :]
    logical = jnp.sum(
        jnp.where(matches, jnp.arange(pool_pages, dtype=jnp.int32)[:, None], 0), axis=0
    )
    key_group = jnp.repeat(logical // prefix_pages, page_len)
    prefix_keys = head_norm(
        cache_keys.reshape(pages_here * page_len, model_width).astype(jnp.float32), scale_qk, HEADS
    ).astype(jnp.bfloat16)
    prefix_values = cache_values.reshape(pages_here * page_len, model_width)
    gathered = lax.all_gather(queries, "pages", axis=0, tiled=True)
    gathered_group = lax.dynamic_slice_in_dim(group_id, row_first, own_rows, 1).reshape(-1)
    row_count = own_rows * lax.axis_size("pages")
    block_rows = row_count if row_count <= 512 else math.gcd(row_count, 512)

    def attend_block(block_first):
        query_block = lax.dynamic_slice_in_dim(gathered, block_first, block_rows, 0)
        group_block = lax.dynamic_slice_in_dim(gathered_group, block_first, block_rows, 0)
        return prefix_block(
            query_block, group_block, prefix_keys, prefix_values, key_group, score_scale
        )

    block_starts = jnp.arange(row_count // block_rows, dtype=jnp.int32) * block_rows
    summed, weight_sum = lax.map(attend_block, block_starts)
    prefix_sum, prefix_total = lax.psum_scatter(
        (summed.reshape(row_count, model_width), weight_sum.reshape(row_count, HEADS)),
        "pages",
        scatter_dimension=0,
        tiled=True,
    )
    denominator = suffix_total.T + prefix_total + (1.0 - live_own.astype(jnp.float32))[:, None]
    mixed = (suffix_sum + prefix_sum.reshape(own_rows, HEADS, head_dim)) / denominator[:, :, None]
    attention = mixed.reshape(own_rows, model_width).astype(jnp.bfloat16)
    projected_out = jnp.dot(
        lax.all_gather(attention, "mp", axis=0, tiled=True),
        w_out,
        preferred_element_type=jnp.float32,
    )
    residual_in = state_in.astype(jnp.float32)
    state_mid = rms_rows(
        residual_in + eigen_rates[0][None, :] * (rms_rows(projected_out) - residual_in)
    ).astype(jnp.bfloat16)
    state_own = lax.dynamic_slice_in_dim(state_mid, row_first, own_rows, 0)
    gate_up = jnp.einsum("sd,jdf->jsf", state_mid, w_gate_up, preferred_element_type=jnp.float32)
    hidden = (
        jax.nn.silu(scale_gate_up[0][None, :] * gate_up[0])
        * (scale_gate_up[1][None, :] * gate_up[1])
    ).astype(jnp.bfloat16)
    feed_sum = lax.psum_scatter(
        jnp.dot(hidden, w_down, preferred_element_type=jnp.float32),
        "mp",
        scatter_dimension=0,
        tiled=True,
    )
    middle = state_own.astype(jnp.float32)
    result = rms_rows(middle + eigen_rates[1][None, :] * (rms_rows(feed_sum) - middle))
    return (live_own.astype(jnp.float32)[:, None] * result).astype(jnp.bfloat16)


def shards_heads(
    hidden_in,
    w_qkv,
    w_out,
    w_gate_up,
    w_down,
    scale_qk,
    scale_gate_up,
    eigen_rates,
    cache_keys,
    cache_values,
    page_table,
    request_group,
    suffix_len,
):
    slot_count, model_width = hidden_in.shape
    head_dim = model_width // HEADS
    score_scale = 1.0 / math.sqrt(head_dim)
    mp_count = lax.axis_size("mp")
    mp_index = lax.axis_index("mp")
    local_heads = HEADS // mp_count
    local_width = local_heads * head_dim
    own_rows = slot_count // mp_count
    row_first = mp_index * own_rows
    shard_index = lax.axis_index("pages")
    pages_here, page_len = (cache_keys.shape[0], cache_keys.shape[1])
    pool_pages = page_table.shape[0]
    prefix_pages = pool_pages // GROUPS
    slot_valid, request, offset, group_id = slot_tables(suffix_len, request_group, slot_count)
    live_shard = lax.dynamic_index_in_dim(slot_valid, shard_index, 0, keepdims=False)
    request_shard = lax.dynamic_index_in_dim(request, shard_index, 0, keepdims=False)
    offset_shard = lax.dynamic_index_in_dim(offset, shard_index, 0, keepdims=False)
    position_shard = prefix_pages * page_len + offset_shard
    live_own = lax.dynamic_slice_in_dim(live_shard, row_first, own_rows, 0)
    scale_local = lax.dynamic_slice_in_dim(scale_qk, mp_index * local_width, local_width, 0)
    state_in = rms_rows(hidden_in.astype(jnp.float32)).astype(jnp.bfloat16)
    projected = jnp.einsum(
        "sd,jdc->jsc", state_in, w_qkv, preferred_element_type=jnp.float32
    ).astype(jnp.bfloat16)
    queries = head_norm(
        rotate(projected[0].astype(jnp.float32), position_shard, local_heads), scale_local, local_heads
    ).astype(jnp.bfloat16)
    keys_new = head_norm(
        rotate(projected[1].astype(jnp.float32), position_shard, local_heads), scale_local, local_heads
    ).astype(jnp.bfloat16)
    value_rows = projected[2]
    gathered = lax.all_gather(queries, "pages", axis=0, tiled=True)
    scores = (
        jnp.einsum(
            "qhd,khd->hqk",
            queries.reshape(slot_count, local_heads, head_dim),
            keys_new.reshape(slot_count, local_heads, head_dim),
            preferred_element_type=jnp.float32,
        )
        * score_scale
    )
    allowed = (
        (request_shard[:, None] == request_shard[None, :])
        & (offset_shard[None, :] <= offset_shard[:, None])
        & live_shard[:, None]
        & live_shard[None, :]
    )
    weights = jnp.where(allowed[None], jnp.exp(scores), 0.0)
    suffix_total = jnp.sum(weights, axis=-1)
    suffix_sum = jnp.einsum(
        "hqk,khd->qhd",
        weights.astype(jnp.bfloat16),
        value_rows.reshape(slot_count, local_heads, head_dim),
        preferred_element_type=jnp.float32,
    )
    physical = shard_index * pages_here + jnp.arange(pages_here, dtype=jnp.int32)
    matches = page_table[:, None] == physical[None, :]
    logical = jnp.sum(
        jnp.where(matches, jnp.arange(pool_pages, dtype=jnp.int32)[:, None], 0), axis=0
    )
    key_group = jnp.repeat(logical // prefix_pages, page_len)
    cache_local = lax.dynamic_slice_in_dim(cache_keys, mp_index * local_width, local_width, 2)
    prefix_keys = head_norm(
        cache_local.reshape(pages_here * page_len, local_width).astype(jnp.float32),
        scale_local,
        local_heads,
    ).astype(jnp.bfloat16)
    prefix_values = lax.dynamic_slice_in_dim(
        cache_values, mp_index * local_width, local_width, 2
    ).reshape(pages_here * page_len, local_width)
    all_groups = group_id.reshape(-1)
    key_heads = prefix_keys.reshape(-1, local_heads, head_dim)
    value_heads = prefix_values.reshape(-1, local_heads, head_dim)
    total_rows = gathered.shape[0]
    chunk_count = 2 if total_rows % 16 == 0 else 1
    row_count = total_rows // chunk_count
    pieces = []
    for chunk in range(chunk_count):
        query_heads = lax.slice_in_dim(
            gathered, chunk * row_count, (chunk + 1) * row_count, axis=0
        ).reshape(row_count, local_heads, head_dim)
        gathered_group = lax.slice_in_dim(
            all_groups, chunk * row_count, (chunk + 1) * row_count, axis=0
        )
        prefix_scores = (
            jnp.einsum("qhd,khd->qhk", query_heads, key_heads, preferred_element_type=jnp.float32)
            * score_scale
        )
        prefix_allowed = gathered_group[:, None] == key_group[None, :]
        prefix_weights = jnp.where(prefix_allowed[:, None, :], jnp.exp(prefix_scores), 0.0)
        weight_sum = jnp.sum(prefix_weights, axis=-1)
        summed = jnp.einsum(
            "qhk,khd->qhd",
            prefix_weights.astype(jnp.bfloat16),
            value_heads,
            preferred_element_type=jnp.float32,
        )
        pieces.append(
            jnp.concatenate([summed.reshape(row_count, local_width), weight_sum], axis=1).astype(
                jnp.bfloat16
            )
        )
    pages_count = lax.axis_size("pages")
    prefix_parts = lax.all_to_all(
        jnp.concatenate(pieces, axis=0),
        "pages",
        0,
        0,
        tiled=True,
    )
    prefix_both = jnp.sum(
        prefix_parts.reshape(pages_count, slot_count, local_width + local_heads).astype(jnp.float32),
        axis=0,
    )
    prefix_sum = prefix_both[:, :local_width]
    prefix_total = prefix_both[:, local_width:]
    denominator = suffix_total.T + prefix_total + (1.0 - live_shard.astype(jnp.float32))[:, None]
    mixed = (suffix_sum + prefix_sum.reshape(slot_count, local_heads, head_dim)) / denominator[
        :, :, None
    ]
    attention_local = mixed.reshape(slot_count, local_width).astype(jnp.bfloat16)
    projected_out = jnp.dot(
        attention_local,
        lax.dynamic_slice_in_dim(w_out, mp_index * local_width, local_width, 0),
        preferred_element_type=jnp.float32,
    )
    for shift in range(1, mp_count):
        arrived = lax.ppermute(
            attention_local,
            "mp",
            [(source, (source + shift) % mp_count) for source in range(mp_count)],
        )
        origin = (mp_index + mp_count - shift) % mp_count
        projected_out = projected_out + jnp.dot(
            arrived,
            lax.dynamic_slice_in_dim(w_out, origin * local_width, local_width, 0),
            preferred_element_type=jnp.float32,
        )
    residual_in = state_in.astype(jnp.float32)
    state_mid = rms_rows(
        residual_in + eigen_rates[0][None, :] * (rms_rows(projected_out) - residual_in)
    ).astype(jnp.bfloat16)
    state_own = lax.dynamic_slice_in_dim(state_mid, row_first, own_rows, 0)
    gate_up = jnp.einsum("sd,jdf->jsf", state_mid, w_gate_up, preferred_element_type=jnp.float32)
    hidden = (
        jax.nn.silu(scale_gate_up[0][None, :] * gate_up[0])
        * (scale_gate_up[1][None, :] * gate_up[1])
    ).astype(jnp.bfloat16)
    feed_parts = lax.all_to_all(
        jnp.dot(hidden, w_down, preferred_element_type=jnp.float32).astype(jnp.bfloat16),
        "mp",
        0,
        0,
        tiled=True,
    )
    feed_sum = jnp.sum(
        feed_parts.reshape(mp_count, own_rows, model_width).astype(jnp.float32), axis=0
    )
    middle = state_own.astype(jnp.float32)
    result = rms_rows(middle + eigen_rates[1][None, :] * (rms_rows(feed_sum) - middle))
    return (live_own.astype(jnp.float32)[:, None] * result).astype(jnp.bfloat16)


def solution(mesh):
    shards = shards_heads if HEADS % mesh.shape["mp"] == 0 else shards_columns
    return jax.shard_map(
        shards,
        mesh=mesh,
        in_specs=(
            P("pages", None),
            P(None, None, "mp"),
            P(),
            P(None, None, "mp"),
            P("mp", None),
            P(),
            P(None, "mp"),
            P(),
            P("pages", None, None),
            P("pages", None, None),
            P(),
            P(),
            P(),
        ),
        out_specs=P(("pages", "mp"), None),
        check_vma=False,
    )
```

```python
import math

import jax
import jax.numpy as jnp
from jax import lax
from jax.sharding import PartitionSpec as P

HEADS = 20
GROUPS = 8


EPSILON = 1e-06


def rms_rows(values_in):
    return values_in * lax.rsqrt(jnp.mean(values_in * values_in, axis=-1, keepdims=True) + EPSILON)


def head_norm(values_in, scale_vec, head_count):
    row_count, model_width = values_in.shape
    per_head = values_in.reshape(row_count, head_count, model_width // head_count)
    normed = per_head * lax.rsqrt(jnp.mean(per_head * per_head, axis=-1, keepdims=True) + EPSILON)
    return normed.reshape(row_count, model_width) * scale_vec[None, :]


def rotate(values_in, position, head_count):
    row_count, model_width = values_in.shape
    head_dim = model_width // head_count
    half_dim = head_dim // 2
    frequency = jnp.exp(
        jnp.arange(half_dim).astype(jnp.float32) * (-2.0 * math.log(10000.0) / head_dim)
    )
    rotation = position.astype(jnp.float32)[:, None] * frequency[None, :]
    cosine_table = jnp.cos(rotation)[:, None, :]
    sine_table = jnp.sin(rotation)[:, None, :]
    per_head = values_in.reshape(row_count, head_count, head_dim)
    lower_half = per_head[:, :, :half_dim]
    upper_half = per_head[:, :, half_dim:]
    turned = jnp.concatenate(
        [
            lower_half * cosine_table - upper_half * sine_table,
            upper_half * cosine_table + lower_half * sine_table,
        ],
        axis=-1,
    )
    return turned.reshape(row_count, model_width)


def slot_tables(suffix_len, request_group, slot_count):
    end_slots = jnp.cumsum(suffix_len, axis=1)
    start_slots = end_slots - suffix_len
    slot_ids = jnp.arange(slot_count)
    inside = (slot_ids[None, None, :] >= start_slots[:, :, None]) & (
        slot_ids[None, None, :] < end_slots[:, :, None]
    )
    request_ids = jnp.arange(suffix_len.shape[1])
    slot_valid = jnp.any(inside, axis=1)
    request = jnp.sum(jnp.where(inside, request_ids[None, :, None], 0), axis=1)
    offset = slot_ids[None, :] - jnp.sum(jnp.where(inside, start_slots[:, :, None], 0), axis=1)
    group_id = jnp.where(
        slot_valid, jnp.sum(jnp.where(inside, request_group[:, :, None], 0), axis=1), -1
    )
    return (slot_valid, request, offset, group_id)


def prefix_block(query_block, group_block, prefix_keys, prefix_values, key_group, score_scale):
    row_count, model_width = query_block.shape
    head_dim = model_width // HEADS
    query_heads = query_block.reshape(row_count, HEADS, head_dim)
    key_heads = prefix_keys.reshape(-1, HEADS, head_dim)
    value_heads = prefix_values.reshape(-1, HEADS, head_dim)
    scores = (
        jnp.einsum("qhd,khd->qhk", query_heads, key_heads, preferred_element_type=jnp.float32)
        * score_scale
    )
    allowed = group_block[:, None] == key_group[None, :]
    weights = jnp.where(allowed[:, None, :], jnp.exp(scores), 0.0)
    weight_sum = jnp.sum(weights, axis=-1)
    summed = jnp.einsum(
        "qhk,khd->qhd",
        weights.astype(jnp.bfloat16),
        value_heads,
        preferred_element_type=jnp.float32,
    )
    return (summed.reshape(row_count, model_width), weight_sum)


def shards_columns(
    hidden_in,
    w_qkv,
    w_out,
    w_gate_up,
    w_down,
    scale_qk,
    scale_gate_up,
    eigen_rates,
    cache_keys,
    cache_values,
    page_table,
    request_group,
    suffix_len,
):
    slot_count, model_width = hidden_in.shape
    head_dim = model_width // HEADS
    score_scale = 1.0 / math.sqrt(head_dim)
    mp_count = lax.axis_size("mp")
    mp_index = lax.axis_index("mp")
    own_rows = slot_count // mp_count
    row_first = mp_index * own_rows
    shard_index = lax.axis_index("pages")
    pages_here, page_len = (cache_keys.shape[0], cache_keys.shape[1])
    pool_pages = page_table.shape[0]
    prefix_pages = pool_pages // GROUPS
    slot_valid, request, offset, group_id = slot_tables(suffix_len, request_group, slot_count)
    live_shard = lax.dynamic_index_in_dim(slot_valid, shard_index, 0, keepdims=False)
    request_shard = lax.dynamic_index_in_dim(request, shard_index, 0, keepdims=False)
    offset_shard = lax.dynamic_index_in_dim(offset, shard_index, 0, keepdims=False)
    position_shard = prefix_pages * page_len + offset_shard
    live_own = lax.dynamic_slice_in_dim(live_shard, row_first, own_rows, 0)
    request_own = lax.dynamic_slice_in_dim(request_shard, row_first, own_rows, 0)
    offset_own = lax.dynamic_slice_in_dim(offset_shard, row_first, own_rows, 0)
    position_own = lax.dynamic_slice_in_dim(position_shard, row_first, own_rows, 0)
    state_in = rms_rows(hidden_in.astype(jnp.float32)).astype(jnp.bfloat16)
    projected = jnp.einsum(
        "sd,jdc->jsc", state_in, w_qkv, preferred_element_type=jnp.float32
    ).astype(jnp.bfloat16)
    columns = lax.all_gather(projected, "mp", axis=2, tiled=True)
    query_raw = lax.dynamic_slice_in_dim(columns[0], row_first, own_rows, 0)
    key_raw, value_rows = (columns[1], columns[2])
    queries = head_norm(
        rotate(query_raw.astype(jnp.float32), position_own, HEADS), scale_qk, HEADS
    ).astype(jnp.bfloat16)
    keys_new = head_norm(
        rotate(key_raw.astype(jnp.float32), position_shard, HEADS), scale_qk, HEADS
    ).astype(jnp.bfloat16)
    query_heads = queries.reshape(own_rows, HEADS, head_dim)
    scores = (
        jnp.einsum(
            "qhd,khd->hqk",
            query_heads,
            keys_new.reshape(slot_count, HEADS, head_dim),
            preferred_element_type=jnp.float32,
        )
        * score_scale
    )
    allowed = (
        (request_own[:, None] == request_shard[None, :])
        & (offset_shard[None, :] <= offset_own[:, None])
        & live_own[:, None]
        & live_shard[None, :]
    )
    weights = jnp.where(allowed[None], jnp.exp(scores), 0.0)
    suffix_total = jnp.sum(weights, axis=-1)
    suffix_sum = jnp.einsum(
        "hqk,khd->qhd",
        weights.astype(jnp.bfloat16),
        value_rows.reshape(slot_count, HEADS, head_dim),
        preferred_element_type=jnp.float32,
    )
    physical = shard_index * pages_here + jnp.arange(pages_here, dtype=jnp.int32)
    matches = page_table[:, None] == physical[None, :]
    logical = jnp.sum(
        jnp.where(matches, jnp.arange(pool_pages, dtype=jnp.int32)[:, None], 0), axis=0
    )
    key_group = jnp.repeat(logical // prefix_pages, page_len)
    prefix_keys = head_norm(
        cache_keys.reshape(pages_here * page_len, model_width).astype(jnp.float32), scale_qk, HEADS
    ).astype(jnp.bfloat16)
    prefix_values = cache_values.reshape(pages_here * page_len, model_width)
    gathered = lax.all_gather(queries, "pages", axis=0, tiled=True)
    gathered_group = lax.dynamic_slice_in_dim(group_id, row_first, own_rows, 1).reshape(-1)
    row_count = own_rows * lax.axis_size("pages")
    block_rows = row_count if row_count <= 512 else math.gcd(row_count, 512)

    def attend_block(block_first):
        query_block = lax.dynamic_slice_in_dim(gathered, block_first, block_rows, 0)
        group_block = lax.dynamic_slice_in_dim(gathered_group, block_first, block_rows, 0)
        return prefix_block(
            query_block, group_block, prefix_keys, prefix_values, key_group, score_scale
        )

    block_starts = jnp.arange(row_count // block_rows, dtype=jnp.int32) * block_rows
    summed, weight_sum = lax.map(attend_block, block_starts)
    prefix_sum, prefix_total = lax.psum_scatter(
        (summed.reshape(row_count, model_width), weight_sum.reshape(row_count, HEADS)),
        "pages",
        scatter_dimension=0,
        tiled=True,
    )
    denominator = suffix_total.T + prefix_total + (1.0 - live_own.astype(jnp.float32))[:, None]
    mixed = (suffix_sum + prefix_sum.reshape(own_rows, HEADS, head_dim)) / denominator[:, :, None]
    attention = mixed.reshape(own_rows, model_width).astype(jnp.bfloat16)
    projected_out = jnp.dot(
        lax.all_gather(attention, "mp", axis=0, tiled=True),
        w_out,
        preferred_element_type=jnp.float32,
    )
    residual_in = state_in.astype(jnp.float32)
    state_mid = rms_rows(
        residual_in + eigen_rates[0][None, :] * (rms_rows(projected_out) - residual_in)
    ).astype(jnp.bfloat16)
    state_own = lax.dynamic_slice_in_dim(state_mid, row_first, own_rows, 0)
    gate_up = jnp.einsum("sd,jdf->jsf", state_mid, w_gate_up, preferred_element_type=jnp.float32)
    hidden = (
        jax.nn.silu(scale_gate_up[0][None, :] * gate_up[0])
        * (scale_gate_up[1][None, :] * gate_up[1])
    ).astype(jnp.bfloat16)
    feed_sum = lax.psum_scatter(
        jnp.dot(hidden, w_down, preferred_element_type=jnp.float32),
        "mp",
        scatter_dimension=0,
        tiled=True,
    )
    middle = state_own.astype(jnp.float32)
    result = rms_rows(middle + eigen_rates[1][None, :] * (rms_rows(feed_sum) - middle))
    return (live_own.astype(jnp.float32)[:, None] * result).astype(jnp.bfloat16)


def shards_heads(
    hidden_in,
    w_qkv,
    w_out,
    w_gate_up,
    w_down,
    scale_qk,
    scale_gate_up,
    eigen_rates,
    cache_keys,
    cache_values,
    page_table,
    request_group,
    suffix_len,
):
    slot_count, model_width = hidden_in.shape
    head_dim = model_width // HEADS
    score_scale = 1.0 / math.sqrt(head_dim)
    mp_count = lax.axis_size("mp")
    mp_index = lax.axis_index("mp")
    local_heads = HEADS // mp_count
    local_width = local_heads * head_dim
    own_rows = slot_count // mp_count
    row_first = mp_index * own_rows
    shard_index = lax.axis_index("pages")
    pages_here, page_len = (cache_keys.shape[0], cache_keys.shape[1])
    pool_pages = page_table.shape[0]
    prefix_pages = pool_pages // GROUPS
    slot_valid, request, offset, group_id = slot_tables(suffix_len, request_group, slot_count)
    live_shard = lax.dynamic_index_in_dim(slot_valid, shard_index, 0, keepdims=False)
    request_shard = lax.dynamic_index_in_dim(request, shard_index, 0, keepdims=False)
    offset_shard = lax.dynamic_index_in_dim(offset, shard_index, 0, keepdims=False)
    position_shard = prefix_pages * page_len + offset_shard
    live_own = lax.dynamic_slice_in_dim(live_shard, row_first, own_rows, 0)
    scale_local = lax.dynamic_slice_in_dim(scale_qk, mp_index * local_width, local_width, 0)
    state_in = rms_rows(hidden_in.astype(jnp.float32)).astype(jnp.bfloat16)
    projected = jnp.einsum(
        "sd,jdc->jsc", state_in, w_qkv, preferred_element_type=jnp.float32
    ).astype(jnp.bfloat16)
    queries = head_norm(
        rotate(projected[0].astype(jnp.float32), position_shard, local_heads), scale_local, local_heads
    ).astype(jnp.bfloat16)
    keys_new = head_norm(
        rotate(projected[1].astype(jnp.float32), position_shard, local_heads), scale_local, local_heads
    ).astype(jnp.bfloat16)
    value_rows = projected[2]
    gathered = lax.all_to_all(
        jnp.tile(queries, (lax.axis_size("pages"), 1)), "pages", 0, 0, tiled=True
    )
    scores = (
        jnp.einsum(
            "qhd,khd->hqk",
            queries.reshape(slot_count, local_heads, head_dim),
            keys_new.reshape(slot_count, local_heads, head_dim),
            preferred_element_type=jnp.float32,
        )
        * score_scale
    )
    allowed = (
        (request_shard[:, None] == request_shard[None, :])
        & (offset_shard[None, :] <= offset_shard[:, None])
        & live_shard[:, None]
        & live_shard[None, :]
    )
    weights = jnp.where(allowed[None], jnp.exp(scores), 0.0)
    suffix_total = jnp.sum(weights, axis=-1)
    suffix_sum = jnp.einsum(
        "hqk,khd->qhd",
        weights.astype(jnp.bfloat16),
        value_rows.reshape(slot_count, local_heads, head_dim),
        preferred_element_type=jnp.float32,
    )
    physical = shard_index * pages_here + jnp.arange(pages_here, dtype=jnp.int32)
    matches = page_table[:, None] == physical[None, :]
    logical = jnp.sum(
        jnp.where(matches, jnp.arange(pool_pages, dtype=jnp.int32)[:, None], 0), axis=0
    )
    key_group = jnp.repeat(logical // prefix_pages, page_len)
    cache_local = lax.dynamic_slice_in_dim(cache_keys, mp_index * local_width, local_width, 2)
    prefix_keys = head_norm(
        cache_local.reshape(pages_here * page_len, local_width).astype(jnp.float32),
        scale_local,
        local_heads,
    ).astype(jnp.bfloat16)
    prefix_values = lax.dynamic_slice_in_dim(
        cache_values, mp_index * local_width, local_width, 2
    ).reshape(pages_here * page_len, local_width)
    all_groups = group_id.reshape(-1)
    key_heads = prefix_keys.reshape(-1, local_heads, head_dim)
    value_heads = prefix_values.reshape(-1, local_heads, head_dim)
    total_rows = gathered.shape[0]
    chunk_count = 2 if total_rows % 16 == 0 else 1
    row_count = total_rows // chunk_count
    pieces = []
    for chunk in range(chunk_count):
        query_heads = lax.slice_in_dim(
            gathered, chunk * row_count, (chunk + 1) * row_count, axis=0
        ).reshape(row_count, local_heads, head_dim)
        gathered_group = lax.slice_in_dim(
            all_groups, chunk * row_count, (chunk + 1) * row_count, axis=0
        )
        prefix_scores = (
            jnp.einsum("qhd,khd->qhk", query_heads, key_heads, preferred_element_type=jnp.float32)
            * score_scale
        )
        prefix_allowed = gathered_group[:, None] == key_group[None, :]
        prefix_weights = jnp.where(prefix_allowed[:, None, :], jnp.exp(prefix_scores), 0.0)
        weight_sum = jnp.sum(prefix_weights, axis=-1)
        summed = jnp.einsum(
            "qhk,khd->qhd",
            prefix_weights.astype(jnp.bfloat16),
            value_heads,
            preferred_element_type=jnp.float32,
        )
        pieces.append(
            jnp.concatenate([summed.reshape(row_count, local_width), weight_sum], axis=1).astype(
                jnp.bfloat16
            )
        )
    pages_count = lax.axis_size("pages")
    prefix_parts = lax.all_to_all(
        jnp.concatenate(pieces, axis=0),
        "pages",
        0,
        0,
        tiled=True,
    )
    prefix_both = jnp.sum(
        prefix_parts.reshape(pages_count, slot_count, local_width + local_heads).astype(jnp.float32),
        axis=0,
    )
    prefix_sum = prefix_both[:, :local_width]
    prefix_total = prefix_both[:, local_width:]
    denominator = suffix_total.T + prefix_total + (1.0 - live_shard.astype(jnp.float32))[:, None]
    mixed = (suffix_sum + prefix_sum.reshape(slot_count, local_heads, head_dim)) / denominator[
        :, :, None
    ]
    attention_local = mixed.reshape(slot_count, local_width).astype(jnp.bfloat16)
    attention = lax.all_gather(attention_local, "mp", axis=1, tiled=True)
    projected_out = jnp.dot(attention, w_out, preferred_element_type=jnp.float32)
    residual_in = state_in.astype(jnp.float32)
    state_mid = rms_rows(
        residual_in + eigen_rates[0][None, :] * (rms_rows(projected_out) - residual_in)
    ).astype(jnp.bfloat16)
    state_own = lax.dynamic_slice_in_dim(state_mid, row_first, own_rows, 0)
    gate_up = jnp.einsum("sd,jdf->jsf", state_mid, w_gate_up, preferred_element_type=jnp.float32)
    hidden = (
        jax.nn.silu(scale_gate_up[0][None, :] * gate_up[0])
        * (scale_gate_up[1][None, :] * gate_up[1])
    ).astype(jnp.bfloat16)
    feed_parts = lax.all_to_all(
        jnp.dot(hidden, w_down, preferred_element_type=jnp.float32).astype(jnp.bfloat16),
        "mp",
        0,
        0,
        tiled=True,
    )
    feed_sum = jnp.sum(
        feed_parts.reshape(mp_count, own_rows, model_width).astype(jnp.float32), axis=0
    )
    middle = state_own.astype(jnp.float32)
    result = rms_rows(middle + eigen_rates[1][None, :] * (rms_rows(feed_sum) - middle))
    return (live_own.astype(jnp.float32)[:, None] * result).astype(jnp.bfloat16)


def solution(mesh):
    shards = shards_heads if HEADS % mesh.shape["mp"] == 0 else shards_columns
    return jax.shard_map(
        shards,
        mesh=mesh,
        in_specs=(
            P("pages", None),
            P(None, None, "mp"),
            P(),
            P(None, None, "mp"),
            P("mp", None),
            P(),
            P(None, "mp"),
            P(),
            P("pages", None, None),
            P("pages", None, None),
            P(),
            P(),
            P(),
        ),
        out_specs=P(("pages", "mp"), None),
        check_vma=False,
    )
```

```python
import math

import jax
import jax.numpy as jnp
from jax import lax
from jax.sharding import PartitionSpec as P

HEADS = 20
GROUPS = 8


EPSILON = 1e-06


def rms_rows(values_in):
    return values_in * lax.rsqrt(jnp.mean(values_in * values_in, axis=-1, keepdims=True) + EPSILON)


def head_norm(values_in, scale_vec, head_count):
    row_count, model_width = values_in.shape
    per_head = values_in.reshape(row_count, head_count, model_width // head_count)
    normed = per_head * lax.rsqrt(jnp.mean(per_head * per_head, axis=-1, keepdims=True) + EPSILON)
    return normed.reshape(row_count, model_width) * scale_vec[None, :]


def rotate(values_in, position, head_count):
    row_count, model_width = values_in.shape
    head_dim = model_width // head_count
    half_dim = head_dim // 2
    frequency = jnp.exp(
        jnp.arange(half_dim).astype(jnp.float32) * (-2.0 * math.log(10000.0) / head_dim)
    )
    rotation = position.astype(jnp.float32)[:, None] * frequency[None, :]
    cosine_table = jnp.cos(rotation)[:, None, :]
    sine_table = jnp.sin(rotation)[:, None, :]
    per_head = values_in.reshape(row_count, head_count, head_dim)
    lower_half = per_head[:, :, :half_dim]
    upper_half = per_head[:, :, half_dim:]
    turned = jnp.concatenate(
        [
            lower_half * cosine_table - upper_half * sine_table,
            upper_half * cosine_table + lower_half * sine_table,
        ],
        axis=-1,
    )
    return turned.reshape(row_count, model_width)


def slot_tables(suffix_len, request_group, slot_count):
    end_slots = jnp.cumsum(suffix_len, axis=1)
    start_slots = end_slots - suffix_len
    slot_ids = jnp.arange(slot_count)
    inside = (slot_ids[None, None, :] >= start_slots[:, :, None]) & (
        slot_ids[None, None, :] < end_slots[:, :, None]
    )
    request_ids = jnp.arange(suffix_len.shape[1])
    slot_valid = jnp.any(inside, axis=1)
    request = jnp.sum(jnp.where(inside, request_ids[None, :, None], 0), axis=1)
    offset = slot_ids[None, :] - jnp.sum(jnp.where(inside, start_slots[:, :, None], 0), axis=1)
    group_id = jnp.where(
        slot_valid, jnp.sum(jnp.where(inside, request_group[:, :, None], 0), axis=1), -1
    )
    return (slot_valid, request, offset, group_id)


def prefix_block(query_block, group_block, prefix_keys, prefix_values, key_group, score_scale):
    row_count, model_width = query_block.shape
    head_dim = model_width // HEADS
    query_heads = query_block.reshape(row_count, HEADS, head_dim)
    key_heads = prefix_keys.reshape(-1, HEADS, head_dim)
    value_heads = prefix_values.reshape(-1, HEADS, head_dim)
    scores = (
        jnp.einsum("qhd,khd->qhk", query_heads, key_heads, preferred_element_type=jnp.float32)
        * score_scale
    )
    allowed = group_block[:, None] == key_group[None, :]
    weights = jnp.where(allowed[:, None, :], jnp.exp(scores), 0.0)
    weight_sum = jnp.sum(weights, axis=-1)
    summed = jnp.einsum(
        "qhk,khd->qhd",
        weights.astype(jnp.bfloat16),
        value_heads,
        preferred_element_type=jnp.float32,
    )
    return (summed.reshape(row_count, model_width), weight_sum)


def shards_columns(
    hidden_in,
    w_qkv,
    w_out,
    w_gate_up,
    w_down,
    scale_qk,
    scale_gate_up,
    eigen_rates,
    cache_keys,
    cache_values,
    page_table,
    request_group,
    suffix_len,
):
    slot_count, model_width = hidden_in.shape
    head_dim = model_width // HEADS
    score_scale = 1.0 / math.sqrt(head_dim)
    mp_count = lax.axis_size("mp")
    mp_index = lax.axis_index("mp")
    own_rows = slot_count // mp_count
    row_first = mp_index * own_rows
    shard_index = lax.axis_index("pages")
    pages_here, page_len = (cache_keys.shape[0], cache_keys.shape[1])
    pool_pages = page_table.shape[0]
    prefix_pages = pool_pages // GROUPS
    slot_valid, request, offset, group_id = slot_tables(suffix_len, request_group, slot_count)
    live_shard = lax.dynamic_index_in_dim(slot_valid, shard_index, 0, keepdims=False)
    request_shard = lax.dynamic_index_in_dim(request, shard_index, 0, keepdims=False)
    offset_shard = lax.dynamic_index_in_dim(offset, shard_index, 0, keepdims=False)
    position_shard = prefix_pages * page_len + offset_shard
    live_own = lax.dynamic_slice_in_dim(live_shard, row_first, own_rows, 0)
    request_own = lax.dynamic_slice_in_dim(request_shard, row_first, own_rows, 0)
    offset_own = lax.dynamic_slice_in_dim(offset_shard, row_first, own_rows, 0)
    position_own = lax.dynamic_slice_in_dim(position_shard, row_first, own_rows, 0)
    state_in = rms_rows(hidden_in.astype(jnp.float32)).astype(jnp.bfloat16)
    projected = jnp.einsum(
        "sd,jdc->jsc", state_in, w_qkv, preferred_element_type=jnp.float32
    ).astype(jnp.bfloat16)
    columns = lax.all_gather(projected, "mp", axis=2, tiled=True)
    query_raw = lax.dynamic_slice_in_dim(columns[0], row_first, own_rows, 0)
    key_raw, value_rows = (columns[1], columns[2])
    queries = head_norm(
        rotate(query_raw.astype(jnp.float32), position_own, HEADS), scale_qk, HEADS
    ).astype(jnp.bfloat16)
    keys_new = head_norm(
        rotate(key_raw.astype(jnp.float32), position_shard, HEADS), scale_qk, HEADS
    ).astype(jnp.bfloat16)
    query_heads = queries.reshape(own_rows, HEADS, head_dim)
    scores = (
        jnp.einsum(
            "qhd,khd->hqk",
            query_heads,
            keys_new.reshape(slot_count, HEADS, head_dim),
            preferred_element_type=jnp.float32,
        )
        * score_scale
    )
    allowed = (
        (request_own[:, None] == request_shard[None, :])
        & (offset_shard[None, :] <= offset_own[:, None])
        & live_own[:, None]
        & live_shard[None, :]
    )
    weights = jnp.where(allowed[None], jnp.exp(scores), 0.0)
    suffix_total = jnp.sum(weights, axis=-1)
    suffix_sum = jnp.einsum(
        "hqk,khd->qhd",
        weights.astype(jnp.bfloat16),
        value_rows.reshape(slot_count, HEADS, head_dim),
        preferred_element_type=jnp.float32,
    )
    physical = shard_index * pages_here + jnp.arange(pages_here, dtype=jnp.int32)
    matches = page_table[:, None] == physical[None, :]
    logical = jnp.sum(
        jnp.where(matches, jnp.arange(pool_pages, dtype=jnp.int32)[:, None], 0), axis=0
    )
    key_group = jnp.repeat(logical // prefix_pages, page_len)
    prefix_keys = head_norm(
        cache_keys.reshape(pages_here * page_len, model_width).astype(jnp.float32), scale_qk, HEADS
    ).astype(jnp.bfloat16)
    prefix_values = cache_values.reshape(pages_here * page_len, model_width)
    gathered = lax.all_gather(queries, "pages", axis=0, tiled=True)
    gathered_group = lax.dynamic_slice_in_dim(group_id, row_first, own_rows, 1).reshape(-1)
    row_count = own_rows * lax.axis_size("pages")
    block_rows = row_count if row_count <= 512 else math.gcd(row_count, 512)

    def attend_block(block_first):
        query_block = lax.dynamic_slice_in_dim(gathered, block_first, block_rows, 0)
        group_block = lax.dynamic_slice_in_dim(gathered_group, block_first, block_rows, 0)
        return prefix_block(
            query_block, group_block, prefix_keys, prefix_values, key_group, score_scale
        )

    block_starts = jnp.arange(row_count // block_rows, dtype=jnp.int32) * block_rows
    summed, weight_sum = lax.map(attend_block, block_starts)
    prefix_sum, prefix_total = lax.psum_scatter(
        (summed.reshape(row_count, model_width), weight_sum.reshape(row_count, HEADS)),
        "pages",
        scatter_dimension=0,
        tiled=True,
    )
    denominator = suffix_total.T + prefix_total + (1.0 - live_own.astype(jnp.float32))[:, None]
    mixed = (suffix_sum + prefix_sum.reshape(own_rows, HEADS, head_dim)) / denominator[:, :, None]
    attention = mixed.reshape(own_rows, model_width).astype(jnp.bfloat16)
    projected_out = jnp.dot(
        lax.all_gather(attention, "mp", axis=0, tiled=True),
        w_out,
        preferred_element_type=jnp.float32,
    )
    residual_in = state_in.astype(jnp.float32)
    state_mid = rms_rows(
        residual_in + eigen_rates[0][None, :] * (rms_rows(projected_out) - residual_in)
    ).astype(jnp.bfloat16)
    state_own = lax.dynamic_slice_in_dim(state_mid, row_first, own_rows, 0)
    gate_up = jnp.einsum("sd,jdf->jsf", state_mid, w_gate_up, preferred_element_type=jnp.float32)
    hidden = (
        jax.nn.silu(scale_gate_up[0][None, :] * gate_up[0])
        * (scale_gate_up[1][None, :] * gate_up[1])
    ).astype(jnp.bfloat16)
    feed_sum = lax.psum_scatter(
        jnp.dot(hidden, w_down, preferred_element_type=jnp.float32),
        "mp",
        scatter_dimension=0,
        tiled=True,
    )
    middle = state_own.astype(jnp.float32)
    result = rms_rows(middle + eigen_rates[1][None, :] * (rms_rows(feed_sum) - middle))
    return (live_own.astype(jnp.float32)[:, None] * result).astype(jnp.bfloat16)


def shards_heads(
    hidden_in,
    w_qkv,
    w_out,
    w_gate_up,
    w_down,
    scale_qk,
    scale_gate_up,
    eigen_rates,
    cache_keys,
    cache_values,
    page_table,
    request_group,
    suffix_len,
):
    slot_count, model_width = hidden_in.shape
    head_dim = model_width // HEADS
    score_scale = 1.0 / math.sqrt(head_dim)
    mp_count = lax.axis_size("mp")
    mp_index = lax.axis_index("mp")
    local_heads = HEADS // mp_count
    local_width = local_heads * head_dim
    own_rows = slot_count // mp_count
    row_first = mp_index * own_rows
    shard_index = lax.axis_index("pages")
    pages_here, page_len = (cache_keys.shape[0], cache_keys.shape[1])
    pool_pages = page_table.shape[0]
    prefix_pages = pool_pages // GROUPS
    slot_valid, request, offset, group_id = slot_tables(suffix_len, request_group, slot_count)
    live_shard = lax.dynamic_index_in_dim(slot_valid, shard_index, 0, keepdims=False)
    request_shard = lax.dynamic_index_in_dim(request, shard_index, 0, keepdims=False)
    offset_shard = lax.dynamic_index_in_dim(offset, shard_index, 0, keepdims=False)
    position_shard = prefix_pages * page_len + offset_shard
    live_own = lax.dynamic_slice_in_dim(live_shard, row_first, own_rows, 0)
    scale_local = lax.dynamic_slice_in_dim(scale_qk, mp_index * local_width, local_width, 0)
    state_in = rms_rows(hidden_in.astype(jnp.float32)).astype(jnp.bfloat16)
    projected = jnp.einsum(
        "sd,jdc->jsc", state_in, w_qkv, preferred_element_type=jnp.float32
    ).astype(jnp.bfloat16)
    queries = head_norm(
        rotate(projected[0].astype(jnp.float32), position_shard, local_heads), scale_local, local_heads
    ).astype(jnp.bfloat16)
    keys_new = head_norm(
        rotate(projected[1].astype(jnp.float32), position_shard, local_heads), scale_local, local_heads
    ).astype(jnp.bfloat16)
    value_rows = projected[2]
    pages_count = lax.axis_size("pages")
    queries_t = jnp.transpose(queries.reshape(slot_count, local_heads, head_dim), (1, 2, 0))
    gathered_t = lax.all_to_all(
        jnp.tile(queries_t[None], (pages_count, 1, 1, 1)), "pages", 0, 3, tiled=True
    ).reshape(local_heads, head_dim, pages_count * slot_count)
    scores = (
        jnp.einsum(
            "qhd,khd->hqk",
            queries.reshape(slot_count, local_heads, head_dim),
            keys_new.reshape(slot_count, local_heads, head_dim),
            preferred_element_type=jnp.float32,
        )
        * score_scale
    )
    allowed = (
        (request_shard[:, None] == request_shard[None, :])
        & (offset_shard[None, :] <= offset_shard[:, None])
        & live_shard[:, None]
        & live_shard[None, :]
    )
    weights = jnp.where(allowed[None], jnp.exp(scores), 0.0)
    suffix_total = jnp.sum(weights, axis=-1)
    suffix_sum = jnp.einsum(
        "hqk,khd->qhd",
        weights.astype(jnp.bfloat16),
        value_rows.reshape(slot_count, local_heads, head_dim),
        preferred_element_type=jnp.float32,
    )
    physical = shard_index * pages_here + jnp.arange(pages_here, dtype=jnp.int32)
    matches = page_table[:, None] == physical[None, :]
    logical = jnp.sum(
        jnp.where(matches, jnp.arange(pool_pages, dtype=jnp.int32)[:, None], 0), axis=0
    )
    key_group = jnp.repeat(logical // prefix_pages, page_len)
    cache_local = lax.dynamic_slice_in_dim(cache_keys, mp_index * local_width, local_width, 2)
    prefix_keys = head_norm(
        cache_local.reshape(pages_here * page_len, local_width).astype(jnp.float32),
        scale_local,
        local_heads,
    ).astype(jnp.bfloat16)
    prefix_values = lax.dynamic_slice_in_dim(
        cache_values, mp_index * local_width, local_width, 2
    ).reshape(pages_here * page_len, local_width)
    all_groups = group_id.reshape(-1)
    key_heads = prefix_keys.reshape(-1, local_heads, head_dim)
    value_heads = prefix_values.reshape(-1, local_heads, head_dim)
    total_rows = gathered_t.shape[2]
    chunk_count = 2 if total_rows % 256 == 0 else 1
    row_count = total_rows // chunk_count
    pieces = []
    for chunk in range(chunk_count):
        query_chunk = lax.slice_in_dim(
            gathered_t, chunk * row_count, (chunk + 1) * row_count, axis=2
        )
        gathered_group = lax.slice_in_dim(
            all_groups, chunk * row_count, (chunk + 1) * row_count, axis=0
        )
        prefix_scores = (
            jnp.einsum("hdq,khd->hkq", query_chunk, key_heads, preferred_element_type=jnp.float32)
            * score_scale
        )
        prefix_allowed = key_group[:, None] == gathered_group[None, :]
        prefix_weights = jnp.where(prefix_allowed[None], jnp.exp(prefix_scores), 0.0)
        weight_sum = jnp.sum(prefix_weights, axis=1)
        summed = jnp.einsum(
            "hkq,khd->hdq",
            prefix_weights.astype(jnp.bfloat16),
            value_heads,
            preferred_element_type=jnp.float32,
        )
        pieces.append(
            jnp.concatenate([summed, weight_sum[:, None, :]], axis=1).astype(jnp.bfloat16)
        )
    prefix_parts = lax.all_to_all(
        jnp.concatenate(pieces, axis=2), "pages", 2, 0, tiled=True
    )
    prefix_both = jnp.sum(
        prefix_parts.reshape(pages_count, local_heads, head_dim + 1, slot_count).astype(
            jnp.float32
        ),
        axis=0,
    )
    prefix_sum = jnp.transpose(prefix_both[:, :head_dim, :], (2, 0, 1))
    prefix_total = prefix_both[:, head_dim, :].T
    denominator = suffix_total.T + prefix_total + (1.0 - live_shard.astype(jnp.float32))[:, None]
    mixed = (suffix_sum + prefix_sum) / denominator[
        :, :, None
    ]
    attention_local = mixed.reshape(slot_count, local_width).astype(jnp.bfloat16)
    attention = lax.all_gather(attention_local, "mp", axis=1, tiled=True)
    projected_out = jnp.dot(attention, w_out, preferred_element_type=jnp.float32)
    residual_in = state_in.astype(jnp.float32)
    state_mid = rms_rows(
        residual_in + eigen_rates[0][None, :] * (rms_rows(projected_out) - residual_in)
    ).astype(jnp.bfloat16)
    state_own = lax.dynamic_slice_in_dim(state_mid, row_first, own_rows, 0)
    gate_up = jnp.einsum("sd,jdf->jsf", state_mid, w_gate_up, preferred_element_type=jnp.float32)
    hidden = (
        jax.nn.silu(scale_gate_up[0][None, :] * gate_up[0])
        * (scale_gate_up[1][None, :] * gate_up[1])
    ).astype(jnp.bfloat16)
    feed_parts = lax.all_to_all(
        jnp.dot(hidden, w_down, preferred_element_type=jnp.float32).astype(jnp.bfloat16),
        "mp",
        0,
        0,
        tiled=True,
    )
    feed_sum = jnp.sum(
        feed_parts.reshape(mp_count, own_rows, model_width).astype(jnp.float32), axis=0
    )
    middle = state_own.astype(jnp.float32)
    result = rms_rows(middle + eigen_rates[1][None, :] * (rms_rows(feed_sum) - middle))
    return (live_own.astype(jnp.float32)[:, None] * result).astype(jnp.bfloat16)


def solution(mesh):
    shards = shards_heads if HEADS % mesh.shape["mp"] == 0 else shards_columns
    return jax.shard_map(
        shards,
        mesh=mesh,
        in_specs=(
            P("pages", None),
            P(None, None, "mp"),
            P(),
            P(None, None, "mp"),
            P("mp", None),
            P(),
            P(None, "mp"),
            P(),
            P("pages", None, None),
            P("pages", None, None),
            P(),
            P(),
            P(),
        ),
        out_specs=P(("pages", "mp"), None),
        check_vma=False,
    )
```

```python
import math

import jax
import jax.numpy as jnp
from jax import lax
from jax.sharding import PartitionSpec as P

HEADS = 20
GROUPS = 8


EPSILON = 1e-06


def rms_rows(values_in):
    return values_in * lax.rsqrt(jnp.mean(values_in * values_in, axis=-1, keepdims=True) + EPSILON)


def head_norm(values_in, scale_vec, head_count):
    row_count, model_width = values_in.shape
    per_head = values_in.reshape(row_count, head_count, model_width // head_count)
    normed = per_head * lax.rsqrt(jnp.mean(per_head * per_head, axis=-1, keepdims=True) + EPSILON)
    return normed.reshape(row_count, model_width) * scale_vec[None, :]


def rotate(values_in, position, head_count):
    row_count, model_width = values_in.shape
    head_dim = model_width // head_count
    half_dim = head_dim // 2
    frequency = jnp.exp(
        jnp.arange(half_dim).astype(jnp.float32) * (-2.0 * math.log(10000.0) / head_dim)
    )
    rotation = position.astype(jnp.float32)[:, None] * frequency[None, :]
    cosine_table = jnp.cos(rotation)[:, None, :]
    sine_table = jnp.sin(rotation)[:, None, :]
    per_head = values_in.reshape(row_count, head_count, head_dim)
    lower_half = per_head[:, :, :half_dim]
    upper_half = per_head[:, :, half_dim:]
    turned = jnp.concatenate(
        [
            lower_half * cosine_table - upper_half * sine_table,
            upper_half * cosine_table + lower_half * sine_table,
        ],
        axis=-1,
    )
    return turned.reshape(row_count, model_width)


def slot_tables(suffix_len, request_group, slot_count):
    end_slots = jnp.cumsum(suffix_len, axis=1)
    start_slots = end_slots - suffix_len
    slot_ids = jnp.arange(slot_count)
    inside = (slot_ids[None, None, :] >= start_slots[:, :, None]) & (
        slot_ids[None, None, :] < end_slots[:, :, None]
    )
    request_ids = jnp.arange(suffix_len.shape[1])
    slot_valid = jnp.any(inside, axis=1)
    request = jnp.sum(jnp.where(inside, request_ids[None, :, None], 0), axis=1)
    offset = slot_ids[None, :] - jnp.sum(jnp.where(inside, start_slots[:, :, None], 0), axis=1)
    group_id = jnp.where(
        slot_valid, jnp.sum(jnp.where(inside, request_group[:, :, None], 0), axis=1), -1
    )
    return (slot_valid, request, offset, group_id)


def prefix_block(query_block, group_block, prefix_keys, prefix_values, key_group, score_scale):
    row_count, model_width = query_block.shape
    head_dim = model_width // HEADS
    query_heads = query_block.reshape(row_count, HEADS, head_dim)
    key_heads = prefix_keys.reshape(-1, HEADS, head_dim)
    value_heads = prefix_values.reshape(-1, HEADS, head_dim)
    scores = (
        jnp.einsum("qhd,khd->qhk", query_heads, key_heads, preferred_element_type=jnp.float32)
        * score_scale
    )
    allowed = group_block[:, None] == key_group[None, :]
    weights = jnp.where(allowed[:, None, :], jnp.exp(scores), 0.0)
    weight_sum = jnp.sum(weights, axis=-1)
    summed = jnp.einsum(
        "qhk,khd->qhd",
        weights.astype(jnp.bfloat16),
        value_heads,
        preferred_element_type=jnp.float32,
    )
    return (summed.reshape(row_count, model_width), weight_sum)


def shards_columns(
    hidden_in,
    w_qkv,
    w_out,
    w_gate_up,
    w_down,
    scale_qk,
    scale_gate_up,
    eigen_rates,
    cache_keys,
    cache_values,
    page_table,
    request_group,
    suffix_len,
):
    slot_count, model_width = hidden_in.shape
    head_dim = model_width // HEADS
    score_scale = 1.0 / math.sqrt(head_dim)
    mp_count = lax.axis_size("mp")
    mp_index = lax.axis_index("mp")
    own_rows = slot_count // mp_count
    row_first = mp_index * own_rows
    shard_index = lax.axis_index("pages")
    pages_here, page_len = (cache_keys.shape[0], cache_keys.shape[1])
    pool_pages = page_table.shape[0]
    prefix_pages = pool_pages // GROUPS
    slot_valid, request, offset, group_id = slot_tables(suffix_len, request_group, slot_count)
    live_shard = lax.dynamic_index_in_dim(slot_valid, shard_index, 0, keepdims=False)
    request_shard = lax.dynamic_index_in_dim(request, shard_index, 0, keepdims=False)
    offset_shard = lax.dynamic_index_in_dim(offset, shard_index, 0, keepdims=False)
    position_shard = prefix_pages * page_len + offset_shard
    live_own = lax.dynamic_slice_in_dim(live_shard, row_first, own_rows, 0)
    request_own = lax.dynamic_slice_in_dim(request_shard, row_first, own_rows, 0)
    offset_own = lax.dynamic_slice_in_dim(offset_shard, row_first, own_rows, 0)
    position_own = lax.dynamic_slice_in_dim(position_shard, row_first, own_rows, 0)
    state_in = rms_rows(hidden_in.astype(jnp.float32)).astype(jnp.bfloat16)
    projected = jnp.einsum(
        "sd,jdc->jsc", state_in, w_qkv, preferred_element_type=jnp.float32
    ).astype(jnp.bfloat16)
    columns = lax.all_gather(projected, "mp", axis=2, tiled=True)
    query_raw = lax.dynamic_slice_in_dim(columns[0], row_first, own_rows, 0)
    key_raw, value_rows = (columns[1], columns[2])
    queries = head_norm(
        rotate(query_raw.astype(jnp.float32), position_own, HEADS), scale_qk, HEADS
    ).astype(jnp.bfloat16)
    keys_new = head_norm(
        rotate(key_raw.astype(jnp.float32), position_shard, HEADS), scale_qk, HEADS
    ).astype(jnp.bfloat16)
    query_heads = queries.reshape(own_rows, HEADS, head_dim)
    scores = (
        jnp.einsum(
            "qhd,khd->hqk",
            query_heads,
            keys_new.reshape(slot_count, HEADS, head_dim),
            preferred_element_type=jnp.float32,
        )
        * score_scale
    )
    allowed = (
        (request_own[:, None] == request_shard[None, :])
        & (offset_shard[None, :] <= offset_own[:, None])
        & live_own[:, None]
        & live_shard[None, :]
    )
    weights = jnp.where(allowed[None], jnp.exp(scores), 0.0)
    suffix_total = jnp.sum(weights, axis=-1)
    suffix_sum = jnp.einsum(
        "hqk,khd->qhd",
        weights.astype(jnp.bfloat16),
        value_rows.reshape(slot_count, HEADS, head_dim),
        preferred_element_type=jnp.float32,
    )
    physical = shard_index * pages_here + jnp.arange(pages_here, dtype=jnp.int32)
    matches = page_table[:, None] == physical[None, :]
    logical = jnp.sum(
        jnp.where(matches, jnp.arange(pool_pages, dtype=jnp.int32)[:, None], 0), axis=0
    )
    key_group = jnp.repeat(logical // prefix_pages, page_len)
    prefix_keys = head_norm(
        cache_keys.reshape(pages_here * page_len, model_width).astype(jnp.float32), scale_qk, HEADS
    ).astype(jnp.bfloat16)
    prefix_values = cache_values.reshape(pages_here * page_len, model_width)
    gathered = lax.all_gather(queries, "pages", axis=0, tiled=True)
    gathered_group = lax.dynamic_slice_in_dim(group_id, row_first, own_rows, 1).reshape(-1)
    row_count = own_rows * lax.axis_size("pages")
    block_rows = row_count if row_count <= 512 else math.gcd(row_count, 512)

    def attend_block(block_first):
        query_block = lax.dynamic_slice_in_dim(gathered, block_first, block_rows, 0)
        group_block = lax.dynamic_slice_in_dim(gathered_group, block_first, block_rows, 0)
        return prefix_block(
            query_block, group_block, prefix_keys, prefix_values, key_group, score_scale
        )

    block_starts = jnp.arange(row_count // block_rows, dtype=jnp.int32) * block_rows
    summed, weight_sum = lax.map(attend_block, block_starts)
    prefix_sum, prefix_total = lax.psum_scatter(
        (summed.reshape(row_count, model_width), weight_sum.reshape(row_count, HEADS)),
        "pages",
        scatter_dimension=0,
        tiled=True,
    )
    denominator = suffix_total.T + prefix_total + (1.0 - live_own.astype(jnp.float32))[:, None]
    mixed = (suffix_sum + prefix_sum.reshape(own_rows, HEADS, head_dim)) / denominator[:, :, None]
    attention = mixed.reshape(own_rows, model_width).astype(jnp.bfloat16)
    projected_out = jnp.dot(
        lax.all_gather(attention, "mp", axis=0, tiled=True),
        w_out,
        preferred_element_type=jnp.float32,
    )
    residual_in = state_in.astype(jnp.float32)
    state_mid = rms_rows(
        residual_in + eigen_rates[0][None, :] * (rms_rows(projected_out) - residual_in)
    ).astype(jnp.bfloat16)
    state_own = lax.dynamic_slice_in_dim(state_mid, row_first, own_rows, 0)
    gate_up = jnp.einsum("sd,jdf->jsf", state_mid, w_gate_up, preferred_element_type=jnp.float32)
    hidden = (
        jax.nn.silu(scale_gate_up[0][None, :] * gate_up[0])
        * (scale_gate_up[1][None, :] * gate_up[1])
    ).astype(jnp.bfloat16)
    feed_sum = lax.psum_scatter(
        jnp.dot(hidden, w_down, preferred_element_type=jnp.float32),
        "mp",
        scatter_dimension=0,
        tiled=True,
    )
    middle = state_own.astype(jnp.float32)
    result = rms_rows(middle + eigen_rates[1][None, :] * (rms_rows(feed_sum) - middle))
    return (live_own.astype(jnp.float32)[:, None] * result).astype(jnp.bfloat16)


def shards_heads(
    hidden_in,
    w_qkv,
    w_out,
    w_gate_up,
    w_down,
    scale_qk,
    scale_gate_up,
    eigen_rates,
    cache_keys,
    cache_values,
    page_table,
    request_group,
    suffix_len,
):
    slot_count, model_width = hidden_in.shape
    head_dim = model_width // HEADS
    score_scale = 1.0 / math.sqrt(head_dim)
    mp_count = lax.axis_size("mp")
    mp_index = lax.axis_index("mp")
    local_heads = HEADS // mp_count
    local_width = local_heads * head_dim
    own_rows = slot_count // mp_count
    row_first = mp_index * own_rows
    shard_index = lax.axis_index("pages")
    pages_here, page_len = (cache_keys.shape[0], cache_keys.shape[1])
    pool_pages = page_table.shape[0]
    prefix_pages = pool_pages // GROUPS
    slot_valid, request, offset, group_id = slot_tables(suffix_len, request_group, slot_count)
    live_shard = lax.dynamic_index_in_dim(slot_valid, shard_index, 0, keepdims=False)
    request_shard = lax.dynamic_index_in_dim(request, shard_index, 0, keepdims=False)
    offset_shard = lax.dynamic_index_in_dim(offset, shard_index, 0, keepdims=False)
    position_shard = prefix_pages * page_len + offset_shard
    live_own = lax.dynamic_slice_in_dim(live_shard, row_first, own_rows, 0)
    scale_local = lax.dynamic_slice_in_dim(scale_qk, mp_index * local_width, local_width, 0)
    state_in = rms_rows(hidden_in.astype(jnp.float32)).astype(jnp.bfloat16)
    projected = jnp.einsum(
        "sd,jdc->jsc", state_in, w_qkv, preferred_element_type=jnp.float32
    ).astype(jnp.bfloat16)
    queries = head_norm(
        rotate(projected[0].astype(jnp.float32), position_shard, local_heads), scale_local, local_heads
    ).astype(jnp.bfloat16)
    keys_new = head_norm(
        rotate(projected[1].astype(jnp.float32), position_shard, local_heads), scale_local, local_heads
    ).astype(jnp.bfloat16)
    value_rows = projected[2]
    gathered = lax.all_to_all(
        jnp.tile(queries, (lax.axis_size("pages"), 1)), "pages", 0, 0, tiled=True
    )
    scores = (
        jnp.einsum(
            "qhd,khd->hqk",
            queries.reshape(slot_count, local_heads, head_dim),
            keys_new.reshape(slot_count, local_heads, head_dim),
            preferred_element_type=jnp.float32,
        )
        * score_scale
    )
    allowed = (
        (request_shard[:, None] == request_shard[None, :])
        & (offset_shard[None, :] <= offset_shard[:, None])
        & live_shard[:, None]
        & live_shard[None, :]
    )
    weights = jnp.where(allowed[None], jnp.exp(scores), 0.0)
    suffix_total = jnp.sum(weights, axis=-1)
    suffix_sum = jnp.einsum(
        "hqk,khd->qhd",
        weights.astype(jnp.bfloat16),
        value_rows.reshape(slot_count, local_heads, head_dim),
        preferred_element_type=jnp.float32,
    )
    physical = shard_index * pages_here + jnp.arange(pages_here, dtype=jnp.int32)
    matches = page_table[:, None] == physical[None, :]
    logical = jnp.sum(
        jnp.where(matches, jnp.arange(pool_pages, dtype=jnp.int32)[:, None], 0), axis=0
    )
    key_group = jnp.repeat(logical // prefix_pages, page_len)
    cache_local = lax.dynamic_slice_in_dim(cache_keys, mp_index * local_width, local_width, 2)
    prefix_keys = head_norm(
        cache_local.reshape(pages_here * page_len, local_width).astype(jnp.float32),
        scale_local,
        local_heads,
    ).astype(jnp.bfloat16)
    prefix_values = lax.dynamic_slice_in_dim(
        cache_values, mp_index * local_width, local_width, 2
    ).reshape(pages_here * page_len, local_width)
    pages_count = lax.axis_size("pages")
    key_heads = prefix_keys.reshape(-1, local_heads, head_dim)
    value_heads = prefix_values.reshape(-1, local_heads, head_dim)
    gathered_heads = gathered.reshape(pages_count, slot_count, local_heads, head_dim)
    chunk_count = 2 if pages_count % 2 == 0 else 1
    chunk_pages = pages_count // chunk_count
    pieces = []
    for chunk in range(chunk_count):
        query_chunk = lax.slice_in_dim(
            gathered_heads, chunk * chunk_pages, (chunk + 1) * chunk_pages, axis=0
        )
        group_chunk = lax.slice_in_dim(
            group_id, chunk * chunk_pages, (chunk + 1) * chunk_pages, axis=0
        )
        prefix_scores = (
            jnp.einsum(
                "pshd,khd->phks", query_chunk, key_heads, preferred_element_type=jnp.float32
            )
            * score_scale
        )
        prefix_allowed = key_group[None, :, None] == group_chunk[:, None, :]
        prefix_weights = jnp.where(prefix_allowed[:, None], jnp.exp(prefix_scores), 0.0)
        weight_sum = jnp.sum(prefix_weights, axis=2)
        summed = jnp.einsum(
            "phks,khd->pshd",
            prefix_weights.astype(jnp.bfloat16),
            value_heads,
            preferred_element_type=jnp.float32,
        )
        pieces.append(
            jnp.concatenate(
                [
                    summed.reshape(chunk_pages, slot_count, local_width),
                    jnp.transpose(weight_sum, (0, 2, 1)),
                ],
                axis=2,
            ).astype(jnp.bfloat16)
        )
    prefix_parts = lax.all_to_all(
        jnp.concatenate(pieces, axis=0).reshape(pages_count * slot_count, local_width + local_heads),
        "pages",
        0,
        0,
        tiled=True,
    )
    prefix_both = jnp.sum(
        prefix_parts.reshape(pages_count, slot_count, local_width + local_heads).astype(jnp.float32),
        axis=0,
    )
    prefix_sum = prefix_both[:, :local_width]
    prefix_total = prefix_both[:, local_width:]
    denominator = suffix_total.T + prefix_total + (1.0 - live_shard.astype(jnp.float32))[:, None]
    mixed = (suffix_sum + prefix_sum.reshape(slot_count, local_heads, head_dim)) / denominator[
        :, :, None
    ]
    attention_local = mixed.reshape(slot_count, local_width).astype(jnp.bfloat16)
    attention = lax.all_gather(attention_local, "mp", axis=1, tiled=True)
    projected_out = jnp.dot(attention, w_out, preferred_element_type=jnp.float32)
    residual_in = state_in.astype(jnp.float32)
    state_mid = rms_rows(
        residual_in + eigen_rates[0][None, :] * (rms_rows(projected_out) - residual_in)
    ).astype(jnp.bfloat16)
    state_own = lax.dynamic_slice_in_dim(state_mid, row_first, own_rows, 0)
    gate_up = jnp.einsum("sd,jdf->jsf", state_mid, w_gate_up, preferred_element_type=jnp.float32)
    hidden = (
        jax.nn.silu(scale_gate_up[0][None, :] * gate_up[0])
        * (scale_gate_up[1][None, :] * gate_up[1])
    ).astype(jnp.bfloat16)
    feed_parts = lax.all_to_all(
        jnp.dot(hidden, w_down, preferred_element_type=jnp.float32).astype(jnp.bfloat16),
        "mp",
        0,
        0,
        tiled=True,
    )
    feed_sum = jnp.sum(
        feed_parts.reshape(mp_count, own_rows, model_width).astype(jnp.float32), axis=0
    )
    middle = state_own.astype(jnp.float32)
    result = rms_rows(middle + eigen_rates[1][None, :] * (rms_rows(feed_sum) - middle))
    return (live_own.astype(jnp.float32)[:, None] * result).astype(jnp.bfloat16)


def solution(mesh):
    shards = shards_heads if HEADS % mesh.shape["mp"] == 0 else shards_columns
    return jax.shard_map(
        shards,
        mesh=mesh,
        in_specs=(
            P("pages", None),
            P(None, None, "mp"),
            P(),
            P(None, None, "mp"),
            P("mp", None),
            P(),
            P(None, "mp"),
            P(),
            P("pages", None, None),
            P("pages", None, None),
            P(),
            P(),
            P(),
        ),
        out_specs=P(("pages", "mp"), None),
        check_vma=False,
    )
```

```python
import math

import jax
import jax.numpy as jnp
from jax import lax
from jax.sharding import PartitionSpec as P

HEADS = 20
GROUPS = 8


EPSILON = 1e-06


def rms_rows(values_in):
    return values_in * lax.rsqrt(jnp.mean(values_in * values_in, axis=-1, keepdims=True) + EPSILON)


def head_norm(values_in, scale_vec, head_count):
    row_count, model_width = values_in.shape
    per_head = values_in.reshape(row_count, head_count, model_width // head_count)
    normed = per_head * lax.rsqrt(jnp.mean(per_head * per_head, axis=-1, keepdims=True) + EPSILON)
    return normed.reshape(row_count, model_width) * scale_vec[None, :]


def rotate(values_in, position, head_count):
    row_count, model_width = values_in.shape
    head_dim = model_width // head_count
    half_dim = head_dim // 2
    frequency = jnp.exp(
        jnp.arange(half_dim).astype(jnp.float32) * (-2.0 * math.log(10000.0) / head_dim)
    )
    rotation = position.astype(jnp.float32)[:, None] * frequency[None, :]
    cosine_table = jnp.cos(rotation)[:, None, :]
    sine_table = jnp.sin(rotation)[:, None, :]
    per_head = values_in.reshape(row_count, head_count, head_dim)
    lower_half = per_head[:, :, :half_dim]
    upper_half = per_head[:, :, half_dim:]
    turned = jnp.concatenate(
        [
            lower_half * cosine_table - upper_half * sine_table,
            upper_half * cosine_table + lower_half * sine_table,
        ],
        axis=-1,
    )
    return turned.reshape(row_count, model_width)


def slot_tables(suffix_len, request_group, slot_count):
    running = [suffix_len[:, 0]]
    for column in range(1, suffix_len.shape[1]):
        running.append(running[-1] + suffix_len[:, column])
    end_slots = jnp.stack(running, axis=1)
    start_slots = end_slots - suffix_len
    slot_ids = jnp.arange(slot_count)
    inside = (slot_ids[None, None, :] >= start_slots[:, :, None]) & (
        slot_ids[None, None, :] < end_slots[:, :, None]
    )
    request_ids = jnp.arange(suffix_len.shape[1])
    slot_valid = jnp.any(inside, axis=1)
    request = jnp.sum(jnp.where(inside, request_ids[None, :, None], 0), axis=1)
    offset = slot_ids[None, :] - jnp.sum(jnp.where(inside, start_slots[:, :, None], 0), axis=1)
    group_id = jnp.where(
        slot_valid, jnp.sum(jnp.where(inside, request_group[:, :, None], 0), axis=1), -1
    )
    return (slot_valid, request, offset, group_id)


def prefix_block(query_block, group_block, prefix_keys, prefix_values, key_group, score_scale):
    row_count, model_width = query_block.shape
    head_dim = model_width // HEADS
    query_heads = query_block.reshape(row_count, HEADS, head_dim)
    key_heads = prefix_keys.reshape(-1, HEADS, head_dim)
    value_heads = prefix_values.reshape(-1, HEADS, head_dim)
    scores = (
        jnp.einsum("qhd,khd->qhk", query_heads, key_heads, preferred_element_type=jnp.float32)
        * score_scale
    )
    allowed = group_block[:, None] == key_group[None, :]
    weights = jnp.where(allowed[:, None, :], jnp.exp(scores), 0.0)
    weight_sum = jnp.sum(weights, axis=-1)
    summed = jnp.einsum(
        "qhk,khd->qhd",
        weights.astype(jnp.bfloat16),
        value_heads,
        preferred_element_type=jnp.float32,
    )
    return (summed.reshape(row_count, model_width), weight_sum)


def shards_columns(
    hidden_in,
    w_qkv,
    w_out,
    w_gate_up,
    w_down,
    scale_qk,
    scale_gate_up,
    eigen_rates,
    cache_keys,
    cache_values,
    page_table,
    request_group,
    suffix_len,
):
    slot_count, model_width = hidden_in.shape
    head_dim = model_width // HEADS
    score_scale = 1.0 / math.sqrt(head_dim)
    mp_count = lax.axis_size("mp")
    mp_index = lax.axis_index("mp")
    own_rows = slot_count // mp_count
    row_first = mp_index * own_rows
    shard_index = lax.axis_index("pages")
    pages_here, page_len = (cache_keys.shape[0], cache_keys.shape[1])
    pool_pages = page_table.shape[0]
    prefix_pages = pool_pages // GROUPS
    slot_valid, request, offset, group_id = slot_tables(suffix_len, request_group, slot_count)
    live_shard = lax.dynamic_index_in_dim(slot_valid, shard_index, 0, keepdims=False)
    request_shard = lax.dynamic_index_in_dim(request, shard_index, 0, keepdims=False)
    offset_shard = lax.dynamic_index_in_dim(offset, shard_index, 0, keepdims=False)
    position_shard = prefix_pages * page_len + offset_shard
    live_own = lax.dynamic_slice_in_dim(live_shard, row_first, own_rows, 0)
    request_own = lax.dynamic_slice_in_dim(request_shard, row_first, own_rows, 0)
    offset_own = lax.dynamic_slice_in_dim(offset_shard, row_first, own_rows, 0)
    position_own = lax.dynamic_slice_in_dim(position_shard, row_first, own_rows, 0)
    state_in = rms_rows(hidden_in.astype(jnp.float32)).astype(jnp.bfloat16)
    projected = jnp.einsum(
        "sd,jdc->jsc", state_in, w_qkv, preferred_element_type=jnp.float32
    ).astype(jnp.bfloat16)
    columns = lax.all_gather(projected, "mp", axis=2, tiled=True)
    query_raw = lax.dynamic_slice_in_dim(columns[0], row_first, own_rows, 0)
    key_raw, value_rows = (columns[1], columns[2])
    queries = head_norm(
        rotate(query_raw.astype(jnp.float32), position_own, HEADS), scale_qk, HEADS
    ).astype(jnp.bfloat16)
    keys_new = head_norm(
        rotate(key_raw.astype(jnp.float32), position_shard, HEADS), scale_qk, HEADS
    ).astype(jnp.bfloat16)
    query_heads = queries.reshape(own_rows, HEADS, head_dim)
    scores = (
        jnp.einsum(
            "qhd,khd->hqk",
            query_heads,
            keys_new.reshape(slot_count, HEADS, head_dim),
            preferred_element_type=jnp.float32,
        )
        * score_scale
    )
    allowed = (
        (request_own[:, None] == request_shard[None, :])
        & (offset_shard[None, :] <= offset_own[:, None])
        & live_own[:, None]
        & live_shard[None, :]
    )
    weights = jnp.where(allowed[None], jnp.exp(scores), 0.0)
    suffix_total = jnp.sum(weights, axis=-1)
    suffix_sum = jnp.einsum(
        "hqk,khd->qhd",
        weights.astype(jnp.bfloat16),
        value_rows.reshape(slot_count, HEADS, head_dim),
        preferred_element_type=jnp.float32,
    )
    physical = shard_index * pages_here + jnp.arange(pages_here, dtype=jnp.int32)
    matches = page_table[:, None] == physical[None, :]
    logical = jnp.sum(
        jnp.where(matches, jnp.arange(pool_pages, dtype=jnp.int32)[:, None], 0), axis=0
    )
    key_group = jnp.repeat(logical // prefix_pages, page_len)
    prefix_keys = head_norm(
        cache_keys.reshape(pages_here * page_len, model_width).astype(jnp.float32), scale_qk, HEADS
    ).astype(jnp.bfloat16)
    prefix_values = cache_values.reshape(pages_here * page_len, model_width)
    gathered = lax.all_gather(queries, "pages", axis=0, tiled=True)
    gathered_group = lax.dynamic_slice_in_dim(group_id, row_first, own_rows, 1).reshape(-1)
    row_count = own_rows * lax.axis_size("pages")
    block_rows = row_count if row_count <= 512 else math.gcd(row_count, 512)

    def attend_block(block_first):
        query_block = lax.dynamic_slice_in_dim(gathered, block_first, block_rows, 0)
        group_block = lax.dynamic_slice_in_dim(gathered_group, block_first, block_rows, 0)
        return prefix_block(
            query_block, group_block, prefix_keys, prefix_values, key_group, score_scale
        )

    block_starts = jnp.arange(row_count // block_rows, dtype=jnp.int32) * block_rows
    summed, weight_sum = lax.map(attend_block, block_starts)
    prefix_sum, prefix_total = lax.psum_scatter(
        (summed.reshape(row_count, model_width), weight_sum.reshape(row_count, HEADS)),
        "pages",
        scatter_dimension=0,
        tiled=True,
    )
    denominator = suffix_total.T + prefix_total + (1.0 - live_own.astype(jnp.float32))[:, None]
    mixed = (suffix_sum + prefix_sum.reshape(own_rows, HEADS, head_dim)) / denominator[:, :, None]
    attention = mixed.reshape(own_rows, model_width).astype(jnp.bfloat16)
    projected_out = jnp.dot(
        lax.all_gather(attention, "mp", axis=0, tiled=True),
        w_out,
        preferred_element_type=jnp.float32,
    )
    residual_in = state_in.astype(jnp.float32)
    state_mid = rms_rows(
        residual_in + eigen_rates[0][None, :] * (rms_rows(projected_out) - residual_in)
    ).astype(jnp.bfloat16)
    state_own = lax.dynamic_slice_in_dim(state_mid, row_first, own_rows, 0)
    gate_up = jnp.einsum("sd,jdf->jsf", state_mid, w_gate_up, preferred_element_type=jnp.float32)
    hidden = (
        jax.nn.silu(scale_gate_up[0][None, :] * gate_up[0])
        * (scale_gate_up[1][None, :] * gate_up[1])
    ).astype(jnp.bfloat16)
    feed_sum = lax.psum_scatter(
        jnp.dot(hidden, w_down, preferred_element_type=jnp.float32),
        "mp",
        scatter_dimension=0,
        tiled=True,
    )
    middle = state_own.astype(jnp.float32)
    result = rms_rows(middle + eigen_rates[1][None, :] * (rms_rows(feed_sum) - middle))
    return (live_own.astype(jnp.float32)[:, None] * result).astype(jnp.bfloat16)


def shards_heads(
    hidden_in,
    w_qkv,
    w_out,
    w_gate_up,
    w_down,
    scale_qk,
    scale_gate_up,
    eigen_rates,
    cache_keys,
    cache_values,
    page_table,
    request_group,
    suffix_len,
):
    slot_count, model_width = hidden_in.shape
    head_dim = model_width // HEADS
    score_scale = 1.0 / math.sqrt(head_dim)
    mp_count = lax.axis_size("mp")
    mp_index = lax.axis_index("mp")
    local_heads = HEADS // mp_count
    local_width = local_heads * head_dim
    own_rows = slot_count // mp_count
    row_first = mp_index * own_rows
    shard_index = lax.axis_index("pages")
    pages_here, page_len = (cache_keys.shape[0], cache_keys.shape[1])
    pool_pages = page_table.shape[0]
    prefix_pages = pool_pages // GROUPS
    slot_valid, request, offset, group_id = slot_tables(suffix_len, request_group, slot_count)
    live_shard = lax.dynamic_index_in_dim(slot_valid, shard_index, 0, keepdims=False)
    request_shard = lax.dynamic_index_in_dim(request, shard_index, 0, keepdims=False)
    offset_shard = lax.dynamic_index_in_dim(offset, shard_index, 0, keepdims=False)
    position_shard = prefix_pages * page_len + offset_shard
    live_own = lax.dynamic_slice_in_dim(live_shard, row_first, own_rows, 0)
    scale_local = lax.dynamic_slice_in_dim(scale_qk, mp_index * local_width, local_width, 0)
    state_in = rms_rows(hidden_in.astype(jnp.float32)).astype(jnp.bfloat16)
    projected_query = jnp.dot(state_in, w_qkv[0], preferred_element_type=jnp.float32).astype(
        jnp.bfloat16
    )
    queries = head_norm(
        rotate(projected_query.astype(jnp.float32), position_shard, local_heads),
        scale_local,
        local_heads,
    ).astype(jnp.bfloat16)
    projected = jnp.einsum(
        "sd,jdc->jsc", state_in, w_qkv[1:], preferred_element_type=jnp.float32
    ).astype(jnp.bfloat16)
    keys_new = head_norm(
        rotate(projected[0].astype(jnp.float32), position_shard, local_heads), scale_local, local_heads
    ).astype(jnp.bfloat16)
    value_rows = projected[1]
    gathered = lax.all_to_all(
        jnp.tile(queries, (lax.axis_size("pages"), 1)), "pages", 0, 0, tiled=True
    )
    scores = (
        jnp.einsum(
            "qhd,khd->hqk",
            queries.reshape(slot_count, local_heads, head_dim),
            keys_new.reshape(slot_count, local_heads, head_dim),
            preferred_element_type=jnp.float32,
        )
        * score_scale
    )
    allowed = (
        (request_shard[:, None] == request_shard[None, :])
        & (offset_shard[None, :] <= offset_shard[:, None])
        & live_shard[:, None]
        & live_shard[None, :]
    )
    weights = jnp.where(allowed[None], jnp.exp(scores), 0.0)
    suffix_total = jnp.sum(weights, axis=-1)
    suffix_sum = jnp.einsum(
        "hqk,khd->qhd",
        weights.astype(jnp.bfloat16),
        value_rows.reshape(slot_count, local_heads, head_dim),
        preferred_element_type=jnp.float32,
    )
    physical = shard_index * pages_here + jnp.arange(pages_here, dtype=jnp.int32)
    matches = page_table[:, None] == physical[None, :]
    logical = jnp.sum(
        jnp.where(matches, jnp.arange(pool_pages, dtype=jnp.int32)[:, None], 0), axis=0
    )
    key_group = jnp.repeat(logical // prefix_pages, page_len)
    cache_local = lax.dynamic_slice_in_dim(cache_keys, mp_index * local_width, local_width, 2)
    prefix_keys = head_norm(
        cache_local.reshape(pages_here * page_len, local_width).astype(jnp.float32),
        scale_local,
        local_heads,
    ).astype(jnp.bfloat16)
    prefix_values = lax.dynamic_slice_in_dim(
        cache_values, mp_index * local_width, local_width, 2
    ).reshape(pages_here * page_len, local_width)
    pages_count = lax.axis_size("pages")
    key_heads = prefix_keys.reshape(-1, local_heads, head_dim)
    value_heads = prefix_values.reshape(-1, local_heads, head_dim)
    gathered_heads = gathered.reshape(pages_count, slot_count, local_heads, head_dim)
    chunk_count = 2 if pages_count % 2 == 0 else 1
    chunk_pages = pages_count // chunk_count
    pieces = []
    for chunk in range(chunk_count):
        query_chunk = lax.slice_in_dim(
            gathered_heads, chunk * chunk_pages, (chunk + 1) * chunk_pages, axis=0
        )
        group_chunk = lax.slice_in_dim(
            group_id, chunk * chunk_pages, (chunk + 1) * chunk_pages, axis=0
        )
        prefix_scores = (
            jnp.einsum(
                "pshd,khd->phks", query_chunk, key_heads, preferred_element_type=jnp.float32
            )
            * score_scale
        )
        prefix_allowed = key_group[None, :, None] == group_chunk[:, None, :]
        prefix_weights = jnp.where(prefix_allowed[:, None], jnp.exp(prefix_scores), 0.0)
        weight_sum = jnp.sum(prefix_weights, axis=2)
        summed = jnp.einsum(
            "phks,khd->pshd",
            prefix_weights.astype(jnp.bfloat16),
            value_heads,
            preferred_element_type=jnp.float32,
        )
        pieces.append(
            jnp.concatenate(
                [
                    summed.reshape(chunk_pages, slot_count, local_width),
                    jnp.transpose(weight_sum, (0, 2, 1)),
                ],
                axis=2,
            ).astype(jnp.bfloat16)
        )
    prefix_parts = lax.all_to_all(
        jnp.concatenate(pieces, axis=0).reshape(pages_count * slot_count, local_width + local_heads),
        "pages",
        0,
        0,
        tiled=True,
    )
    prefix_both = jnp.sum(
        prefix_parts.reshape(pages_count, slot_count, local_width + local_heads).astype(jnp.float32),
        axis=0,
    )
    prefix_sum = prefix_both[:, :local_width]
    prefix_total = prefix_both[:, local_width:]
    denominator = suffix_total.T + prefix_total + (1.0 - live_shard.astype(jnp.float32))[:, None]
    mixed = (suffix_sum + prefix_sum.reshape(slot_count, local_heads, head_dim)) / denominator[
        :, :, None
    ]
    attention_local = mixed.reshape(slot_count, local_width).astype(jnp.bfloat16)
    attention = lax.all_gather(attention_local, "mp", axis=1, tiled=True)
    projected_out = jnp.dot(attention, w_out, preferred_element_type=jnp.float32)
    residual_in = state_in.astype(jnp.float32)
    state_mid = rms_rows(
        residual_in + eigen_rates[0][None, :] * (rms_rows(projected_out) - residual_in)
    ).astype(jnp.bfloat16)
    state_own = lax.dynamic_slice_in_dim(state_mid, row_first, own_rows, 0)
    gate_up = jnp.einsum("sd,jdf->jsf", state_mid, w_gate_up, preferred_element_type=jnp.float32)
    hidden = (
        jax.nn.silu(scale_gate_up[0][None, :] * gate_up[0])
        * (scale_gate_up[1][None, :] * gate_up[1])
    ).astype(jnp.bfloat16)
    feed_parts = lax.all_to_all(
        jnp.dot(hidden, w_down, preferred_element_type=jnp.float32).astype(jnp.bfloat16),
        "mp",
        0,
        0,
        tiled=True,
    )
    feed_sum = jnp.sum(
        feed_parts.reshape(mp_count, own_rows, model_width).astype(jnp.float32), axis=0
    )
    middle = state_own.astype(jnp.float32)
    result = rms_rows(middle + eigen_rates[1][None, :] * (rms_rows(feed_sum) - middle))
    return (live_own.astype(jnp.float32)[:, None] * result).astype(jnp.bfloat16)


def solution(mesh):
    shards = shards_heads if HEADS % mesh.shape["mp"] == 0 else shards_columns
    return jax.shard_map(
        shards,
        mesh=mesh,
        in_specs=(
            P("pages", None),
            P(None, None, "mp"),
            P(),
            P(None, None, "mp"),
            P("mp", None),
            P(),
            P(None, "mp"),
            P(),
            P("pages", None, None),
            P("pages", None, None),
            P(),
            P(),
            P(),
        ),
        out_specs=P(("pages", "mp"), None),
        check_vma=False,
    )
```

```python
import math

import jax
import jax.numpy as jnp
from jax import lax
from jax.sharding import PartitionSpec as P

HEADS = 20
GROUPS = 8


EPSILON = 1e-06


def rms_rows(values_in):
    return values_in * lax.rsqrt(jnp.mean(values_in * values_in, axis=-1, keepdims=True) + EPSILON)


def head_norm(values_in, scale_vec, head_count):
    row_count, model_width = values_in.shape
    per_head = values_in.reshape(row_count, head_count, model_width // head_count)
    normed = per_head * lax.rsqrt(jnp.mean(per_head * per_head, axis=-1, keepdims=True) + EPSILON)
    return normed.reshape(row_count, model_width) * scale_vec[None, :]


def rotate(values_in, position, head_count):
    row_count, model_width = values_in.shape
    head_dim = model_width // head_count
    half_dim = head_dim // 2
    frequency = jnp.exp(
        jnp.arange(half_dim).astype(jnp.float32) * (-2.0 * math.log(10000.0) / head_dim)
    )
    rotation = position.astype(jnp.float32)[:, None] * frequency[None, :]
    cosine_table = jnp.cos(rotation)[:, None, :]
    sine_table = jnp.sin(rotation)[:, None, :]
    per_head = values_in.reshape(row_count, head_count, head_dim)
    lower_half = per_head[:, :, :half_dim]
    upper_half = per_head[:, :, half_dim:]
    turned = jnp.concatenate(
        [
            lower_half * cosine_table - upper_half * sine_table,
            upper_half * cosine_table + lower_half * sine_table,
        ],
        axis=-1,
    )
    return turned.reshape(row_count, model_width)


def slot_tables(suffix_len, request_group, slot_count):
    running = [suffix_len[:, 0]]
    for column in range(1, suffix_len.shape[1]):
        running.append(running[-1] + suffix_len[:, column])
    end_slots = jnp.stack(running, axis=1)
    start_slots = end_slots - suffix_len
    slot_ids = jnp.arange(slot_count)
    inside = (slot_ids[None, None, :] >= start_slots[:, :, None]) & (
        slot_ids[None, None, :] < end_slots[:, :, None]
    )
    request_ids = jnp.arange(suffix_len.shape[1])
    slot_valid = jnp.any(inside, axis=1)
    request = jnp.sum(jnp.where(inside, request_ids[None, :, None], 0), axis=1)
    offset = slot_ids[None, :] - jnp.sum(jnp.where(inside, start_slots[:, :, None], 0), axis=1)
    group_id = jnp.where(
        slot_valid, jnp.sum(jnp.where(inside, request_group[:, :, None], 0), axis=1), -1
    )
    return (slot_valid, request, offset, group_id)


def prefix_block(query_block, group_block, prefix_keys, prefix_values, key_group, score_scale):
    row_count, model_width = query_block.shape
    head_dim = model_width // HEADS
    query_heads = query_block.reshape(row_count, HEADS, head_dim)
    key_heads = prefix_keys.reshape(-1, HEADS, head_dim)
    value_heads = prefix_values.reshape(-1, HEADS, head_dim)
    scores = (
        jnp.einsum("qhd,khd->qhk", query_heads, key_heads, preferred_element_type=jnp.float32)
        * score_scale
    )
    allowed = group_block[:, None] == key_group[None, :]
    weights = jnp.where(allowed[:, None, :], jnp.exp(scores), 0.0)
    weight_sum = jnp.sum(weights, axis=-1)
    summed = jnp.einsum(
        "qhk,khd->qhd",
        weights.astype(jnp.bfloat16),
        value_heads,
        preferred_element_type=jnp.float32,
    )
    return (summed.reshape(row_count, model_width), weight_sum)


def shards_columns(
    hidden_in,
    w_qkv,
    w_out,
    w_gate_up,
    w_down,
    scale_qk,
    scale_gate_up,
    eigen_rates,
    cache_keys,
    cache_values,
    page_table,
    request_group,
    suffix_len,
):
    slot_count, model_width = hidden_in.shape
    head_dim = model_width // HEADS
    score_scale = 1.0 / math.sqrt(head_dim)
    mp_count = lax.axis_size("mp")
    mp_index = lax.axis_index("mp")
    own_rows = slot_count // mp_count
    row_first = mp_index * own_rows
    shard_index = lax.axis_index("pages")
    pages_here, page_len = (cache_keys.shape[0], cache_keys.shape[1])
    pool_pages = page_table.shape[0]
    prefix_pages = pool_pages // GROUPS
    slot_valid, request, offset, group_id = slot_tables(suffix_len, request_group, slot_count)
    live_shard = lax.dynamic_index_in_dim(slot_valid, shard_index, 0, keepdims=False)
    request_shard = lax.dynamic_index_in_dim(request, shard_index, 0, keepdims=False)
    offset_shard = lax.dynamic_index_in_dim(offset, shard_index, 0, keepdims=False)
    position_shard = prefix_pages * page_len + offset_shard
    live_own = lax.dynamic_slice_in_dim(live_shard, row_first, own_rows, 0)
    request_own = lax.dynamic_slice_in_dim(request_shard, row_first, own_rows, 0)
    offset_own = lax.dynamic_slice_in_dim(offset_shard, row_first, own_rows, 0)
    position_own = lax.dynamic_slice_in_dim(position_shard, row_first, own_rows, 0)
    state_in = rms_rows(hidden_in.astype(jnp.float32)).astype(jnp.bfloat16)
    projected = jnp.einsum(
        "sd,jdc->jsc", state_in, w_qkv, preferred_element_type=jnp.float32
    ).astype(jnp.bfloat16)
    columns = lax.all_gather(projected, "mp", axis=2, tiled=True)
    query_raw = lax.dynamic_slice_in_dim(columns[0], row_first, own_rows, 0)
    key_raw, value_rows = (columns[1], columns[2])
    queries = head_norm(
        rotate(query_raw.astype(jnp.float32), position_own, HEADS), scale_qk, HEADS
    ).astype(jnp.bfloat16)
    keys_new = head_norm(
        rotate(key_raw.astype(jnp.float32), position_shard, HEADS), scale_qk, HEADS
    ).astype(jnp.bfloat16)
    query_heads = queries.reshape(own_rows, HEADS, head_dim)
    scores = (
        jnp.einsum(
            "qhd,khd->hqk",
            query_heads,
            keys_new.reshape(slot_count, HEADS, head_dim),
            preferred_element_type=jnp.float32,
        )
        * score_scale
    )
    allowed = (
        (request_own[:, None] == request_shard[None, :])
        & (offset_shard[None, :] <= offset_own[:, None])
        & live_own[:, None]
        & live_shard[None, :]
    )
    weights = jnp.where(allowed[None], jnp.exp(scores), 0.0)
    suffix_total = jnp.sum(weights, axis=-1)
    suffix_sum = jnp.einsum(
        "hqk,khd->qhd",
        weights.astype(jnp.bfloat16),
        value_rows.reshape(slot_count, HEADS, head_dim),
        preferred_element_type=jnp.float32,
    )
    physical = shard_index * pages_here + jnp.arange(pages_here, dtype=jnp.int32)
    matches = page_table[:, None] == physical[None, :]
    logical = jnp.sum(
        jnp.where(matches, jnp.arange(pool_pages, dtype=jnp.int32)[:, None], 0), axis=0
    )
    key_group = jnp.repeat(logical // prefix_pages, page_len)
    prefix_keys = head_norm(
        cache_keys.reshape(pages_here * page_len, model_width).astype(jnp.float32), scale_qk, HEADS
    ).astype(jnp.bfloat16)
    prefix_values = cache_values.reshape(pages_here * page_len, model_width)
    gathered = lax.all_gather(queries, "pages", axis=0, tiled=True)
    gathered_group = lax.dynamic_slice_in_dim(group_id, row_first, own_rows, 1).reshape(-1)
    row_count = own_rows * lax.axis_size("pages")
    block_rows = row_count if row_count <= 512 else math.gcd(row_count, 512)

    def attend_block(block_first):
        query_block = lax.dynamic_slice_in_dim(gathered, block_first, block_rows, 0)
        group_block = lax.dynamic_slice_in_dim(gathered_group, block_first, block_rows, 0)
        return prefix_block(
            query_block, group_block, prefix_keys, prefix_values, key_group, score_scale
        )

    block_starts = jnp.arange(row_count // block_rows, dtype=jnp.int32) * block_rows
    summed, weight_sum = lax.map(attend_block, block_starts)
    prefix_sum, prefix_total = lax.psum_scatter(
        (summed.reshape(row_count, model_width), weight_sum.reshape(row_count, HEADS)),
        "pages",
        scatter_dimension=0,
        tiled=True,
    )
    denominator = suffix_total.T + prefix_total + (1.0 - live_own.astype(jnp.float32))[:, None]
    mixed = (suffix_sum + prefix_sum.reshape(own_rows, HEADS, head_dim)) / denominator[:, :, None]
    attention = mixed.reshape(own_rows, model_width).astype(jnp.bfloat16)
    projected_out = jnp.dot(
        lax.all_gather(attention, "mp", axis=0, tiled=True),
        w_out,
        preferred_element_type=jnp.float32,
    )
    residual_in = state_in.astype(jnp.float32)
    state_mid = rms_rows(
        residual_in + eigen_rates[0][None, :] * (rms_rows(projected_out) - residual_in)
    ).astype(jnp.bfloat16)
    state_own = lax.dynamic_slice_in_dim(state_mid, row_first, own_rows, 0)
    gate_up = jnp.einsum("sd,jdf->jsf", state_mid, w_gate_up, preferred_element_type=jnp.float32)
    hidden = (
        jax.nn.silu(scale_gate_up[0][None, :] * gate_up[0])
        * (scale_gate_up[1][None, :] * gate_up[1])
    ).astype(jnp.bfloat16)
    feed_sum = lax.psum_scatter(
        jnp.dot(hidden, w_down, preferred_element_type=jnp.float32),
        "mp",
        scatter_dimension=0,
        tiled=True,
    )
    middle = state_own.astype(jnp.float32)
    result = rms_rows(middle + eigen_rates[1][None, :] * (rms_rows(feed_sum) - middle))
    return (live_own.astype(jnp.float32)[:, None] * result).astype(jnp.bfloat16)


def shards_heads(
    hidden_in,
    w_qkv,
    w_out,
    w_gate_up,
    w_down,
    scale_qk,
    scale_gate_up,
    eigen_rates,
    cache_keys,
    cache_values,
    page_table,
    request_group,
    suffix_len,
):
    slot_count, model_width = hidden_in.shape
    head_dim = model_width // HEADS
    score_scale = 1.0 / math.sqrt(head_dim)
    mp_count = lax.axis_size("mp")
    mp_index = lax.axis_index("mp")
    local_heads = HEADS // mp_count
    local_width = local_heads * head_dim
    own_rows = slot_count // mp_count
    row_first = mp_index * own_rows
    shard_index = lax.axis_index("pages")
    pages_here, page_len = (cache_keys.shape[0], cache_keys.shape[1])
    pool_pages = page_table.shape[0]
    prefix_pages = pool_pages // GROUPS
    slot_valid, request, offset, group_id = slot_tables(suffix_len, request_group, slot_count)
    live_shard = lax.dynamic_index_in_dim(slot_valid, shard_index, 0, keepdims=False)
    request_shard = lax.dynamic_index_in_dim(request, shard_index, 0, keepdims=False)
    offset_shard = lax.dynamic_index_in_dim(offset, shard_index, 0, keepdims=False)
    position_shard = prefix_pages * page_len + offset_shard
    live_own = lax.dynamic_slice_in_dim(live_shard, row_first, own_rows, 0)
    scale_local = lax.dynamic_slice_in_dim(scale_qk, mp_index * local_width, local_width, 0)
    state_in = rms_rows(hidden_in.astype(jnp.float32)).astype(jnp.bfloat16)
    projected_query = jnp.dot(state_in, w_qkv[0], preferred_element_type=jnp.float32).astype(
        jnp.bfloat16
    )
    queries = head_norm(
        rotate(projected_query.astype(jnp.float32), position_shard, local_heads),
        scale_local,
        local_heads,
    ).astype(jnp.bfloat16)
    gathered = lax.all_to_all(
        jnp.tile(queries, (lax.axis_size("pages"), 1)), "pages", 0, 0, tiled=True
    )
    state_kv, gathered = lax.optimization_barrier((state_in, gathered))
    projected = jnp.einsum(
        "sd,jdc->jsc", state_kv, w_qkv[1:], preferred_element_type=jnp.float32
    ).astype(jnp.bfloat16)
    keys_new = head_norm(
        rotate(projected[0].astype(jnp.float32), position_shard, local_heads), scale_local, local_heads
    ).astype(jnp.bfloat16)
    value_rows = projected[1]
    scores = (
        jnp.einsum(
            "qhd,khd->hqk",
            queries.reshape(slot_count, local_heads, head_dim),
            keys_new.reshape(slot_count, local_heads, head_dim),
            preferred_element_type=jnp.float32,
        )
        * score_scale
    )
    allowed = (
        (request_shard[:, None] == request_shard[None, :])
        & (offset_shard[None, :] <= offset_shard[:, None])
        & live_shard[:, None]
        & live_shard[None, :]
    )
    weights = jnp.where(allowed[None], jnp.exp(scores), 0.0)
    suffix_total = jnp.sum(weights, axis=-1)
    suffix_sum = jnp.einsum(
        "hqk,khd->qhd",
        weights.astype(jnp.bfloat16),
        value_rows.reshape(slot_count, local_heads, head_dim),
        preferred_element_type=jnp.float32,
    )
    physical = shard_index * pages_here + jnp.arange(pages_here, dtype=jnp.int32)
    matches = page_table[:, None] == physical[None, :]
    logical = jnp.sum(
        jnp.where(matches, jnp.arange(pool_pages, dtype=jnp.int32)[:, None], 0), axis=0
    )
    key_group = jnp.repeat(logical // prefix_pages, page_len)
    cache_local = lax.dynamic_slice_in_dim(cache_keys, mp_index * local_width, local_width, 2)
    prefix_keys = head_norm(
        cache_local.reshape(pages_here * page_len, local_width).astype(jnp.float32),
        scale_local,
        local_heads,
    ).astype(jnp.bfloat16)
    prefix_values = lax.dynamic_slice_in_dim(
        cache_values, mp_index * local_width, local_width, 2
    ).reshape(pages_here * page_len, local_width)
    pages_count = lax.axis_size("pages")
    key_heads = prefix_keys.reshape(-1, local_heads, head_dim)
    value_heads = prefix_values.reshape(-1, local_heads, head_dim)
    gathered_heads = gathered.reshape(pages_count, slot_count, local_heads, head_dim)
    chunk_count = 2 if pages_count % 2 == 0 else 1
    chunk_pages = pages_count // chunk_count
    pieces = []
    for chunk in range(chunk_count):
        query_chunk = lax.slice_in_dim(
            gathered_heads, chunk * chunk_pages, (chunk + 1) * chunk_pages, axis=0
        )
        group_chunk = lax.slice_in_dim(
            group_id, chunk * chunk_pages, (chunk + 1) * chunk_pages, axis=0
        )
        prefix_scores = (
            jnp.einsum(
                "pshd,khd->phks", query_chunk, key_heads, preferred_element_type=jnp.float32
            )
            * score_scale
        )
        prefix_allowed = key_group[None, :, None] == group_chunk[:, None, :]
        prefix_weights = jnp.where(prefix_allowed[:, None], jnp.exp(prefix_scores), 0.0)
        weight_sum = jnp.sum(prefix_weights, axis=2)
        summed = jnp.einsum(
            "phks,khd->pshd",
            prefix_weights.astype(jnp.bfloat16),
            value_heads,
            preferred_element_type=jnp.float32,
        )
        pieces.append(
            jnp.concatenate(
                [
                    summed.reshape(chunk_pages, slot_count, local_width),
                    jnp.transpose(weight_sum, (0, 2, 1)),
                ],
                axis=2,
            ).astype(jnp.bfloat16)
        )
    prefix_parts = lax.all_to_all(
        jnp.concatenate(pieces, axis=0).reshape(pages_count * slot_count, local_width + local_heads),
        "pages",
        0,
        0,
        tiled=True,
    )
    prefix_both = jnp.sum(
        prefix_parts.reshape(pages_count, slot_count, local_width + local_heads).astype(jnp.float32),
        axis=0,
    )
    prefix_sum = prefix_both[:, :local_width]
    prefix_total = prefix_both[:, local_width:]
    denominator = suffix_total.T + prefix_total + (1.0 - live_shard.astype(jnp.float32))[:, None]
    mixed = (suffix_sum + prefix_sum.reshape(slot_count, local_heads, head_dim)) / denominator[
        :, :, None
    ]
    attention_local = mixed.reshape(slot_count, local_width).astype(jnp.bfloat16)
    attention = lax.all_gather(attention_local, "mp", axis=1, tiled=True)
    projected_out = jnp.dot(attention, w_out, preferred_element_type=jnp.float32)
    residual_in = state_in.astype(jnp.float32)
    state_mid = rms_rows(
        residual_in + eigen_rates[0][None, :] * (rms_rows(projected_out) - residual_in)
    ).astype(jnp.bfloat16)
    state_own = lax.dynamic_slice_in_dim(state_mid, row_first, own_rows, 0)
    gate_up = jnp.einsum("sd,jdf->jsf", state_mid, w_gate_up, preferred_element_type=jnp.float32)
    hidden = (
        jax.nn.silu(scale_gate_up[0][None, :] * gate_up[0])
        * (scale_gate_up[1][None, :] * gate_up[1])
    ).astype(jnp.bfloat16)
    feed_parts = lax.all_to_all(
        jnp.dot(hidden, w_down, preferred_element_type=jnp.float32).astype(jnp.bfloat16),
        "mp",
        0,
        0,
        tiled=True,
    )
    feed_sum = jnp.sum(
        feed_parts.reshape(mp_count, own_rows, model_width).astype(jnp.float32), axis=0
    )
    middle = state_own.astype(jnp.float32)
    result = rms_rows(middle + eigen_rates[1][None, :] * (rms_rows(feed_sum) - middle))
    return (live_own.astype(jnp.float32)[:, None] * result).astype(jnp.bfloat16)


def solution(mesh):
    shards = shards_heads if HEADS % mesh.shape["mp"] == 0 else shards_columns
    return jax.shard_map(
        shards,
        mesh=mesh,
        in_specs=(
            P("pages", None),
            P(None, None, "mp"),
            P(),
            P(None, None, "mp"),
            P("mp", None),
            P(),
            P(None, "mp"),
            P(),
            P("pages", None, None),
            P("pages", None, None),
            P(),
            P(),
            P(),
        ),
        out_specs=P(("pages", "mp"), None),
        check_vma=False,
    )
```

```python
import math

import jax
import jax.numpy as jnp
from jax import lax
from jax.sharding import PartitionSpec as P

HEADS = 20
GROUPS = 8


EPSILON = 1e-06


def rms_rows(values_in):
    return values_in * lax.rsqrt(jnp.mean(values_in * values_in, axis=-1, keepdims=True) + EPSILON)


def head_norm(values_in, scale_vec, head_count):
    row_count, model_width = values_in.shape
    per_head = values_in.reshape(row_count, head_count, model_width // head_count)
    normed = per_head * lax.rsqrt(jnp.mean(per_head * per_head, axis=-1, keepdims=True) + EPSILON)
    return normed.reshape(row_count, model_width) * scale_vec[None, :]


def rotate(values_in, position, head_count):
    row_count, model_width = values_in.shape
    head_dim = model_width // head_count
    half_dim = head_dim // 2
    frequency = jnp.exp(
        jnp.arange(half_dim).astype(jnp.float32) * (-2.0 * math.log(10000.0) / head_dim)
    )
    rotation = position.astype(jnp.float32)[:, None] * frequency[None, :]
    cosine_table = jnp.cos(rotation)[:, None, :]
    sine_table = jnp.sin(rotation)[:, None, :]
    per_head = values_in.reshape(row_count, head_count, head_dim)
    lower_half = per_head[:, :, :half_dim]
    upper_half = per_head[:, :, half_dim:]
    turned = jnp.concatenate(
        [
            lower_half * cosine_table - upper_half * sine_table,
            upper_half * cosine_table + lower_half * sine_table,
        ],
        axis=-1,
    )
    return turned.reshape(row_count, model_width)


def slot_tables(suffix_len, request_group, slot_count):
    end_slots = jnp.cumsum(suffix_len, axis=1)
    start_slots = end_slots - suffix_len
    slot_ids = jnp.arange(slot_count)
    inside = (slot_ids[None, None, :] >= start_slots[:, :, None]) & (
        slot_ids[None, None, :] < end_slots[:, :, None]
    )
    request_ids = jnp.arange(suffix_len.shape[1])
    slot_valid = jnp.any(inside, axis=1)
    request = jnp.sum(jnp.where(inside, request_ids[None, :, None], 0), axis=1)
    offset = slot_ids[None, :] - jnp.sum(jnp.where(inside, start_slots[:, :, None], 0), axis=1)
    group_id = jnp.where(
        slot_valid, jnp.sum(jnp.where(inside, request_group[:, :, None], 0), axis=1), -1
    )
    return (slot_valid, request, offset, group_id)


def prefix_block(query_block, group_block, prefix_keys, prefix_values, key_group, score_scale):
    row_count, model_width = query_block.shape
    head_dim = model_width // HEADS
    query_heads = query_block.reshape(row_count, HEADS, head_dim)
    key_heads = prefix_keys.reshape(-1, HEADS, head_dim)
    value_heads = prefix_values.reshape(-1, HEADS, head_dim)
    scores = (
        jnp.einsum("qhd,khd->qhk", query_heads, key_heads, preferred_element_type=jnp.float32)
        * score_scale
    )
    allowed = group_block[:, None] == key_group[None, :]
    weights = jnp.where(allowed[:, None, :], jnp.exp(scores), 0.0)
    weight_sum = jnp.sum(weights, axis=-1)
    summed = jnp.einsum(
        "qhk,khd->qhd",
        weights.astype(jnp.bfloat16),
        value_heads,
        preferred_element_type=jnp.float32,
    )
    return (summed.reshape(row_count, model_width), weight_sum)


def shards_columns(
    hidden_in,
    w_qkv,
    w_out,
    w_gate_up,
    w_down,
    scale_qk,
    scale_gate_up,
    eigen_rates,
    cache_keys,
    cache_values,
    page_table,
    request_group,
    suffix_len,
):
    slot_count, model_width = hidden_in.shape
    head_dim = model_width // HEADS
    score_scale = 1.0 / math.sqrt(head_dim)
    mp_count = lax.axis_size("mp")
    mp_index = lax.axis_index("mp")
    own_rows = slot_count // mp_count
    row_first = mp_index * own_rows
    shard_index = lax.axis_index("pages")
    pages_here, page_len = (cache_keys.shape[0], cache_keys.shape[1])
    pool_pages = page_table.shape[0]
    prefix_pages = pool_pages // GROUPS
    slot_valid, request, offset, group_id = slot_tables(suffix_len, request_group, slot_count)
    live_shard = lax.dynamic_index_in_dim(slot_valid, shard_index, 0, keepdims=False)
    request_shard = lax.dynamic_index_in_dim(request, shard_index, 0, keepdims=False)
    offset_shard = lax.dynamic_index_in_dim(offset, shard_index, 0, keepdims=False)
    position_shard = prefix_pages * page_len + offset_shard
    live_own = lax.dynamic_slice_in_dim(live_shard, row_first, own_rows, 0)
    request_own = lax.dynamic_slice_in_dim(request_shard, row_first, own_rows, 0)
    offset_own = lax.dynamic_slice_in_dim(offset_shard, row_first, own_rows, 0)
    position_own = lax.dynamic_slice_in_dim(position_shard, row_first, own_rows, 0)
    state_in = rms_rows(hidden_in.astype(jnp.float32)).astype(jnp.bfloat16)
    projected = jnp.einsum(
        "sd,jdc->jsc", state_in, w_qkv, preferred_element_type=jnp.float32
    ).astype(jnp.bfloat16)
    columns = lax.all_gather(projected, "mp", axis=2, tiled=True)
    query_raw = lax.dynamic_slice_in_dim(columns[0], row_first, own_rows, 0)
    key_raw, value_rows = (columns[1], columns[2])
    queries = head_norm(
        rotate(query_raw.astype(jnp.float32), position_own, HEADS), scale_qk, HEADS
    ).astype(jnp.bfloat16)
    keys_new = head_norm(
        rotate(key_raw.astype(jnp.float32), position_shard, HEADS), scale_qk, HEADS
    ).astype(jnp.bfloat16)
    query_heads = queries.reshape(own_rows, HEADS, head_dim)
    scores = (
        jnp.einsum(
            "qhd,khd->hqk",
            query_heads,
            keys_new.reshape(slot_count, HEADS, head_dim),
            preferred_element_type=jnp.float32,
        )
        * score_scale
    )
    allowed = (
        (request_own[:, None] == request_shard[None, :])
        & (offset_shard[None, :] <= offset_own[:, None])
        & live_own[:, None]
        & live_shard[None, :]
    )
    weights = jnp.where(allowed[None], jnp.exp(scores), 0.0)
    suffix_total = jnp.sum(weights, axis=-1)
    suffix_sum = jnp.einsum(
        "hqk,khd->qhd",
        weights.astype(jnp.bfloat16),
        value_rows.reshape(slot_count, HEADS, head_dim),
        preferred_element_type=jnp.float32,
    )
    physical = shard_index * pages_here + jnp.arange(pages_here, dtype=jnp.int32)
    matches = page_table[:, None] == physical[None, :]
    logical = jnp.sum(
        jnp.where(matches, jnp.arange(pool_pages, dtype=jnp.int32)[:, None], 0), axis=0
    )
    key_group = jnp.repeat(logical // prefix_pages, page_len)
    prefix_keys = head_norm(
        cache_keys.reshape(pages_here * page_len, model_width).astype(jnp.float32), scale_qk, HEADS
    ).astype(jnp.bfloat16)
    prefix_values = cache_values.reshape(pages_here * page_len, model_width)
    gathered = lax.all_gather(queries, "pages", axis=0, tiled=True)
    gathered_group = lax.dynamic_slice_in_dim(group_id, row_first, own_rows, 1).reshape(-1)
    row_count = own_rows * lax.axis_size("pages")
    block_rows = row_count if row_count <= 512 else math.gcd(row_count, 512)

    def attend_block(block_first):
        query_block = lax.dynamic_slice_in_dim(gathered, block_first, block_rows, 0)
        group_block = lax.dynamic_slice_in_dim(gathered_group, block_first, block_rows, 0)
        return prefix_block(
            query_block, group_block, prefix_keys, prefix_values, key_group, score_scale
        )

    block_starts = jnp.arange(row_count // block_rows, dtype=jnp.int32) * block_rows
    summed, weight_sum = lax.map(attend_block, block_starts)
    prefix_sum, prefix_total = lax.psum_scatter(
        (summed.reshape(row_count, model_width), weight_sum.reshape(row_count, HEADS)),
        "pages",
        scatter_dimension=0,
        tiled=True,
    )
    denominator = suffix_total.T + prefix_total + (1.0 - live_own.astype(jnp.float32))[:, None]
    mixed = (suffix_sum + prefix_sum.reshape(own_rows, HEADS, head_dim)) / denominator[:, :, None]
    attention = mixed.reshape(own_rows, model_width).astype(jnp.bfloat16)
    projected_out = jnp.dot(
        lax.all_gather(attention, "mp", axis=0, tiled=True),
        w_out,
        preferred_element_type=jnp.float32,
    )
    residual_in = state_in.astype(jnp.float32)
    state_mid = rms_rows(
        residual_in + eigen_rates[0][None, :] * (rms_rows(projected_out) - residual_in)
    ).astype(jnp.bfloat16)
    state_own = lax.dynamic_slice_in_dim(state_mid, row_first, own_rows, 0)
    gate_up = jnp.einsum("sd,jdf->jsf", state_mid, w_gate_up, preferred_element_type=jnp.float32)
    hidden = (
        jax.nn.silu(scale_gate_up[0][None, :] * gate_up[0])
        * (scale_gate_up[1][None, :] * gate_up[1])
    ).astype(jnp.bfloat16)
    feed_sum = lax.psum_scatter(
        jnp.dot(hidden, w_down, preferred_element_type=jnp.float32),
        "mp",
        scatter_dimension=0,
        tiled=True,
    )
    middle = state_own.astype(jnp.float32)
    result = rms_rows(middle + eigen_rates[1][None, :] * (rms_rows(feed_sum) - middle))
    return (live_own.astype(jnp.float32)[:, None] * result).astype(jnp.bfloat16)


def shards_heads(
    hidden_in,
    w_qkv,
    w_out,
    w_gate_up,
    w_down,
    scale_qk,
    scale_gate_up,
    eigen_rates,
    cache_keys,
    cache_values,
    page_table,
    request_group,
    suffix_len,
):
    slot_count, model_width = hidden_in.shape
    head_dim = model_width // HEADS
    score_scale = 1.0 / math.sqrt(head_dim)
    mp_count = lax.axis_size("mp")
    mp_index = lax.axis_index("mp")
    local_heads = HEADS // mp_count
    local_width = local_heads * head_dim
    own_rows = slot_count // mp_count
    row_first = mp_index * own_rows
    shard_index = lax.axis_index("pages")
    pages_here, page_len = (cache_keys.shape[0], cache_keys.shape[1])
    pool_pages = page_table.shape[0]
    prefix_pages = pool_pages // GROUPS
    slot_valid, request, offset, group_id = slot_tables(suffix_len, request_group, slot_count)
    live_shard = lax.dynamic_index_in_dim(slot_valid, shard_index, 0, keepdims=False)
    request_shard = lax.dynamic_index_in_dim(request, shard_index, 0, keepdims=False)
    offset_shard = lax.dynamic_index_in_dim(offset, shard_index, 0, keepdims=False)
    position_shard = prefix_pages * page_len + offset_shard
    live_own = lax.dynamic_slice_in_dim(live_shard, row_first, own_rows, 0)
    scale_local = lax.dynamic_slice_in_dim(scale_qk, mp_index * local_width, local_width, 0)
    state_in = rms_rows(hidden_in.astype(jnp.float32)).astype(jnp.bfloat16)
    projected = jnp.einsum(
        "sd,jdc->jsc", state_in, w_qkv, preferred_element_type=jnp.float32
    ).astype(jnp.bfloat16)
    queries = head_norm(
        rotate(projected[0].astype(jnp.float32), position_shard, local_heads), scale_local, local_heads
    ).astype(jnp.bfloat16)
    keys_new = head_norm(
        rotate(projected[1].astype(jnp.float32), position_shard, local_heads), scale_local, local_heads
    ).astype(jnp.bfloat16)
    value_rows = projected[2]
    gathered = lax.all_to_all(
        jnp.tile(queries, (lax.axis_size("pages"), 1)), "pages", 0, 0, tiled=True
    )
    scores = (
        jnp.einsum(
            "qhd,khd->hqk",
            queries.reshape(slot_count, local_heads, head_dim),
            keys_new.reshape(slot_count, local_heads, head_dim),
            preferred_element_type=jnp.float32,
        )
        * score_scale
    )
    allowed = (
        (request_shard[:, None] == request_shard[None, :])
        & (offset_shard[None, :] <= offset_shard[:, None])
        & live_shard[:, None]
        & live_shard[None, :]
    )
    weights = jnp.where(allowed[None], jnp.exp(scores), 0.0)
    suffix_total = jnp.sum(weights, axis=-1)
    suffix_sum = jnp.einsum(
        "hqk,khd->qhd",
        weights.astype(jnp.bfloat16),
        value_rows.reshape(slot_count, local_heads, head_dim),
        preferred_element_type=jnp.float32,
    )
    physical = shard_index * pages_here + jnp.arange(pages_here, dtype=jnp.int32)
    matches = page_table[:, None] == physical[None, :]
    logical = jnp.sum(
        jnp.where(matches, jnp.arange(pool_pages, dtype=jnp.int32)[:, None], 0), axis=0
    )
    key_group = jnp.repeat(logical // prefix_pages, page_len)
    cache_local = lax.dynamic_slice_in_dim(cache_keys, mp_index * local_width, local_width, 2)
    prefix_keys = head_norm(
        cache_local.reshape(pages_here * page_len, local_width).astype(jnp.float32),
        scale_local,
        local_heads,
    ).astype(jnp.bfloat16)
    prefix_values = lax.dynamic_slice_in_dim(
        cache_values, mp_index * local_width, local_width, 2
    ).reshape(pages_here * page_len, local_width)
    pages_count = lax.axis_size("pages")
    key_heads = prefix_keys.reshape(-1, local_heads, head_dim)
    value_heads = prefix_values.reshape(-1, local_heads, head_dim)
    gathered_heads = gathered.reshape(pages_count, slot_count, local_heads, head_dim)
    chunk_count = 4 if pages_count % 4 == 0 else 1
    chunk_pages = pages_count // chunk_count
    pieces = []
    for chunk in range(chunk_count):
        query_chunk = lax.slice_in_dim(
            gathered_heads, chunk * chunk_pages, (chunk + 1) * chunk_pages, axis=0
        )
        group_chunk = lax.slice_in_dim(
            group_id, chunk * chunk_pages, (chunk + 1) * chunk_pages, axis=0
        )
        prefix_scores = (
            jnp.einsum(
                "pshd,khd->phks", query_chunk, key_heads, preferred_element_type=jnp.float32
            )
            * score_scale
        )
        prefix_allowed = key_group[None, :, None] == group_chunk[:, None, :]
        prefix_weights = jnp.where(prefix_allowed[:, None], jnp.exp(prefix_scores), 0.0)
        weight_sum = jnp.sum(prefix_weights, axis=2)
        summed = jnp.einsum(
            "phks,khd->pshd",
            prefix_weights.astype(jnp.bfloat16),
            value_heads,
            preferred_element_type=jnp.float32,
        )
        pieces.append(
            jnp.concatenate(
                [
                    summed.reshape(chunk_pages, slot_count, local_width),
                    jnp.transpose(weight_sum, (0, 2, 1)),
                ],
                axis=2,
            ).astype(jnp.bfloat16)
        )
    prefix_parts = lax.all_to_all(
        jnp.concatenate(pieces, axis=0).reshape(pages_count * slot_count, local_width + local_heads),
        "pages",
        0,
        0,
        tiled=True,
    )
    prefix_both = jnp.sum(
        prefix_parts.reshape(pages_count, slot_count, local_width + local_heads).astype(jnp.float32),
        axis=0,
    )
    prefix_sum = prefix_both[:, :local_width]
    prefix_total = prefix_both[:, local_width:]
    denominator = suffix_total.T + prefix_total + (1.0 - live_shard.astype(jnp.float32))[:, None]
    mixed = (suffix_sum + prefix_sum.reshape(slot_count, local_heads, head_dim)) / denominator[
        :, :, None
    ]
    attention_local = mixed.reshape(slot_count, local_width).astype(jnp.bfloat16)
    attention = lax.all_gather(attention_local, "mp", axis=1, tiled=True)
    projected_out = jnp.dot(attention, w_out, preferred_element_type=jnp.float32)
    residual_in = state_in.astype(jnp.float32)
    state_mid = rms_rows(
        residual_in + eigen_rates[0][None, :] * (rms_rows(projected_out) - residual_in)
    ).astype(jnp.bfloat16)
    state_own = lax.dynamic_slice_in_dim(state_mid, row_first, own_rows, 0)
    gate_up = jnp.einsum("sd,jdf->jsf", state_mid, w_gate_up, preferred_element_type=jnp.float32)
    hidden = (
        jax.nn.silu(scale_gate_up[0][None, :] * gate_up[0])
        * (scale_gate_up[1][None, :] * gate_up[1])
    ).astype(jnp.bfloat16)
    feed_parts = lax.all_to_all(
        jnp.dot(hidden, w_down, preferred_element_type=jnp.float32).astype(jnp.bfloat16),
        "mp",
        0,
        0,
        tiled=True,
    )
    feed_sum = jnp.sum(
        feed_parts.reshape(mp_count, own_rows, model_width).astype(jnp.float32), axis=0
    )
    middle = state_own.astype(jnp.float32)
    result = rms_rows(middle + eigen_rates[1][None, :] * (rms_rows(feed_sum) - middle))
    return (live_own.astype(jnp.float32)[:, None] * result).astype(jnp.bfloat16)


def solution(mesh):
    shards = shards_heads if HEADS % mesh.shape["mp"] == 0 else shards_columns
    return jax.shard_map(
        shards,
        mesh=mesh,
        in_specs=(
            P("pages", None),
            P(None, None, "mp"),
            P(),
            P(None, None, "mp"),
            P("mp", None),
            P(),
            P(None, "mp"),
            P(),
            P("pages", None, None),
            P("pages", None, None),
            P(),
            P(),
            P(),
        ),
        out_specs=P(("pages", "mp"), None),
        check_vma=False,
    )
```

```python
import math

import jax
import jax.numpy as jnp
from jax import lax
from jax.sharding import PartitionSpec as P

HEADS = 20
GROUPS = 8


EPSILON = 1e-06


def rms_rows(values_in):
    return values_in * lax.rsqrt(jnp.mean(values_in * values_in, axis=-1, keepdims=True) + EPSILON)


def head_norm(values_in, scale_vec, head_count):
    row_count, model_width = values_in.shape
    per_head = values_in.reshape(row_count, head_count, model_width // head_count)
    normed = per_head * lax.rsqrt(jnp.mean(per_head * per_head, axis=-1, keepdims=True) + EPSILON)
    return normed.reshape(row_count, model_width) * scale_vec[None, :]


def rotate(values_in, position, head_count):
    row_count, model_width = values_in.shape
    head_dim = model_width // head_count
    half_dim = head_dim // 2
    frequency = jnp.exp(
        jnp.arange(half_dim).astype(jnp.float32) * (-2.0 * math.log(10000.0) / head_dim)
    )
    rotation = position.astype(jnp.float32)[:, None] * frequency[None, :]
    cosine_table = jnp.cos(rotation)[:, None, :]
    sine_table = jnp.sin(rotation)[:, None, :]
    per_head = values_in.reshape(row_count, head_count, head_dim)
    lower_half = per_head[:, :, :half_dim]
    upper_half = per_head[:, :, half_dim:]
    turned = jnp.concatenate(
        [
            lower_half * cosine_table - upper_half * sine_table,
            upper_half * cosine_table + lower_half * sine_table,
        ],
        axis=-1,
    )
    return turned.reshape(row_count, model_width)


def slot_tables(suffix_len, request_group, slot_count):
    running = [suffix_len[:, 0]]
    for column in range(1, suffix_len.shape[1]):
        running.append(running[-1] + suffix_len[:, column])
    end_slots = jnp.stack(running, axis=1)
    start_slots = end_slots - suffix_len
    slot_ids = jnp.arange(slot_count)
    inside = (slot_ids[None, None, :] >= start_slots[:, :, None]) & (
        slot_ids[None, None, :] < end_slots[:, :, None]
    )
    request_ids = jnp.arange(suffix_len.shape[1])
    slot_valid = jnp.any(inside, axis=1)
    request = jnp.sum(jnp.where(inside, request_ids[None, :, None], 0), axis=1)
    offset = slot_ids[None, :] - jnp.sum(jnp.where(inside, start_slots[:, :, None], 0), axis=1)
    group_id = jnp.where(
        slot_valid, jnp.sum(jnp.where(inside, request_group[:, :, None], 0), axis=1), -1
    )
    return (slot_valid, request, offset, group_id)


def prefix_block(query_block, group_block, prefix_keys, prefix_values, key_group, score_scale):
    row_count, model_width = query_block.shape
    head_dim = model_width // HEADS
    query_heads = query_block.reshape(row_count, HEADS, head_dim)
    key_heads = prefix_keys.reshape(-1, HEADS, head_dim)
    value_heads = prefix_values.reshape(-1, HEADS, head_dim)
    scores = (
        jnp.einsum("qhd,khd->qhk", query_heads, key_heads, preferred_element_type=jnp.float32)
        * score_scale
    )
    allowed = group_block[:, None] == key_group[None, :]
    weights = jnp.where(allowed[:, None, :], jnp.exp(scores), 0.0)
    weight_sum = jnp.sum(weights, axis=-1)
    summed = jnp.einsum(
        "qhk,khd->qhd",
        weights.astype(jnp.bfloat16),
        value_heads,
        preferred_element_type=jnp.float32,
    )
    return (summed.reshape(row_count, model_width), weight_sum)


def shards_columns(
    hidden_in,
    w_qkv,
    w_out,
    w_gate_up,
    w_down,
    scale_qk,
    scale_gate_up,
    eigen_rates,
    cache_keys,
    cache_values,
    page_table,
    request_group,
    suffix_len,
):
    slot_count, model_width = hidden_in.shape
    head_dim = model_width // HEADS
    score_scale = 1.0 / math.sqrt(head_dim)
    mp_count = lax.axis_size("mp")
    mp_index = lax.axis_index("mp")
    own_rows = slot_count // mp_count
    row_first = mp_index * own_rows
    shard_index = lax.axis_index("pages")
    pages_here, page_len = (cache_keys.shape[0], cache_keys.shape[1])
    pool_pages = page_table.shape[0]
    prefix_pages = pool_pages // GROUPS
    slot_valid, request, offset, group_id = slot_tables(suffix_len, request_group, slot_count)
    live_shard = lax.dynamic_index_in_dim(slot_valid, shard_index, 0, keepdims=False)
    request_shard = lax.dynamic_index_in_dim(request, shard_index, 0, keepdims=False)
    offset_shard = lax.dynamic_index_in_dim(offset, shard_index, 0, keepdims=False)
    position_shard = prefix_pages * page_len + offset_shard
    live_own = lax.dynamic_slice_in_dim(live_shard, row_first, own_rows, 0)
    request_own = lax.dynamic_slice_in_dim(request_shard, row_first, own_rows, 0)
    offset_own = lax.dynamic_slice_in_dim(offset_shard, row_first, own_rows, 0)
    position_own = lax.dynamic_slice_in_dim(position_shard, row_first, own_rows, 0)
    state_in = rms_rows(hidden_in.astype(jnp.float32)).astype(jnp.bfloat16)
    projected = jnp.einsum(
        "sd,jdc->jsc", state_in, w_qkv, preferred_element_type=jnp.float32
    ).astype(jnp.bfloat16)
    columns = lax.all_gather(projected, "mp", axis=2, tiled=True)
    query_raw = lax.dynamic_slice_in_dim(columns[0], row_first, own_rows, 0)
    key_raw, value_rows = (columns[1], columns[2])
    queries = head_norm(
        rotate(query_raw.astype(jnp.float32), position_own, HEADS), scale_qk, HEADS
    ).astype(jnp.bfloat16)
    keys_new = head_norm(
        rotate(key_raw.astype(jnp.float32), position_shard, HEADS), scale_qk, HEADS
    ).astype(jnp.bfloat16)
    query_heads = queries.reshape(own_rows, HEADS, head_dim)
    scores = (
        jnp.einsum(
            "qhd,khd->hqk",
            query_heads,
            keys_new.reshape(slot_count, HEADS, head_dim),
            preferred_element_type=jnp.float32,
        )
        * score_scale
    )
    allowed = (
        (request_own[:, None] == request_shard[None, :])
        & (offset_shard[None, :] <= offset_own[:, None])
        & live_own[:, None]
        & live_shard[None, :]
    )
    weights = jnp.where(allowed[None], jnp.exp(scores), 0.0)
    suffix_total = jnp.sum(weights, axis=-1)
    suffix_sum = jnp.einsum(
        "hqk,khd->qhd",
        weights.astype(jnp.bfloat16),
        value_rows.reshape(slot_count, HEADS, head_dim),
        preferred_element_type=jnp.float32,
    )
    physical = shard_index * pages_here + jnp.arange(pages_here, dtype=jnp.int32)
    matches = page_table[:, None] == physical[None, :]
    logical = jnp.sum(
        jnp.where(matches, jnp.arange(pool_pages, dtype=jnp.int32)[:, None], 0), axis=0
    )
    key_group = jnp.repeat(logical // prefix_pages, page_len)
    prefix_keys = head_norm(
        cache_keys.reshape(pages_here * page_len, model_width).astype(jnp.float32), scale_qk, HEADS
    ).astype(jnp.bfloat16)
    prefix_values = cache_values.reshape(pages_here * page_len, model_width)
    gathered = lax.all_gather(queries, "pages", axis=0, tiled=True)
    gathered_group = lax.dynamic_slice_in_dim(group_id, row_first, own_rows, 1).reshape(-1)
    row_count = own_rows * lax.axis_size("pages")
    block_rows = row_count if row_count <= 512 else math.gcd(row_count, 512)

    def attend_block(block_first):
        query_block = lax.dynamic_slice_in_dim(gathered, block_first, block_rows, 0)
        group_block = lax.dynamic_slice_in_dim(gathered_group, block_first, block_rows, 0)
        return prefix_block(
            query_block, group_block, prefix_keys, prefix_values, key_group, score_scale
        )

    block_starts = jnp.arange(row_count // block_rows, dtype=jnp.int32) * block_rows
    summed, weight_sum = lax.map(attend_block, block_starts)
    prefix_sum, prefix_total = lax.psum_scatter(
        (summed.reshape(row_count, model_width), weight_sum.reshape(row_count, HEADS)),
        "pages",
        scatter_dimension=0,
        tiled=True,
    )
    denominator = suffix_total.T + prefix_total + (1.0 - live_own.astype(jnp.float32))[:, None]
    mixed = (suffix_sum + prefix_sum.reshape(own_rows, HEADS, head_dim)) / denominator[:, :, None]
    attention = mixed.reshape(own_rows, model_width).astype(jnp.bfloat16)
    projected_out = jnp.dot(
        lax.all_gather(attention, "mp", axis=0, tiled=True),
        w_out,
        preferred_element_type=jnp.float32,
    )
    residual_in = state_in.astype(jnp.float32)
    state_mid = rms_rows(
        residual_in + eigen_rates[0][None, :] * (rms_rows(projected_out) - residual_in)
    ).astype(jnp.bfloat16)
    state_own = lax.dynamic_slice_in_dim(state_mid, row_first, own_rows, 0)
    gate_up = jnp.einsum("sd,jdf->jsf", state_mid, w_gate_up, preferred_element_type=jnp.float32)
    hidden = (
        jax.nn.silu(scale_gate_up[0][None, :] * gate_up[0])
        * (scale_gate_up[1][None, :] * gate_up[1])
    ).astype(jnp.bfloat16)
    feed_sum = lax.psum_scatter(
        jnp.dot(hidden, w_down, preferred_element_type=jnp.float32),
        "mp",
        scatter_dimension=0,
        tiled=True,
    )
    middle = state_own.astype(jnp.float32)
    result = rms_rows(middle + eigen_rates[1][None, :] * (rms_rows(feed_sum) - middle))
    return (live_own.astype(jnp.float32)[:, None] * result).astype(jnp.bfloat16)


def shards_heads(
    hidden_in,
    w_qkv,
    w_out,
    w_gate_up,
    w_down,
    scale_qk,
    scale_gate_up,
    eigen_rates,
    cache_keys,
    cache_values,
    page_table,
    request_group,
    suffix_len,
):
    slot_count, model_width = hidden_in.shape
    head_dim = model_width // HEADS
    score_scale = 1.0 / math.sqrt(head_dim)
    mp_count = lax.axis_size("mp")
    mp_index = lax.axis_index("mp")
    local_heads = HEADS // mp_count
    local_width = local_heads * head_dim
    own_rows = slot_count // mp_count
    row_first = mp_index * own_rows
    shard_index = lax.axis_index("pages")
    pages_here, page_len = (cache_keys.shape[0], cache_keys.shape[1])
    pool_pages = page_table.shape[0]
    prefix_pages = pool_pages // GROUPS
    slot_valid, request, offset, group_id = slot_tables(suffix_len, request_group, slot_count)
    live_shard = lax.dynamic_index_in_dim(slot_valid, shard_index, 0, keepdims=False)
    request_shard = lax.dynamic_index_in_dim(request, shard_index, 0, keepdims=False)
    offset_shard = lax.dynamic_index_in_dim(offset, shard_index, 0, keepdims=False)
    position_shard = prefix_pages * page_len + offset_shard
    live_own = lax.dynamic_slice_in_dim(live_shard, row_first, own_rows, 0)
    scale_local = lax.dynamic_slice_in_dim(scale_qk, mp_index * local_width, local_width, 0)
    state_in = rms_rows(hidden_in.astype(jnp.float32)).astype(jnp.bfloat16)
    projected_query = jnp.dot(state_in, w_qkv[0], preferred_element_type=jnp.float32).astype(
        jnp.bfloat16
    )
    queries = head_norm(
        rotate(projected_query.astype(jnp.float32), position_shard, local_heads),
        scale_local,
        local_heads,
    ).astype(jnp.bfloat16)
    gathered = lax.all_to_all(
        jnp.tile(queries, (lax.axis_size("pages"), 1)), "pages", 0, 0, tiled=True
    )
    state_kv, _ = lax.optimization_barrier((state_in, gathered[:1, :1]))
    projected = jnp.einsum(
        "sd,jdc->jsc", state_kv, w_qkv[1:], preferred_element_type=jnp.float32
    ).astype(jnp.bfloat16)
    keys_new = head_norm(
        rotate(projected[0].astype(jnp.float32), position_shard, local_heads), scale_local, local_heads
    ).astype(jnp.bfloat16)
    value_rows = projected[1]
    scores = (
        jnp.einsum(
            "qhd,khd->hqk",
            queries.reshape(slot_count, local_heads, head_dim),
            keys_new.reshape(slot_count, local_heads, head_dim),
            preferred_element_type=jnp.float32,
        )
        * score_scale
    )
    allowed = (
        (request_shard[:, None] == request_shard[None, :])
        & (offset_shard[None, :] <= offset_shard[:, None])
        & live_shard[:, None]
        & live_shard[None, :]
    )
    weights = jnp.where(allowed[None], jnp.exp(scores), 0.0)
    suffix_total = jnp.sum(weights, axis=-1)
    suffix_sum = jnp.einsum(
        "hqk,khd->qhd",
        weights.astype(jnp.bfloat16),
        value_rows.reshape(slot_count, local_heads, head_dim),
        preferred_element_type=jnp.float32,
    )
    physical = shard_index * pages_here + jnp.arange(pages_here, dtype=jnp.int32)
    matches = page_table[:, None] == physical[None, :]
    logical = jnp.sum(
        jnp.where(matches, jnp.arange(pool_pages, dtype=jnp.int32)[:, None], 0), axis=0
    )
    key_group = jnp.repeat(logical // prefix_pages, page_len)
    cache_local = lax.dynamic_slice_in_dim(cache_keys, mp_index * local_width, local_width, 2)
    prefix_keys = head_norm(
        cache_local.reshape(pages_here * page_len, local_width).astype(jnp.float32),
        scale_local,
        local_heads,
    ).astype(jnp.bfloat16)
    prefix_values = lax.dynamic_slice_in_dim(
        cache_values, mp_index * local_width, local_width, 2
    ).reshape(pages_here * page_len, local_width)
    pages_count = lax.axis_size("pages")
    key_heads = prefix_keys.reshape(-1, local_heads, head_dim)
    value_heads = prefix_values.reshape(-1, local_heads, head_dim)
    gathered_heads = gathered.reshape(pages_count, slot_count, local_heads, head_dim)
    chunk_count = 2 if pages_count % 2 == 0 else 1
    chunk_pages = pages_count // chunk_count
    pieces = []
    for chunk in range(chunk_count):
        query_chunk = lax.slice_in_dim(
            gathered_heads, chunk * chunk_pages, (chunk + 1) * chunk_pages, axis=0
        )
        group_chunk = lax.slice_in_dim(
            group_id, chunk * chunk_pages, (chunk + 1) * chunk_pages, axis=0
        )
        prefix_scores = (
            jnp.einsum(
                "pshd,khd->phks", query_chunk, key_heads, preferred_element_type=jnp.float32
            )
            * score_scale
        )
        prefix_allowed = key_group[None, :, None] == group_chunk[:, None, :]
        prefix_weights = jnp.where(prefix_allowed[:, None], jnp.exp(prefix_scores), 0.0)
        weight_sum = jnp.sum(prefix_weights, axis=2)
        summed = jnp.einsum(
            "phks,khd->pshd",
            prefix_weights.astype(jnp.bfloat16),
            value_heads,
            preferred_element_type=jnp.float32,
        )
        pieces.append(
            jnp.concatenate(
                [
                    summed.reshape(chunk_pages, slot_count, local_width),
                    jnp.transpose(weight_sum, (0, 2, 1)),
                ],
                axis=2,
            ).astype(jnp.bfloat16)
        )
    prefix_parts = lax.all_to_all(
        jnp.concatenate(pieces, axis=0).reshape(pages_count * slot_count, local_width + local_heads),
        "pages",
        0,
        0,
        tiled=True,
    )
    prefix_both = jnp.sum(
        prefix_parts.reshape(pages_count, slot_count, local_width + local_heads).astype(jnp.float32),
        axis=0,
    )
    prefix_sum = prefix_both[:, :local_width]
    prefix_total = prefix_both[:, local_width:]
    denominator = suffix_total.T + prefix_total + (1.0 - live_shard.astype(jnp.float32))[:, None]
    mixed = (suffix_sum + prefix_sum.reshape(slot_count, local_heads, head_dim)) / denominator[
        :, :, None
    ]
    attention_local = mixed.reshape(slot_count, local_width).astype(jnp.bfloat16)
    attention = lax.all_gather(attention_local, "mp", axis=1, tiled=True)
    projected_out = jnp.dot(attention, w_out, preferred_element_type=jnp.float32)
    residual_in = state_in.astype(jnp.float32)
    state_mid = rms_rows(
        residual_in + eigen_rates[0][None, :] * (rms_rows(projected_out) - residual_in)
    ).astype(jnp.bfloat16)
    state_own = lax.dynamic_slice_in_dim(state_mid, row_first, own_rows, 0)
    gate_up = jnp.einsum("sd,jdf->jsf", state_mid, w_gate_up, preferred_element_type=jnp.float32)
    hidden = (
        jax.nn.silu(scale_gate_up[0][None, :] * gate_up[0])
        * (scale_gate_up[1][None, :] * gate_up[1])
    ).astype(jnp.bfloat16)
    feed_parts = lax.all_to_all(
        jnp.dot(hidden, w_down, preferred_element_type=jnp.float32).astype(jnp.bfloat16),
        "mp",
        0,
        0,
        tiled=True,
    )
    feed_sum = jnp.sum(
        feed_parts.reshape(mp_count, own_rows, model_width).astype(jnp.float32), axis=0
    )
    middle = state_own.astype(jnp.float32)
    result = rms_rows(middle + eigen_rates[1][None, :] * (rms_rows(feed_sum) - middle))
    return (live_own.astype(jnp.float32)[:, None] * result).astype(jnp.bfloat16)


def solution(mesh):
    shards = shards_heads if HEADS % mesh.shape["mp"] == 0 else shards_columns
    return jax.shard_map(
        shards,
        mesh=mesh,
        in_specs=(
            P("pages", None),
            P(None, None, "mp"),
            P(),
            P(None, None, "mp"),
            P("mp", None),
            P(),
            P(None, "mp"),
            P(),
            P("pages", None, None),
            P("pages", None, None),
            P(),
            P(),
            P(),
        ),
        out_specs=P(("pages", "mp"), None),
        check_vma=False,
    )
```

```python
import math

import jax
import jax.numpy as jnp
from jax import lax
from jax.sharding import PartitionSpec as P

HEADS = 20
GROUPS = 8


EPSILON = 1e-06


def rms_rows(values_in):
    return values_in * lax.rsqrt(jnp.mean(values_in * values_in, axis=-1, keepdims=True) + EPSILON)


def head_norm(values_in, scale_vec, head_count):
    row_count, model_width = values_in.shape
    per_head = values_in.reshape(row_count, head_count, model_width // head_count)
    normed = per_head * lax.rsqrt(jnp.mean(per_head * per_head, axis=-1, keepdims=True) + EPSILON)
    return normed.reshape(row_count, model_width) * scale_vec[None, :]


def rotate(values_in, position, head_count):
    row_count, model_width = values_in.shape
    head_dim = model_width // head_count
    half_dim = head_dim // 2
    frequency = jnp.exp(
        jnp.arange(half_dim).astype(jnp.float32) * (-2.0 * math.log(10000.0) / head_dim)
    )
    rotation = position.astype(jnp.float32)[:, None] * frequency[None, :]
    cosine_table = jnp.cos(rotation)[:, None, :]
    sine_table = jnp.sin(rotation)[:, None, :]
    per_head = values_in.reshape(row_count, head_count, head_dim)
    lower_half = per_head[:, :, :half_dim]
    upper_half = per_head[:, :, half_dim:]
    turned = jnp.concatenate(
        [
            lower_half * cosine_table - upper_half * sine_table,
            upper_half * cosine_table + lower_half * sine_table,
        ],
        axis=-1,
    )
    return turned.reshape(row_count, model_width)


def slot_tables(suffix_len, request_group, slot_count):
    end_slots = jnp.cumsum(suffix_len, axis=1)
    start_slots = end_slots - suffix_len
    slot_ids = jnp.arange(slot_count)
    inside = (slot_ids[None, None, :] >= start_slots[:, :, None]) & (
        slot_ids[None, None, :] < end_slots[:, :, None]
    )
    request_ids = jnp.arange(suffix_len.shape[1])
    slot_valid = jnp.any(inside, axis=1)
    request = jnp.sum(jnp.where(inside, request_ids[None, :, None], 0), axis=1)
    offset = slot_ids[None, :] - jnp.sum(jnp.where(inside, start_slots[:, :, None], 0), axis=1)
    group_id = jnp.where(
        slot_valid, jnp.sum(jnp.where(inside, request_group[:, :, None], 0), axis=1), -1
    )
    return (slot_valid, request, offset, group_id)


def prefix_block(query_block, group_block, prefix_keys, prefix_values, key_group, score_scale):
    row_count, model_width = query_block.shape
    head_dim = model_width // HEADS
    query_heads = query_block.reshape(row_count, HEADS, head_dim)
    key_heads = prefix_keys.reshape(-1, HEADS, head_dim)
    value_heads = prefix_values.reshape(-1, HEADS, head_dim)
    scores = (
        jnp.einsum("qhd,khd->qhk", query_heads, key_heads, preferred_element_type=jnp.float32)
        * score_scale
    )
    allowed = group_block[:, None] == key_group[None, :]
    weights = jnp.where(allowed[:, None, :], jnp.exp(scores), 0.0)
    weight_sum = jnp.sum(weights, axis=-1)
    summed = jnp.einsum(
        "qhk,khd->qhd",
        weights.astype(jnp.bfloat16),
        value_heads,
        preferred_element_type=jnp.float32,
    )
    return (summed.reshape(row_count, model_width), weight_sum)


def shards_columns(
    hidden_in,
    w_qkv,
    w_out,
    w_gate_up,
    w_down,
    scale_qk,
    scale_gate_up,
    eigen_rates,
    cache_keys,
    cache_values,
    page_table,
    request_group,
    suffix_len,
):
    slot_count, model_width = hidden_in.shape
    head_dim = model_width // HEADS
    score_scale = 1.0 / math.sqrt(head_dim)
    mp_count = lax.axis_size("mp")
    mp_index = lax.axis_index("mp")
    own_rows = slot_count // mp_count
    row_first = mp_index * own_rows
    shard_index = lax.axis_index("pages")
    pages_here, page_len = (cache_keys.shape[0], cache_keys.shape[1])
    pool_pages = page_table.shape[0]
    prefix_pages = pool_pages // GROUPS
    slot_valid, request, offset, group_id = slot_tables(suffix_len, request_group, slot_count)
    live_shard = lax.dynamic_index_in_dim(slot_valid, shard_index, 0, keepdims=False)
    request_shard = lax.dynamic_index_in_dim(request, shard_index, 0, keepdims=False)
    offset_shard = lax.dynamic_index_in_dim(offset, shard_index, 0, keepdims=False)
    position_shard = prefix_pages * page_len + offset_shard
    live_own = lax.dynamic_slice_in_dim(live_shard, row_first, own_rows, 0)
    request_own = lax.dynamic_slice_in_dim(request_shard, row_first, own_rows, 0)
    offset_own = lax.dynamic_slice_in_dim(offset_shard, row_first, own_rows, 0)
    position_own = lax.dynamic_slice_in_dim(position_shard, row_first, own_rows, 0)
    state_in = rms_rows(hidden_in.astype(jnp.float32)).astype(jnp.bfloat16)
    projected = jnp.einsum(
        "sd,jdc->jsc", state_in, w_qkv, preferred_element_type=jnp.float32
    ).astype(jnp.bfloat16)
    columns = lax.all_gather(projected, "mp", axis=2, tiled=True)
    query_raw = lax.dynamic_slice_in_dim(columns[0], row_first, own_rows, 0)
    key_raw, value_rows = (columns[1], columns[2])
    queries = head_norm(
        rotate(query_raw.astype(jnp.float32), position_own, HEADS), scale_qk, HEADS
    ).astype(jnp.bfloat16)
    keys_new = head_norm(
        rotate(key_raw.astype(jnp.float32), position_shard, HEADS), scale_qk, HEADS
    ).astype(jnp.bfloat16)
    query_heads = queries.reshape(own_rows, HEADS, head_dim)
    scores = (
        jnp.einsum(
            "qhd,khd->hqk",
            query_heads,
            keys_new.reshape(slot_count, HEADS, head_dim),
            preferred_element_type=jnp.float32,
        )
        * score_scale
    )
    allowed = (
        (request_own[:, None] == request_shard[None, :])
        & (offset_shard[None, :] <= offset_own[:, None])
        & live_own[:, None]
        & live_shard[None, :]
    )
    weights = jnp.where(allowed[None], jnp.exp(scores), 0.0)
    suffix_total = jnp.sum(weights, axis=-1)
    suffix_sum = jnp.einsum(
        "hqk,khd->qhd",
        weights.astype(jnp.bfloat16),
        value_rows.reshape(slot_count, HEADS, head_dim),
        preferred_element_type=jnp.float32,
    )
    physical = shard_index * pages_here + jnp.arange(pages_here, dtype=jnp.int32)
    matches = page_table[:, None] == physical[None, :]
    logical = jnp.sum(
        jnp.where(matches, jnp.arange(pool_pages, dtype=jnp.int32)[:, None], 0), axis=0
    )
    key_group = jnp.repeat(logical // prefix_pages, page_len)
    prefix_keys = head_norm(
        cache_keys.reshape(pages_here * page_len, model_width).astype(jnp.float32), scale_qk, HEADS
    ).astype(jnp.bfloat16)
    prefix_values = cache_values.reshape(pages_here * page_len, model_width)
    gathered = lax.all_gather(queries, "pages", axis=0, tiled=True)
    gathered_group = lax.dynamic_slice_in_dim(group_id, row_first, own_rows, 1).reshape(-1)
    row_count = own_rows * lax.axis_size("pages")
    block_rows = row_count if row_count <= 512 else math.gcd(row_count, 512)

    def attend_block(block_first):
        query_block = lax.dynamic_slice_in_dim(gathered, block_first, block_rows, 0)
        group_block = lax.dynamic_slice_in_dim(gathered_group, block_first, block_rows, 0)
        return prefix_block(
            query_block, group_block, prefix_keys, prefix_values, key_group, score_scale
        )

    block_starts = jnp.arange(row_count // block_rows, dtype=jnp.int32) * block_rows
    summed, weight_sum = lax.map(attend_block, block_starts)
    prefix_sum, prefix_total = lax.psum_scatter(
        (summed.reshape(row_count, model_width), weight_sum.reshape(row_count, HEADS)),
        "pages",
        scatter_dimension=0,
        tiled=True,
    )
    denominator = suffix_total.T + prefix_total + (1.0 - live_own.astype(jnp.float32))[:, None]
    mixed = (suffix_sum + prefix_sum.reshape(own_rows, HEADS, head_dim)) / denominator[:, :, None]
    attention = mixed.reshape(own_rows, model_width).astype(jnp.bfloat16)
    projected_out = jnp.dot(
        lax.all_gather(attention, "mp", axis=0, tiled=True),
        w_out,
        preferred_element_type=jnp.float32,
    )
    residual_in = state_in.astype(jnp.float32)
    state_mid = rms_rows(
        residual_in + eigen_rates[0][None, :] * (rms_rows(projected_out) - residual_in)
    ).astype(jnp.bfloat16)
    state_own = lax.dynamic_slice_in_dim(state_mid, row_first, own_rows, 0)
    gate_up = jnp.einsum("sd,jdf->jsf", state_mid, w_gate_up, preferred_element_type=jnp.float32)
    hidden = (
        jax.nn.silu(scale_gate_up[0][None, :] * gate_up[0])
        * (scale_gate_up[1][None, :] * gate_up[1])
    ).astype(jnp.bfloat16)
    feed_sum = lax.psum_scatter(
        jnp.dot(hidden, w_down, preferred_element_type=jnp.float32),
        "mp",
        scatter_dimension=0,
        tiled=True,
    )
    middle = state_own.astype(jnp.float32)
    result = rms_rows(middle + eigen_rates[1][None, :] * (rms_rows(feed_sum) - middle))
    return (live_own.astype(jnp.float32)[:, None] * result).astype(jnp.bfloat16)


def shards_heads(
    hidden_in,
    w_qkv,
    w_out,
    w_gate_up,
    w_down,
    scale_qk,
    scale_gate_up,
    eigen_rates,
    cache_keys,
    cache_values,
    page_table,
    request_group,
    suffix_len,
):
    slot_count, model_width = hidden_in.shape
    head_dim = model_width // HEADS
    score_scale = 1.0 / math.sqrt(head_dim)
    mp_count = lax.axis_size("mp")
    mp_index = lax.axis_index("mp")
    local_heads = HEADS // mp_count
    local_width = local_heads * head_dim
    own_rows = slot_count // mp_count
    row_first = mp_index * own_rows
    shard_index = lax.axis_index("pages")
    pages_here, page_len = (cache_keys.shape[0], cache_keys.shape[1])
    pool_pages = page_table.shape[0]
    prefix_pages = pool_pages // GROUPS
    slot_valid, request, offset, group_id = slot_tables(suffix_len, request_group, slot_count)
    live_shard = lax.dynamic_index_in_dim(slot_valid, shard_index, 0, keepdims=False)
    request_shard = lax.dynamic_index_in_dim(request, shard_index, 0, keepdims=False)
    offset_shard = lax.dynamic_index_in_dim(offset, shard_index, 0, keepdims=False)
    position_shard = prefix_pages * page_len + offset_shard
    live_own = lax.dynamic_slice_in_dim(live_shard, row_first, own_rows, 0)
    scale_local = lax.dynamic_slice_in_dim(scale_qk, mp_index * local_width, local_width, 0)
    state_in = rms_rows(hidden_in.astype(jnp.float32)).astype(jnp.bfloat16)
    projected = jnp.einsum(
        "sd,jdc->jsc", state_in, w_qkv, preferred_element_type=jnp.float32
    ).astype(jnp.bfloat16)
    queries = head_norm(
        rotate(projected[0].astype(jnp.float32), position_shard, local_heads), scale_local, local_heads
    ).astype(jnp.bfloat16)
    keys_new = head_norm(
        rotate(projected[1].astype(jnp.float32), position_shard, local_heads), scale_local, local_heads
    ).astype(jnp.bfloat16)
    value_rows = projected[2]
    gathered = lax.all_to_all(
        jnp.tile(queries, (lax.axis_size("pages"), 1)), "pages", 0, 0, tiled=True
    )
    scores = (
        jnp.einsum(
            "qhd,khd->hqk",
            queries.reshape(slot_count, local_heads, head_dim),
            keys_new.reshape(slot_count, local_heads, head_dim),
            preferred_element_type=jnp.float32,
        )
        * score_scale
    )
    allowed = (
        (request_shard[:, None] == request_shard[None, :])
        & (offset_shard[None, :] <= offset_shard[:, None])
        & live_shard[:, None]
        & live_shard[None, :]
    )
    weights = jnp.where(allowed[None], jnp.exp(scores), 0.0)
    suffix_total = jnp.sum(weights, axis=-1)
    suffix_sum = jnp.einsum(
        "hqk,khd->qhd",
        weights.astype(jnp.bfloat16),
        value_rows.reshape(slot_count, local_heads, head_dim),
        preferred_element_type=jnp.float32,
    )
    physical = shard_index * pages_here + jnp.arange(pages_here, dtype=jnp.int32)
    matches = page_table[:, None] == physical[None, :]
    logical = jnp.sum(
        jnp.where(matches, jnp.arange(pool_pages, dtype=jnp.int32)[:, None], 0), axis=0
    )
    key_group = jnp.repeat(logical // prefix_pages, page_len)
    cache_local = lax.dynamic_slice_in_dim(cache_keys, mp_index * local_width, local_width, 2)
    prefix_keys = head_norm(
        cache_local.reshape(pages_here * page_len, local_width).astype(jnp.float32),
        scale_local,
        local_heads,
    ).astype(jnp.bfloat16)
    prefix_values = lax.dynamic_slice_in_dim(
        cache_values, mp_index * local_width, local_width, 2
    ).reshape(pages_here * page_len, local_width)
    pages_count = lax.axis_size("pages")
    key_heads = prefix_keys.reshape(-1, local_heads, head_dim)
    value_heads = prefix_values.reshape(-1, local_heads, head_dim)
    gathered_heads = gathered.reshape(pages_count, slot_count, local_heads, head_dim)
    chunk_count = 2 if pages_count % 2 == 0 else 1
    chunk_pages = pages_count // chunk_count
    pieces = []
    for chunk in range(chunk_count):
        query_chunk = lax.slice_in_dim(
            gathered_heads, chunk * chunk_pages, (chunk + 1) * chunk_pages, axis=0
        )
        group_chunk = lax.slice_in_dim(
            group_id, chunk * chunk_pages, (chunk + 1) * chunk_pages, axis=0
        )
        prefix_scores = (
            jnp.einsum(
                "pshd,khd->phks", query_chunk, key_heads, preferred_element_type=jnp.float32
            )
            * score_scale
        )
        prefix_allowed = key_group[None, :, None] == group_chunk[:, None, :]
        prefix_weights = jnp.where(prefix_allowed[:, None], jnp.exp(prefix_scores), 0.0)
        weight_sum = jnp.sum(prefix_weights, axis=2)
        summed = jnp.einsum(
            "phks,khd->pshd",
            prefix_weights.astype(jnp.bfloat16),
            value_heads,
            preferred_element_type=jnp.float32,
        )
        pieces.append(
            jnp.concatenate(
                [
                    summed.reshape(chunk_pages, slot_count, local_width),
                    jnp.transpose(weight_sum, (0, 2, 1)),
                ],
                axis=2,
            ).astype(jnp.bfloat16)
        )
    prefix_parts = lax.all_to_all(
        jnp.concatenate(pieces, axis=0).reshape(pages_count * slot_count, local_width + local_heads),
        "pages",
        0,
        0,
        tiled=True,
    )
    prefix_both = jnp.sum(
        prefix_parts.reshape(pages_count, slot_count, local_width + local_heads).astype(jnp.float32),
        axis=0,
    )
    prefix_sum = prefix_both[:, :local_width]
    prefix_total = prefix_both[:, local_width:]
    denominator = suffix_total.T + prefix_total + (1.0 - live_shard.astype(jnp.float32))[:, None]
    mixed = (suffix_sum + prefix_sum.reshape(slot_count, local_heads, head_dim)) / denominator[
        :, :, None
    ]
    attention_local = mixed.reshape(slot_count, local_width).astype(jnp.bfloat16)
    projected_out = jnp.dot(
        attention_local,
        lax.dynamic_slice_in_dim(w_out, mp_index * local_width, local_width, 0),
        preferred_element_type=jnp.float32,
    )
    for shift in range(1, mp_count):
        arrived = lax.ppermute(
            attention_local,
            "mp",
            [(source, (source + shift) % mp_count) for source in range(mp_count)],
        )
        origin = (mp_index + mp_count - shift) % mp_count
        projected_out = projected_out + jnp.dot(
            arrived,
            lax.dynamic_slice_in_dim(w_out, origin * local_width, local_width, 0),
            preferred_element_type=jnp.float32,
        )
    residual_in = state_in.astype(jnp.float32)
    state_mid = rms_rows(
        residual_in + eigen_rates[0][None, :] * (rms_rows(projected_out) - residual_in)
    ).astype(jnp.bfloat16)
    state_own = lax.dynamic_slice_in_dim(state_mid, row_first, own_rows, 0)
    gate_up = jnp.einsum("sd,jdf->jsf", state_mid, w_gate_up, preferred_element_type=jnp.float32)
    hidden = (
        jax.nn.silu(scale_gate_up[0][None, :] * gate_up[0])
        * (scale_gate_up[1][None, :] * gate_up[1])
    ).astype(jnp.bfloat16)
    feed_parts = lax.all_to_all(
        jnp.dot(hidden, w_down, preferred_element_type=jnp.float32).astype(jnp.bfloat16),
        "mp",
        0,
        0,
        tiled=True,
    )
    feed_sum = jnp.sum(
        feed_parts.reshape(mp_count, own_rows, model_width).astype(jnp.float32), axis=0
    )
    middle = state_own.astype(jnp.float32)
    result = rms_rows(middle + eigen_rates[1][None, :] * (rms_rows(feed_sum) - middle))
    return (live_own.astype(jnp.float32)[:, None] * result).astype(jnp.bfloat16)


def solution(mesh):
    shards = shards_heads if HEADS % mesh.shape["mp"] == 0 else shards_columns
    return jax.shard_map(
        shards,
        mesh=mesh,
        in_specs=(
            P("pages", None),
            P(None, None, "mp"),
            P(),
            P(None, None, "mp"),
            P("mp", None),
            P(),
            P(None, "mp"),
            P(),
            P("pages", None, None),
            P("pages", None, None),
            P(),
            P(),
            P(),
        ),
        out_specs=P(("pages", "mp"), None),
        check_vma=False,
    )
```

```python
import math

import jax
import jax.numpy as jnp
from jax import lax
from jax.sharding import PartitionSpec as P

HEADS = 20
GROUPS = 8


EPSILON = 1e-06


def rms_rows(values_in):
    return values_in * lax.rsqrt(jnp.mean(values_in * values_in, axis=-1, keepdims=True) + EPSILON)


def head_norm(values_in, scale_vec, head_count):
    row_count, model_width = values_in.shape
    per_head = values_in.reshape(row_count, head_count, model_width // head_count)
    normed = per_head * lax.rsqrt(jnp.mean(per_head * per_head, axis=-1, keepdims=True) + EPSILON)
    return normed.reshape(row_count, model_width) * scale_vec[None, :]


def rotate(values_in, position, head_count):
    row_count, model_width = values_in.shape
    head_dim = model_width // head_count
    half_dim = head_dim // 2
    frequency = jnp.exp(
        jnp.arange(half_dim).astype(jnp.float32) * (-2.0 * math.log(10000.0) / head_dim)
    )
    rotation = position.astype(jnp.float32)[:, None] * frequency[None, :]
    cosine_table = jnp.cos(rotation)[:, None, :]
    sine_table = jnp.sin(rotation)[:, None, :]
    per_head = values_in.reshape(row_count, head_count, head_dim)
    lower_half = per_head[:, :, :half_dim]
    upper_half = per_head[:, :, half_dim:]
    turned = jnp.concatenate(
        [
            lower_half * cosine_table - upper_half * sine_table,
            upper_half * cosine_table + lower_half * sine_table,
        ],
        axis=-1,
    )
    return turned.reshape(row_count, model_width)


def slot_tables(suffix_len, request_group, slot_count):
    end_slots = jnp.cumsum(suffix_len, axis=1)
    start_slots = end_slots - suffix_len
    slot_ids = jnp.arange(slot_count)
    inside = (slot_ids[None, None, :] >= start_slots[:, :, None]) & (
        slot_ids[None, None, :] < end_slots[:, :, None]
    )
    request_ids = jnp.arange(suffix_len.shape[1])
    slot_valid = jnp.any(inside, axis=1)
    request = jnp.sum(jnp.where(inside, request_ids[None, :, None], 0), axis=1)
    offset = slot_ids[None, :] - jnp.sum(jnp.where(inside, start_slots[:, :, None], 0), axis=1)
    group_id = jnp.where(
        slot_valid, jnp.sum(jnp.where(inside, request_group[:, :, None], 0), axis=1), -1
    )
    return (slot_valid, request, offset, group_id)


def prefix_block(query_block, group_block, prefix_keys, prefix_values, key_group, score_scale):
    row_count, model_width = query_block.shape
    head_dim = model_width // HEADS
    query_heads = query_block.reshape(row_count, HEADS, head_dim)
    key_heads = prefix_keys.reshape(-1, HEADS, head_dim)
    value_heads = prefix_values.reshape(-1, HEADS, head_dim)
    scores = (
        jnp.einsum("qhd,khd->qhk", query_heads, key_heads, preferred_element_type=jnp.float32)
        * score_scale
    )
    allowed = group_block[:, None] == key_group[None, :]
    weights = jnp.where(allowed[:, None, :], jnp.exp(scores), 0.0)
    weight_sum = jnp.sum(weights, axis=-1)
    summed = jnp.einsum(
        "qhk,khd->qhd",
        weights.astype(jnp.bfloat16),
        value_heads,
        preferred_element_type=jnp.float32,
    )
    return (summed.reshape(row_count, model_width), weight_sum)


def shards_columns(
    hidden_in,
    w_qkv,
    w_out,
    w_gate_up,
    w_down,
    scale_qk,
    scale_gate_up,
    eigen_rates,
    cache_keys,
    cache_values,
    page_table,
    request_group,
    suffix_len,
):
    slot_count, model_width = hidden_in.shape
    head_dim = model_width // HEADS
    score_scale = 1.0 / math.sqrt(head_dim)
    mp_count = lax.axis_size("mp")
    mp_index = lax.axis_index("mp")
    own_rows = slot_count // mp_count
    row_first = mp_index * own_rows
    shard_index = lax.axis_index("pages")
    pages_here, page_len = (cache_keys.shape[0], cache_keys.shape[1])
    pool_pages = page_table.shape[0]
    prefix_pages = pool_pages // GROUPS
    slot_valid, request, offset, group_id = slot_tables(suffix_len, request_group, slot_count)
    live_shard = lax.dynamic_index_in_dim(slot_valid, shard_index, 0, keepdims=False)
    request_shard = lax.dynamic_index_in_dim(request, shard_index, 0, keepdims=False)
    offset_shard = lax.dynamic_index_in_dim(offset, shard_index, 0, keepdims=False)
    position_shard = prefix_pages * page_len + offset_shard
    live_own = lax.dynamic_slice_in_dim(live_shard, row_first, own_rows, 0)
    request_own = lax.dynamic_slice_in_dim(request_shard, row_first, own_rows, 0)
    offset_own = lax.dynamic_slice_in_dim(offset_shard, row_first, own_rows, 0)
    position_own = lax.dynamic_slice_in_dim(position_shard, row_first, own_rows, 0)
    state_in = rms_rows(hidden_in.astype(jnp.float32)).astype(jnp.bfloat16)
    projected = jnp.einsum(
        "sd,jdc->jsc", state_in, w_qkv, preferred_element_type=jnp.float32
    ).astype(jnp.bfloat16)
    columns = lax.all_gather(projected, "mp", axis=2, tiled=True)
    query_raw = lax.dynamic_slice_in_dim(columns[0], row_first, own_rows, 0)
    key_raw, value_rows = (columns[1], columns[2])
    queries = head_norm(
        rotate(query_raw.astype(jnp.float32), position_own, HEADS), scale_qk, HEADS
    ).astype(jnp.bfloat16)
    keys_new = head_norm(
        rotate(key_raw.astype(jnp.float32), position_shard, HEADS), scale_qk, HEADS
    ).astype(jnp.bfloat16)
    query_heads = queries.reshape(own_rows, HEADS, head_dim)
    scores = (
        jnp.einsum(
            "qhd,khd->hqk",
            query_heads,
            keys_new.reshape(slot_count, HEADS, head_dim),
            preferred_element_type=jnp.float32,
        )
        * score_scale
    )
    allowed = (
        (request_own[:, None] == request_shard[None, :])
        & (offset_shard[None, :] <= offset_own[:, None])
        & live_own[:, None]
        & live_shard[None, :]
    )
    weights = jnp.where(allowed[None], jnp.exp(scores), 0.0)
    suffix_total = jnp.sum(weights, axis=-1)
    suffix_sum = jnp.einsum(
        "hqk,khd->qhd",
        weights.astype(jnp.bfloat16),
        value_rows.reshape(slot_count, HEADS, head_dim),
        preferred_element_type=jnp.float32,
    )
    physical = shard_index * pages_here + jnp.arange(pages_here, dtype=jnp.int32)
    matches = page_table[:, None] == physical[None, :]
    logical = jnp.sum(
        jnp.where(matches, jnp.arange(pool_pages, dtype=jnp.int32)[:, None], 0), axis=0
    )
    key_group = jnp.repeat(logical // prefix_pages, page_len)
    prefix_keys = head_norm(
        cache_keys.reshape(pages_here * page_len, model_width).astype(jnp.float32), scale_qk, HEADS
    ).astype(jnp.bfloat16)
    prefix_values = cache_values.reshape(pages_here * page_len, model_width)
    gathered = lax.all_gather(queries, "pages", axis=0, tiled=True)
    gathered_group = lax.dynamic_slice_in_dim(group_id, row_first, own_rows, 1).reshape(-1)
    row_count = own_rows * lax.axis_size("pages")
    block_rows = row_count if row_count <= 512 else math.gcd(row_count, 512)

    def attend_block(block_first):
        query_block = lax.dynamic_slice_in_dim(gathered, block_first, block_rows, 0)
        group_block = lax.dynamic_slice_in_dim(gathered_group, block_first, block_rows, 0)
        return prefix_block(
            query_block, group_block, prefix_keys, prefix_values, key_group, score_scale
        )

    block_starts = jnp.arange(row_count // block_rows, dtype=jnp.int32) * block_rows
    summed, weight_sum = lax.map(attend_block, block_starts)
    prefix_sum, prefix_total = lax.psum_scatter(
        (summed.reshape(row_count, model_width), weight_sum.reshape(row_count, HEADS)),
        "pages",
        scatter_dimension=0,
        tiled=True,
    )
    denominator = suffix_total.T + prefix_total + (1.0 - live_own.astype(jnp.float32))[:, None]
    mixed = (suffix_sum + prefix_sum.reshape(own_rows, HEADS, head_dim)) / denominator[:, :, None]
    attention = mixed.reshape(own_rows, model_width).astype(jnp.bfloat16)
    projected_out = jnp.dot(
        lax.all_gather(attention, "mp", axis=0, tiled=True),
        w_out,
        preferred_element_type=jnp.float32,
    )
    residual_in = state_in.astype(jnp.float32)
    state_mid = rms_rows(
        residual_in + eigen_rates[0][None, :] * (rms_rows(projected_out) - residual_in)
    ).astype(jnp.bfloat16)
    state_own = lax.dynamic_slice_in_dim(state_mid, row_first, own_rows, 0)
    gate_up = jnp.einsum("sd,jdf->jsf", state_mid, w_gate_up, preferred_element_type=jnp.float32)
    hidden = (
        jax.nn.silu(scale_gate_up[0][None, :] * gate_up[0])
        * (scale_gate_up[1][None, :] * gate_up[1])
    ).astype(jnp.bfloat16)
    feed_sum = lax.psum_scatter(
        jnp.dot(hidden, w_down, preferred_element_type=jnp.float32),
        "mp",
        scatter_dimension=0,
        tiled=True,
    )
    middle = state_own.astype(jnp.float32)
    result = rms_rows(middle + eigen_rates[1][None, :] * (rms_rows(feed_sum) - middle))
    return (live_own.astype(jnp.float32)[:, None] * result).astype(jnp.bfloat16)


def shards_heads(
    hidden_in,
    w_qkv,
    w_out,
    w_gate_up,
    w_down,
    scale_qk,
    scale_gate_up,
    eigen_rates,
    cache_keys,
    cache_values,
    page_table,
    request_group,
    suffix_len,
):
    slot_count, model_width = hidden_in.shape
    head_dim = model_width // HEADS
    score_scale = 1.0 / math.sqrt(head_dim)
    mp_count = lax.axis_size("mp")
    mp_index = lax.axis_index("mp")
    local_heads = HEADS // mp_count
    local_width = local_heads * head_dim
    own_rows = slot_count // mp_count
    row_first = mp_index * own_rows
    shard_index = lax.axis_index("pages")
    pages_here, page_len = (cache_keys.shape[0], cache_keys.shape[1])
    pool_pages = page_table.shape[0]
    prefix_pages = pool_pages // GROUPS
    slot_valid, request, offset, group_id = slot_tables(suffix_len, request_group, slot_count)
    live_shard = lax.dynamic_index_in_dim(slot_valid, shard_index, 0, keepdims=False)
    request_shard = lax.dynamic_index_in_dim(request, shard_index, 0, keepdims=False)
    offset_shard = lax.dynamic_index_in_dim(offset, shard_index, 0, keepdims=False)
    position_shard = prefix_pages * page_len + offset_shard
    live_own = lax.dynamic_slice_in_dim(live_shard, row_first, own_rows, 0)
    scale_local = lax.dynamic_slice_in_dim(scale_qk, mp_index * local_width, local_width, 0)
    state_in = rms_rows(hidden_in.astype(jnp.float32)).astype(jnp.bfloat16)
    projected = jnp.einsum(
        "sd,jdc->jsc", state_in, w_qkv, preferred_element_type=jnp.float32
    ).astype(jnp.bfloat16)
    queries = head_norm(
        rotate(projected[0].astype(jnp.float32), position_shard, local_heads), scale_local, local_heads
    ).astype(jnp.bfloat16)
    keys_new = head_norm(
        rotate(projected[1].astype(jnp.float32), position_shard, local_heads), scale_local, local_heads
    ).astype(jnp.bfloat16)
    value_rows = projected[2]
    gathered = lax.all_to_all(
        jnp.tile(queries, (lax.axis_size("pages"), 1)), "pages", 0, 0, tiled=True
    )
    scores = (
        jnp.einsum(
            "qhd,khd->hqk",
            queries.reshape(slot_count, local_heads, head_dim),
            keys_new.reshape(slot_count, local_heads, head_dim),
            preferred_element_type=jnp.float32,
        )
        * score_scale
    )
    allowed = (
        (request_shard[:, None] == request_shard[None, :])
        & (offset_shard[None, :] <= offset_shard[:, None])
        & live_shard[:, None]
        & live_shard[None, :]
    )
    weights = jnp.where(allowed[None], jnp.exp(scores), 0.0)
    suffix_total = jnp.sum(weights, axis=-1)
    suffix_sum = jnp.einsum(
        "hqk,khd->qhd",
        weights.astype(jnp.bfloat16),
        value_rows.reshape(slot_count, local_heads, head_dim),
        preferred_element_type=jnp.float32,
    )
    physical = shard_index * pages_here + jnp.arange(pages_here, dtype=jnp.int32)
    matches = page_table[:, None] == physical[None, :]
    logical = jnp.sum(
        jnp.where(matches, jnp.arange(pool_pages, dtype=jnp.int32)[:, None], 0), axis=0
    )
    key_group = jnp.repeat(logical // prefix_pages, page_len)
    cache_local = lax.dynamic_slice_in_dim(cache_keys, mp_index * local_width, local_width, 2)
    prefix_keys = head_norm(
        cache_local.reshape(pages_here * page_len, local_width).astype(jnp.float32),
        scale_local,
        local_heads,
    ).astype(jnp.bfloat16)
    prefix_values = lax.dynamic_slice_in_dim(
        cache_values, mp_index * local_width, local_width, 2
    ).reshape(pages_here * page_len, local_width)
    pages_count = lax.axis_size("pages")
    key_heads = prefix_keys.reshape(-1, local_heads, head_dim)
    value_heads = prefix_values.reshape(-1, local_heads, head_dim)
    gathered_heads = gathered.reshape(pages_count, slot_count, local_heads, head_dim)
    chunk_count = 1
    chunk_pages = pages_count // chunk_count
    pieces = []
    for chunk in range(chunk_count):
        query_chunk = lax.slice_in_dim(
            gathered_heads, chunk * chunk_pages, (chunk + 1) * chunk_pages, axis=0
        )
        group_chunk = lax.slice_in_dim(
            group_id, chunk * chunk_pages, (chunk + 1) * chunk_pages, axis=0
        )
        prefix_scores = (
            jnp.einsum(
                "pshd,khd->phks", query_chunk, key_heads, preferred_element_type=jnp.float32
            )
            * score_scale
        )
        prefix_allowed = key_group[None, :, None] == group_chunk[:, None, :]
        prefix_weights = jnp.where(prefix_allowed[:, None], jnp.exp(prefix_scores), 0.0)
        weight_sum = jnp.sum(prefix_weights, axis=2)
        summed = jnp.einsum(
            "phks,khd->pshd",
            prefix_weights.astype(jnp.bfloat16),
            value_heads,
            preferred_element_type=jnp.float32,
        )
        pieces.append(
            jnp.concatenate(
                [
                    summed.reshape(chunk_pages, slot_count, local_width),
                    jnp.transpose(weight_sum, (0, 2, 1)),
                ],
                axis=2,
            ).astype(jnp.bfloat16)
        )
    prefix_parts = lax.all_to_all(
        jnp.concatenate(pieces, axis=0).reshape(pages_count * slot_count, local_width + local_heads),
        "pages",
        0,
        0,
        tiled=True,
    )
    prefix_both = jnp.sum(
        prefix_parts.reshape(pages_count, slot_count, local_width + local_heads).astype(jnp.float32),
        axis=0,
    )
    prefix_sum = prefix_both[:, :local_width]
    prefix_total = prefix_both[:, local_width:]
    denominator = suffix_total.T + prefix_total + (1.0 - live_shard.astype(jnp.float32))[:, None]
    mixed = (suffix_sum + prefix_sum.reshape(slot_count, local_heads, head_dim)) / denominator[
        :, :, None
    ]
    attention_local = mixed.reshape(slot_count, local_width).astype(jnp.bfloat16)
    attention = lax.all_gather(attention_local, "mp", axis=1, tiled=True)
    projected_out = jnp.dot(attention, w_out, preferred_element_type=jnp.float32)
    residual_in = state_in.astype(jnp.float32)
    state_mid = rms_rows(
        residual_in + eigen_rates[0][None, :] * (rms_rows(projected_out) - residual_in)
    ).astype(jnp.bfloat16)
    state_own = lax.dynamic_slice_in_dim(state_mid, row_first, own_rows, 0)
    gate_up = jnp.einsum("sd,jdf->jsf", state_mid, w_gate_up, preferred_element_type=jnp.float32)
    hidden = (
        jax.nn.silu(scale_gate_up[0][None, :] * gate_up[0])
        * (scale_gate_up[1][None, :] * gate_up[1])
    ).astype(jnp.bfloat16)
    feed_parts = lax.all_to_all(
        jnp.dot(hidden, w_down, preferred_element_type=jnp.float32).astype(jnp.bfloat16),
        "mp",
        0,
        0,
        tiled=True,
    )
    feed_sum = jnp.sum(
        feed_parts.reshape(mp_count, own_rows, model_width).astype(jnp.float32), axis=0
    )
    middle = state_own.astype(jnp.float32)
    result = rms_rows(middle + eigen_rates[1][None, :] * (rms_rows(feed_sum) - middle))
    return (live_own.astype(jnp.float32)[:, None] * result).astype(jnp.bfloat16)


def solution(mesh):
    shards = shards_heads if HEADS % mesh.shape["mp"] == 0 else shards_columns
    return jax.shard_map(
        shards,
        mesh=mesh,
        in_specs=(
            P("pages", None),
            P(None, None, "mp"),
            P(),
            P(None, None, "mp"),
            P("mp", None),
            P(),
            P(None, "mp"),
            P(),
            P("pages", None, None),
            P("pages", None, None),
            P(),
            P(),
            P(),
        ),
        out_specs=P(("pages", "mp"), None),
        check_vma=False,
    )
```

```python
import math

import jax
import jax.numpy as jnp
from jax import lax
from jax.sharding import PartitionSpec as P

HEADS = 20
GROUPS = 8


EPSILON = 1e-06


def rms_rows(values_in):
    return values_in * lax.rsqrt(jnp.mean(values_in * values_in, axis=-1, keepdims=True) + EPSILON)


def head_norm(values_in, scale_vec, head_count):
    row_count, model_width = values_in.shape
    per_head = values_in.reshape(row_count, head_count, model_width // head_count)
    normed = per_head * lax.rsqrt(jnp.mean(per_head * per_head, axis=-1, keepdims=True) + EPSILON)
    return normed.reshape(row_count, model_width) * scale_vec[None, :]


def rotate(values_in, position, head_count):
    row_count, model_width = values_in.shape
    head_dim = model_width // head_count
    half_dim = head_dim // 2
    frequency = jnp.exp(
        jnp.arange(half_dim).astype(jnp.float32) * (-2.0 * math.log(10000.0) / head_dim)
    )
    rotation = position.astype(jnp.float32)[:, None] * frequency[None, :]
    cosine_table = jnp.cos(rotation)[:, None, :]
    sine_table = jnp.sin(rotation)[:, None, :]
    per_head = values_in.reshape(row_count, head_count, head_dim)
    lower_half = per_head[:, :, :half_dim]
    upper_half = per_head[:, :, half_dim:]
    turned = jnp.concatenate(
        [
            lower_half * cosine_table - upper_half * sine_table,
            upper_half * cosine_table + lower_half * sine_table,
        ],
        axis=-1,
    )
    return turned.reshape(row_count, model_width)


def slot_tables(suffix_len, request_group, slot_count):
    running = [suffix_len[:, 0]]
    for column in range(1, suffix_len.shape[1]):
        running.append(running[-1] + suffix_len[:, column])
    end_slots = jnp.stack(running, axis=1)
    start_slots = end_slots - suffix_len
    slot_ids = jnp.arange(slot_count)
    inside = (slot_ids[None, None, :] >= start_slots[:, :, None]) & (
        slot_ids[None, None, :] < end_slots[:, :, None]
    )
    request_ids = jnp.arange(suffix_len.shape[1])
    slot_valid = jnp.any(inside, axis=1)
    request = jnp.sum(jnp.where(inside, request_ids[None, :, None], 0), axis=1)
    offset = slot_ids[None, :] - jnp.sum(jnp.where(inside, start_slots[:, :, None], 0), axis=1)
    group_id = jnp.where(
        slot_valid, jnp.sum(jnp.where(inside, request_group[:, :, None], 0), axis=1), -1
    )
    return (slot_valid, request, offset, group_id)


def prefix_block(query_block, group_block, prefix_keys, prefix_values, key_group, score_scale):
    row_count, model_width = query_block.shape
    head_dim = model_width // HEADS
    query_heads = query_block.reshape(row_count, HEADS, head_dim)
    key_heads = prefix_keys.reshape(-1, HEADS, head_dim)
    value_heads = prefix_values.reshape(-1, HEADS, head_dim)
    scores = (
        jnp.einsum("qhd,khd->qhk", query_heads, key_heads, preferred_element_type=jnp.float32)
        * score_scale
    )
    allowed = group_block[:, None] == key_group[None, :]
    weights = jnp.where(allowed[:, None, :], jnp.exp(scores), 0.0)
    weight_sum = jnp.sum(weights, axis=-1)
    summed = jnp.einsum(
        "qhk,khd->qhd",
        weights.astype(jnp.bfloat16),
        value_heads,
        preferred_element_type=jnp.float32,
    )
    return (summed.reshape(row_count, model_width), weight_sum)


def shards_columns(
    hidden_in,
    w_qkv,
    w_out,
    w_gate_up,
    w_down,
    scale_qk,
    scale_gate_up,
    eigen_rates,
    cache_keys,
    cache_values,
    page_table,
    request_group,
    suffix_len,
):
    slot_count, model_width = hidden_in.shape
    head_dim = model_width // HEADS
    score_scale = 1.0 / math.sqrt(head_dim)
    mp_count = lax.axis_size("mp")
    mp_index = lax.axis_index("mp")
    own_rows = slot_count // mp_count
    row_first = mp_index * own_rows
    shard_index = lax.axis_index("pages")
    pages_here, page_len = (cache_keys.shape[0], cache_keys.shape[1])
    pool_pages = page_table.shape[0]
    prefix_pages = pool_pages // GROUPS
    slot_valid, request, offset, group_id = slot_tables(suffix_len, request_group, slot_count)
    live_shard = lax.dynamic_index_in_dim(slot_valid, shard_index, 0, keepdims=False)
    request_shard = lax.dynamic_index_in_dim(request, shard_index, 0, keepdims=False)
    offset_shard = lax.dynamic_index_in_dim(offset, shard_index, 0, keepdims=False)
    position_shard = prefix_pages * page_len + offset_shard
    live_own = lax.dynamic_slice_in_dim(live_shard, row_first, own_rows, 0)
    request_own = lax.dynamic_slice_in_dim(request_shard, row_first, own_rows, 0)
    offset_own = lax.dynamic_slice_in_dim(offset_shard, row_first, own_rows, 0)
    position_own = lax.dynamic_slice_in_dim(position_shard, row_first, own_rows, 0)
    state_in = rms_rows(hidden_in.astype(jnp.float32)).astype(jnp.bfloat16)
    projected = jnp.einsum(
        "sd,jdc->jsc", state_in, w_qkv, preferred_element_type=jnp.float32
    ).astype(jnp.bfloat16)
    columns = lax.all_gather(projected, "mp", axis=2, tiled=True)
    query_raw = lax.dynamic_slice_in_dim(columns[0], row_first, own_rows, 0)
    key_raw, value_rows = (columns[1], columns[2])
    queries = head_norm(
        rotate(query_raw.astype(jnp.float32), position_own, HEADS), scale_qk, HEADS
    ).astype(jnp.bfloat16)
    keys_new = head_norm(
        rotate(key_raw.astype(jnp.float32), position_shard, HEADS), scale_qk, HEADS
    ).astype(jnp.bfloat16)
    query_heads = queries.reshape(own_rows, HEADS, head_dim)
    scores = (
        jnp.einsum(
            "qhd,khd->hqk",
            query_heads,
            keys_new.reshape(slot_count, HEADS, head_dim),
            preferred_element_type=jnp.float32,
        )
        * score_scale
    )
    allowed = (
        (request_own[:, None] == request_shard[None, :])
        & (offset_shard[None, :] <= offset_own[:, None])
        & live_own[:, None]
        & live_shard[None, :]
    )
    weights = jnp.where(allowed[None], jnp.exp(scores), 0.0)
    suffix_total = jnp.sum(weights, axis=-1)
    suffix_sum = jnp.einsum(
        "hqk,khd->qhd",
        weights.astype(jnp.bfloat16),
        value_rows.reshape(slot_count, HEADS, head_dim),
        preferred_element_type=jnp.float32,
    )
    physical = shard_index * pages_here + jnp.arange(pages_here, dtype=jnp.int32)
    matches = page_table[:, None] == physical[None, :]
    logical = jnp.sum(
        jnp.where(matches, jnp.arange(pool_pages, dtype=jnp.int32)[:, None], 0), axis=0
    )
    key_group = jnp.repeat(logical // prefix_pages, page_len)
    prefix_keys = head_norm(
        cache_keys.reshape(pages_here * page_len, model_width).astype(jnp.float32), scale_qk, HEADS
    ).astype(jnp.bfloat16)
    prefix_values = cache_values.reshape(pages_here * page_len, model_width)
    gathered = lax.all_gather(queries, "pages", axis=0, tiled=True)
    gathered_group = lax.dynamic_slice_in_dim(group_id, row_first, own_rows, 1).reshape(-1)
    row_count = own_rows * lax.axis_size("pages")
    block_rows = row_count if row_count <= 512 else math.gcd(row_count, 512)

    def attend_block(block_first):
        query_block = lax.dynamic_slice_in_dim(gathered, block_first, block_rows, 0)
        group_block = lax.dynamic_slice_in_dim(gathered_group, block_first, block_rows, 0)
        return prefix_block(
            query_block, group_block, prefix_keys, prefix_values, key_group, score_scale
        )

    block_starts = jnp.arange(row_count // block_rows, dtype=jnp.int32) * block_rows
    summed, weight_sum = lax.map(attend_block, block_starts)
    prefix_sum, prefix_total = lax.psum_scatter(
        (summed.reshape(row_count, model_width), weight_sum.reshape(row_count, HEADS)),
        "pages",
        scatter_dimension=0,
        tiled=True,
    )
    denominator = suffix_total.T + prefix_total + (1.0 - live_own.astype(jnp.float32))[:, None]
    mixed = (suffix_sum + prefix_sum.reshape(own_rows, HEADS, head_dim)) / denominator[:, :, None]
    attention = mixed.reshape(own_rows, model_width).astype(jnp.bfloat16)
    projected_out = jnp.dot(
        lax.all_gather(attention, "mp", axis=0, tiled=True),
        w_out,
        preferred_element_type=jnp.float32,
    )
    residual_in = state_in.astype(jnp.float32)
    state_mid = rms_rows(
        residual_in + eigen_rates[0][None, :] * (rms_rows(projected_out) - residual_in)
    ).astype(jnp.bfloat16)
    state_own = lax.dynamic_slice_in_dim(state_mid, row_first, own_rows, 0)
    gate_up = jnp.einsum("sd,jdf->jsf", state_mid, w_gate_up, preferred_element_type=jnp.float32)
    hidden = (
        jax.nn.silu(scale_gate_up[0][None, :] * gate_up[0])
        * (scale_gate_up[1][None, :] * gate_up[1])
    ).astype(jnp.bfloat16)
    feed_sum = lax.psum_scatter(
        jnp.dot(hidden, w_down, preferred_element_type=jnp.float32),
        "mp",
        scatter_dimension=0,
        tiled=True,
    )
    middle = state_own.astype(jnp.float32)
    result = rms_rows(middle + eigen_rates[1][None, :] * (rms_rows(feed_sum) - middle))
    return (live_own.astype(jnp.float32)[:, None] * result).astype(jnp.bfloat16)


def shards_heads(
    hidden_in,
    w_qkv,
    w_out,
    w_gate_up,
    w_down,
    scale_qk,
    scale_gate_up,
    eigen_rates,
    cache_keys,
    cache_values,
    page_table,
    request_group,
    suffix_len,
):
    slot_count, model_width = hidden_in.shape
    head_dim = model_width // HEADS
    score_scale = 1.0 / math.sqrt(head_dim)
    mp_count = lax.axis_size("mp")
    mp_index = lax.axis_index("mp")
    local_heads = HEADS // mp_count
    local_width = local_heads * head_dim
    own_rows = slot_count // mp_count
    row_first = mp_index * own_rows
    shard_index = lax.axis_index("pages")
    pages_here, page_len = (cache_keys.shape[0], cache_keys.shape[1])
    pool_pages = page_table.shape[0]
    prefix_pages = pool_pages // GROUPS
    slot_valid, request, offset, group_id = slot_tables(suffix_len, request_group, slot_count)
    live_shard = lax.dynamic_index_in_dim(slot_valid, shard_index, 0, keepdims=False)
    request_shard = lax.dynamic_index_in_dim(request, shard_index, 0, keepdims=False)
    offset_shard = lax.dynamic_index_in_dim(offset, shard_index, 0, keepdims=False)
    position_shard = prefix_pages * page_len + offset_shard
    live_own = lax.dynamic_slice_in_dim(live_shard, row_first, own_rows, 0)
    scale_local = lax.dynamic_slice_in_dim(scale_qk, mp_index * local_width, local_width, 0)
    state_in = rms_rows(hidden_in.astype(jnp.float32)).astype(jnp.bfloat16)
    projected_query = jnp.dot(state_in, w_qkv[0], preferred_element_type=jnp.float32).astype(
        jnp.bfloat16
    )
    queries = head_norm(
        rotate(projected_query.astype(jnp.float32), position_shard, local_heads),
        scale_local,
        local_heads,
    ).astype(jnp.bfloat16)
    gathered = lax.all_to_all(
        jnp.tile(queries, (lax.axis_size("pages"), 1)), "pages", 0, 0, tiled=True
    )
    state_kv = state_in + jnp.zeros_like(state_in) * gathered[0, 0]
    projected = jnp.einsum(
        "sd,jdc->jsc", state_kv, w_qkv[1:], preferred_element_type=jnp.float32
    ).astype(jnp.bfloat16)
    keys_new = head_norm(
        rotate(projected[0].astype(jnp.float32), position_shard, local_heads), scale_local, local_heads
    ).astype(jnp.bfloat16)
    value_rows = projected[1]
    scores = (
        jnp.einsum(
            "qhd,khd->hqk",
            queries.reshape(slot_count, local_heads, head_dim),
            keys_new.reshape(slot_count, local_heads, head_dim),
            preferred_element_type=jnp.float32,
        )
        * score_scale
    )
    allowed = (
        (request_shard[:, None] == request_shard[None, :])
        & (offset_shard[None, :] <= offset_shard[:, None])
        & live_shard[:, None]
        & live_shard[None, :]
    )
    weights = jnp.where(allowed[None], jnp.exp(scores), 0.0)
    suffix_total = jnp.sum(weights, axis=-1)
    suffix_sum = jnp.einsum(
        "hqk,khd->qhd",
        weights.astype(jnp.bfloat16),
        value_rows.reshape(slot_count, local_heads, head_dim),
        preferred_element_type=jnp.float32,
    )
    physical = shard_index * pages_here + jnp.arange(pages_here, dtype=jnp.int32)
    matches = page_table[:, None] == physical[None, :]
    logical = jnp.sum(
        jnp.where(matches, jnp.arange(pool_pages, dtype=jnp.int32)[:, None], 0), axis=0
    )
    key_group = jnp.repeat(logical // prefix_pages, page_len)
    cache_local = lax.dynamic_slice_in_dim(cache_keys, mp_index * local_width, local_width, 2)
    prefix_keys = head_norm(
        cache_local.reshape(pages_here * page_len, local_width).astype(jnp.float32),
        scale_local,
        local_heads,
    ).astype(jnp.bfloat16)
    prefix_values = lax.dynamic_slice_in_dim(
        cache_values, mp_index * local_width, local_width, 2
    ).reshape(pages_here * page_len, local_width)
    pages_count = lax.axis_size("pages")
    key_heads = prefix_keys.reshape(-1, local_heads, head_dim)
    value_heads = prefix_values.reshape(-1, local_heads, head_dim)
    gathered_heads = gathered.reshape(pages_count, slot_count, local_heads, head_dim)
    chunk_count = 2 if pages_count % 2 == 0 else 1
    chunk_pages = pages_count // chunk_count
    pieces = []
    for chunk in range(chunk_count):
        query_chunk = lax.slice_in_dim(
            gathered_heads, chunk * chunk_pages, (chunk + 1) * chunk_pages, axis=0
        )
        group_chunk = lax.slice_in_dim(
            group_id, chunk * chunk_pages, (chunk + 1) * chunk_pages, axis=0
        )
        prefix_scores = (
            jnp.einsum(
                "pshd,khd->phks", query_chunk, key_heads, preferred_element_type=jnp.float32
            )
            * score_scale
        )
        prefix_allowed = key_group[None, :, None] == group_chunk[:, None, :]
        prefix_weights = jnp.where(prefix_allowed[:, None], jnp.exp(prefix_scores), 0.0)
        weight_sum = jnp.sum(prefix_weights, axis=2)
        summed = jnp.einsum(
            "phks,khd->pshd",
            prefix_weights.astype(jnp.bfloat16),
            value_heads,
            preferred_element_type=jnp.float32,
        )
        pieces.append(
            jnp.concatenate(
                [
                    summed.reshape(chunk_pages, slot_count, local_width),
                    jnp.transpose(weight_sum, (0, 2, 1)),
                ],
                axis=2,
            ).astype(jnp.bfloat16)
        )
    prefix_parts = lax.all_to_all(
        jnp.concatenate(pieces, axis=0).reshape(pages_count * slot_count, local_width + local_heads),
        "pages",
        0,
        0,
        tiled=True,
    )
    prefix_both = jnp.sum(
        prefix_parts.reshape(pages_count, slot_count, local_width + local_heads).astype(jnp.float32),
        axis=0,
    )
    prefix_sum = prefix_both[:, :local_width]
    prefix_total = prefix_both[:, local_width:]
    denominator = suffix_total.T + prefix_total + (1.0 - live_shard.astype(jnp.float32))[:, None]
    mixed = (suffix_sum + prefix_sum.reshape(slot_count, local_heads, head_dim)) / denominator[
        :, :, None
    ]
    attention_local = mixed.reshape(slot_count, local_width).astype(jnp.bfloat16)
    attention = lax.all_gather(attention_local, "mp", axis=1, tiled=True)
    projected_out = jnp.dot(attention, w_out, preferred_element_type=jnp.float32)
    residual_in = state_in.astype(jnp.float32)
    state_mid = rms_rows(
        residual_in + eigen_rates[0][None, :] * (rms_rows(projected_out) - residual_in)
    ).astype(jnp.bfloat16)
    state_own = lax.dynamic_slice_in_dim(state_mid, row_first, own_rows, 0)
    gate_up = jnp.einsum("sd,jdf->jsf", state_mid, w_gate_up, preferred_element_type=jnp.float32)
    hidden = (
        jax.nn.silu(scale_gate_up[0][None, :] * gate_up[0])
        * (scale_gate_up[1][None, :] * gate_up[1])
    ).astype(jnp.bfloat16)
    feed_parts = lax.all_to_all(
        jnp.dot(hidden, w_down, preferred_element_type=jnp.float32).astype(jnp.bfloat16),
        "mp",
        0,
        0,
        tiled=True,
    )
    feed_sum = jnp.sum(
        feed_parts.reshape(mp_count, own_rows, model_width).astype(jnp.float32), axis=0
    )
    middle = state_own.astype(jnp.float32)
    result = rms_rows(middle + eigen_rates[1][None, :] * (rms_rows(feed_sum) - middle))
    return (live_own.astype(jnp.float32)[:, None] * result).astype(jnp.bfloat16)


def solution(mesh):
    shards = shards_heads if HEADS % mesh.shape["mp"] == 0 else shards_columns
    return jax.shard_map(
        shards,
        mesh=mesh,
        in_specs=(
            P("pages", None),
            P(None, None, "mp"),
            P(),
            P(None, None, "mp"),
            P("mp", None),
            P(),
            P(None, "mp"),
            P(),
            P("pages", None, None),
            P("pages", None, None),
            P(),
            P(),
            P(),
        ),
        out_specs=P(("pages", "mp"), None),
        check_vma=False,
    )
```

```python
import math

import jax
import jax.numpy as jnp
from jax import lax
from jax.sharding import PartitionSpec as P

HEADS = 20
GROUPS = 8


EPSILON = 1e-06


def rms_rows(values_in):
    return values_in * lax.rsqrt(jnp.mean(values_in * values_in, axis=-1, keepdims=True) + EPSILON)


def head_norm(values_in, scale_vec, head_count):
    row_count, model_width = values_in.shape
    per_head = values_in.reshape(row_count, head_count, model_width // head_count)
    normed = per_head * lax.rsqrt(jnp.mean(per_head * per_head, axis=-1, keepdims=True) + EPSILON)
    return normed.reshape(row_count, model_width) * scale_vec[None, :]


def rotate(values_in, position, head_count):
    row_count, model_width = values_in.shape
    head_dim = model_width // head_count
    half_dim = head_dim // 2
    frequency = jnp.exp(
        jnp.arange(half_dim).astype(jnp.float32) * (-2.0 * math.log(10000.0) / head_dim)
    )
    rotation = position.astype(jnp.float32)[:, None] * frequency[None, :]
    cosine_table = jnp.cos(rotation)[:, None, :]
    sine_table = jnp.sin(rotation)[:, None, :]
    per_head = values_in.reshape(row_count, head_count, head_dim)
    lower_half = per_head[:, :, :half_dim]
    upper_half = per_head[:, :, half_dim:]
    turned = jnp.concatenate(
        [
            lower_half * cosine_table - upper_half * sine_table,
            upper_half * cosine_table + lower_half * sine_table,
        ],
        axis=-1,
    )
    return turned.reshape(row_count, model_width)


def slot_tables(suffix_len, request_group, slot_count):
    running = [suffix_len[:, 0]]
    for column in range(1, suffix_len.shape[1]):
        running.append(running[-1] + suffix_len[:, column])
    end_slots = jnp.stack(running, axis=1)
    start_slots = end_slots - suffix_len
    slot_ids = jnp.arange(slot_count)
    inside = (slot_ids[None, None, :] >= start_slots[:, :, None]) & (
        slot_ids[None, None, :] < end_slots[:, :, None]
    )
    request_ids = jnp.arange(suffix_len.shape[1])
    slot_valid = jnp.any(inside, axis=1)
    request = jnp.sum(jnp.where(inside, request_ids[None, :, None], 0), axis=1)
    offset = slot_ids[None, :] - jnp.sum(jnp.where(inside, start_slots[:, :, None], 0), axis=1)
    group_id = jnp.where(
        slot_valid, jnp.sum(jnp.where(inside, request_group[:, :, None], 0), axis=1), -1
    )
    return (slot_valid, request, offset, group_id)


def prefix_block(query_block, group_block, prefix_keys, prefix_values, key_group, score_scale):
    row_count, model_width = query_block.shape
    head_dim = model_width // HEADS
    query_heads = query_block.reshape(row_count, HEADS, head_dim)
    key_heads = prefix_keys.reshape(-1, HEADS, head_dim)
    value_heads = prefix_values.reshape(-1, HEADS, head_dim)
    scores = (
        jnp.einsum("qhd,khd->qhk", query_heads, key_heads, preferred_element_type=jnp.float32)
        * score_scale
    )
    allowed = group_block[:, None] == key_group[None, :]
    weights = jnp.where(allowed[:, None, :], jnp.exp(scores), 0.0)
    weight_sum = jnp.sum(weights, axis=-1)
    summed = jnp.einsum(
        "qhk,khd->qhd",
        weights.astype(jnp.bfloat16),
        value_heads,
        preferred_element_type=jnp.float32,
    )
    return (summed.reshape(row_count, model_width), weight_sum)


def shards_columns(
    hidden_in,
    w_qkv,
    w_out,
    w_gate_up,
    w_down,
    scale_qk,
    scale_gate_up,
    eigen_rates,
    cache_keys,
    cache_values,
    page_table,
    request_group,
    suffix_len,
):
    slot_count, model_width = hidden_in.shape
    head_dim = model_width // HEADS
    score_scale = 1.0 / math.sqrt(head_dim)
    mp_count = lax.axis_size("mp")
    mp_index = lax.axis_index("mp")
    own_rows = slot_count // mp_count
    row_first = mp_index * own_rows
    shard_index = lax.axis_index("pages")
    pages_here, page_len = (cache_keys.shape[0], cache_keys.shape[1])
    pool_pages = page_table.shape[0]
    prefix_pages = pool_pages // GROUPS
    slot_valid, request, offset, group_id = slot_tables(suffix_len, request_group, slot_count)
    live_shard = lax.dynamic_index_in_dim(slot_valid, shard_index, 0, keepdims=False)
    request_shard = lax.dynamic_index_in_dim(request, shard_index, 0, keepdims=False)
    offset_shard = lax.dynamic_index_in_dim(offset, shard_index, 0, keepdims=False)
    position_shard = prefix_pages * page_len + offset_shard
    live_own = lax.dynamic_slice_in_dim(live_shard, row_first, own_rows, 0)
    request_own = lax.dynamic_slice_in_dim(request_shard, row_first, own_rows, 0)
    offset_own = lax.dynamic_slice_in_dim(offset_shard, row_first, own_rows, 0)
    position_own = lax.dynamic_slice_in_dim(position_shard, row_first, own_rows, 0)
    state_in = rms_rows(hidden_in.astype(jnp.float32)).astype(jnp.bfloat16)
    projected = jnp.einsum(
        "sd,jdc->jsc", state_in, w_qkv, preferred_element_type=jnp.float32
    ).astype(jnp.bfloat16)
    columns = lax.all_gather(projected, "mp", axis=2, tiled=True)
    query_raw = lax.dynamic_slice_in_dim(columns[0], row_first, own_rows, 0)
    key_raw, value_rows = (columns[1], columns[2])
    queries = head_norm(
        rotate(query_raw.astype(jnp.float32), position_own, HEADS), scale_qk, HEADS
    ).astype(jnp.bfloat16)
    keys_new = head_norm(
        rotate(key_raw.astype(jnp.float32), position_shard, HEADS), scale_qk, HEADS
    ).astype(jnp.bfloat16)
    query_heads = queries.reshape(own_rows, HEADS, head_dim)
    scores = (
        jnp.einsum(
            "qhd,khd->hqk",
            query_heads,
            keys_new.reshape(slot_count, HEADS, head_dim),
            preferred_element_type=jnp.float32,
        )
        * score_scale
    )
    allowed = (
        (request_own[:, None] == request_shard[None, :])
        & (offset_shard[None, :] <= offset_own[:, None])
        & live_own[:, None]
        & live_shard[None, :]
    )
    weights = jnp.where(allowed[None], jnp.exp(scores), 0.0)
    suffix_total = jnp.sum(weights, axis=-1)
    suffix_sum = jnp.einsum(
        "hqk,khd->qhd",
        weights.astype(jnp.bfloat16),
        value_rows.reshape(slot_count, HEADS, head_dim),
        preferred_element_type=jnp.float32,
    )
    physical = shard_index * pages_here + jnp.arange(pages_here, dtype=jnp.int32)
    matches = page_table[:, None] == physical[None, :]
    logical = jnp.sum(
        jnp.where(matches, jnp.arange(pool_pages, dtype=jnp.int32)[:, None], 0), axis=0
    )
    key_group = jnp.repeat(logical // prefix_pages, page_len)
    prefix_keys = head_norm(
        cache_keys.reshape(pages_here * page_len, model_width).astype(jnp.float32), scale_qk, HEADS
    ).astype(jnp.bfloat16)
    prefix_values = cache_values.reshape(pages_here * page_len, model_width)
    gathered = lax.all_gather(queries, "pages", axis=0, tiled=True)
    gathered_group = lax.dynamic_slice_in_dim(group_id, row_first, own_rows, 1).reshape(-1)
    row_count = own_rows * lax.axis_size("pages")
    block_rows = row_count if row_count <= 512 else math.gcd(row_count, 512)

    def attend_block(block_first):
        query_block = lax.dynamic_slice_in_dim(gathered, block_first, block_rows, 0)
        group_block = lax.dynamic_slice_in_dim(gathered_group, block_first, block_rows, 0)
        return prefix_block(
            query_block, group_block, prefix_keys, prefix_values, key_group, score_scale
        )

    block_starts = jnp.arange(row_count // block_rows, dtype=jnp.int32) * block_rows
    summed, weight_sum = lax.map(attend_block, block_starts)
    prefix_sum, prefix_total = lax.psum_scatter(
        (summed.reshape(row_count, model_width), weight_sum.reshape(row_count, HEADS)),
        "pages",
        scatter_dimension=0,
        tiled=True,
    )
    denominator = suffix_total.T + prefix_total + (1.0 - live_own.astype(jnp.float32))[:, None]
    mixed = (suffix_sum + prefix_sum.reshape(own_rows, HEADS, head_dim)) / denominator[:, :, None]
    attention = mixed.reshape(own_rows, model_width).astype(jnp.bfloat16)
    projected_out = jnp.dot(
        lax.all_gather(attention, "mp", axis=0, tiled=True),
        w_out,
        preferred_element_type=jnp.float32,
    )
    residual_in = state_in.astype(jnp.float32)
    state_mid = rms_rows(
        residual_in + eigen_rates[0][None, :] * (rms_rows(projected_out) - residual_in)
    ).astype(jnp.bfloat16)
    state_own = lax.dynamic_slice_in_dim(state_mid, row_first, own_rows, 0)
    gate_up = jnp.einsum("sd,jdf->jsf", state_mid, w_gate_up, preferred_element_type=jnp.float32)
    hidden = (
        jax.nn.silu(scale_gate_up[0][None, :] * gate_up[0])
        * (scale_gate_up[1][None, :] * gate_up[1])
    ).astype(jnp.bfloat16)
    feed_sum = lax.psum_scatter(
        jnp.dot(hidden, w_down, preferred_element_type=jnp.float32),
        "mp",
        scatter_dimension=0,
        tiled=True,
    )
    middle = state_own.astype(jnp.float32)
    result = rms_rows(middle + eigen_rates[1][None, :] * (rms_rows(feed_sum) - middle))
    return (live_own.astype(jnp.float32)[:, None] * result).astype(jnp.bfloat16)


def shards_heads(
    hidden_in,
    w_qkv,
    w_out,
    w_gate_up,
    w_down,
    scale_qk,
    scale_gate_up,
    eigen_rates,
    cache_keys,
    cache_values,
    page_table,
    request_group,
    suffix_len,
):
    slot_count, model_width = hidden_in.shape
    head_dim = model_width // HEADS
    score_scale = 1.0 / math.sqrt(head_dim)
    mp_count = lax.axis_size("mp")
    mp_index = lax.axis_index("mp")
    local_heads = HEADS // mp_count
    local_width = local_heads * head_dim
    own_rows = slot_count // mp_count
    row_first = mp_index * own_rows
    shard_index = lax.axis_index("pages")
    pages_here, page_len = (cache_keys.shape[0], cache_keys.shape[1])
    pool_pages = page_table.shape[0]
    prefix_pages = pool_pages // GROUPS
    slot_valid, request, offset, group_id = slot_tables(suffix_len, request_group, slot_count)
    live_shard = lax.dynamic_index_in_dim(slot_valid, shard_index, 0, keepdims=False)
    request_shard = lax.dynamic_index_in_dim(request, shard_index, 0, keepdims=False)
    offset_shard = lax.dynamic_index_in_dim(offset, shard_index, 0, keepdims=False)
    position_shard = prefix_pages * page_len + offset_shard
    live_own = lax.dynamic_slice_in_dim(live_shard, row_first, own_rows, 0)
    scale_local = lax.dynamic_slice_in_dim(scale_qk, mp_index * local_width, local_width, 0)
    state_in = rms_rows(hidden_in.astype(jnp.float32)).astype(jnp.bfloat16)
    projected_query = jnp.dot(state_in, w_qkv[0], preferred_element_type=jnp.float32).astype(
        jnp.bfloat16
    )
    queries = head_norm(
        rotate(projected_query.astype(jnp.float32), position_shard, local_heads),
        scale_local,
        local_heads,
    ).astype(jnp.bfloat16)
    gathered = lax.all_to_all(
        jnp.tile(queries, (lax.axis_size("pages"), 1)), "pages", 0, 0, tiled=True
    )
    physical = shard_index * pages_here + jnp.arange(pages_here, dtype=jnp.int32)
    matches = page_table[:, None] == physical[None, :]
    logical = jnp.sum(
        jnp.where(matches, jnp.arange(pool_pages, dtype=jnp.int32)[:, None], 0), axis=0
    )
    key_group = jnp.repeat(logical // prefix_pages, page_len)
    cache_local = lax.dynamic_slice_in_dim(cache_keys, mp_index * local_width, local_width, 2)
    prefix_keys = head_norm(
        cache_local.reshape(pages_here * page_len, local_width).astype(jnp.float32),
        scale_local,
        local_heads,
    ).astype(jnp.bfloat16)
    prefix_values = lax.dynamic_slice_in_dim(
        cache_values, mp_index * local_width, local_width, 2
    ).reshape(pages_here * page_len, local_width)
    pages_count = lax.axis_size("pages")
    key_heads = prefix_keys.reshape(-1, local_heads, head_dim)
    value_heads = prefix_values.reshape(-1, local_heads, head_dim)
    gathered_heads = gathered.reshape(pages_count, slot_count, local_heads, head_dim)
    chunk_count = 2 if pages_count % 2 == 0 else 1
    chunk_pages = pages_count // chunk_count
    pieces = []
    for chunk in range(chunk_count):
        query_chunk = lax.slice_in_dim(
            gathered_heads, chunk * chunk_pages, (chunk + 1) * chunk_pages, axis=0
        )
        group_chunk = lax.slice_in_dim(
            group_id, chunk * chunk_pages, (chunk + 1) * chunk_pages, axis=0
        )
        prefix_scores = (
            jnp.einsum(
                "pshd,khd->phks", query_chunk, key_heads, preferred_element_type=jnp.float32
            )
            * score_scale
        )
        prefix_allowed = key_group[None, :, None] == group_chunk[:, None, :]
        prefix_weights = jnp.where(prefix_allowed[:, None], jnp.exp(prefix_scores), 0.0)
        weight_sum = jnp.sum(prefix_weights, axis=2)
        summed = jnp.einsum(
            "phks,khd->pshd",
            prefix_weights.astype(jnp.bfloat16),
            value_heads,
            preferred_element_type=jnp.float32,
        )
        pieces.append(
            jnp.concatenate(
                [
                    summed.reshape(chunk_pages, slot_count, local_width),
                    jnp.transpose(weight_sum, (0, 2, 1)),
                ],
                axis=2,
            ).astype(jnp.bfloat16)
        )
    state_kv = state_in + jnp.zeros_like(state_in) * pieces[0][0, 0, 0]
    projected = jnp.einsum(
        "sd,jdc->jsc", state_kv, w_qkv[1:], preferred_element_type=jnp.float32
    ).astype(jnp.bfloat16)
    keys_new = head_norm(
        rotate(projected[0].astype(jnp.float32), position_shard, local_heads), scale_local, local_heads
    ).astype(jnp.bfloat16)
    value_rows = projected[1]
    scores = (
        jnp.einsum(
            "qhd,khd->hqk",
            queries.reshape(slot_count, local_heads, head_dim),
            keys_new.reshape(slot_count, local_heads, head_dim),
            preferred_element_type=jnp.float32,
        )
        * score_scale
    )
    allowed = (
        (request_shard[:, None] == request_shard[None, :])
        & (offset_shard[None, :] <= offset_shard[:, None])
        & live_shard[:, None]
        & live_shard[None, :]
    )
    weights = jnp.where(allowed[None], jnp.exp(scores), 0.0)
    suffix_total = jnp.sum(weights, axis=-1)
    suffix_sum = jnp.einsum(
        "hqk,khd->qhd",
        weights.astype(jnp.bfloat16),
        value_rows.reshape(slot_count, local_heads, head_dim),
        preferred_element_type=jnp.float32,
    )
    prefix_parts = lax.all_to_all(
        jnp.concatenate(pieces, axis=0).reshape(pages_count * slot_count, local_width + local_heads),
        "pages",
        0,
        0,
        tiled=True,
    )
    prefix_both = jnp.sum(
        prefix_parts.reshape(pages_count, slot_count, local_width + local_heads).astype(jnp.float32),
        axis=0,
    )
    prefix_sum = prefix_both[:, :local_width]
    prefix_total = prefix_both[:, local_width:]
    denominator = suffix_total.T + prefix_total + (1.0 - live_shard.astype(jnp.float32))[:, None]
    mixed = (suffix_sum + prefix_sum.reshape(slot_count, local_heads, head_dim)) / denominator[
        :, :, None
    ]
    attention_local = mixed.reshape(slot_count, local_width).astype(jnp.bfloat16)
    attention = lax.all_gather(attention_local, "mp", axis=1, tiled=True)
    projected_out = jnp.dot(attention, w_out, preferred_element_type=jnp.float32)
    residual_in = state_in.astype(jnp.float32)
    state_mid = rms_rows(
        residual_in + eigen_rates[0][None, :] * (rms_rows(projected_out) - residual_in)
    ).astype(jnp.bfloat16)
    state_own = lax.dynamic_slice_in_dim(state_mid, row_first, own_rows, 0)
    gate_up = jnp.einsum("sd,jdf->jsf", state_mid, w_gate_up, preferred_element_type=jnp.float32)
    hidden = (
        jax.nn.silu(scale_gate_up[0][None, :] * gate_up[0])
        * (scale_gate_up[1][None, :] * gate_up[1])
    ).astype(jnp.bfloat16)
    feed_parts = lax.all_to_all(
        jnp.dot(hidden, w_down, preferred_element_type=jnp.float32).astype(jnp.bfloat16),
        "mp",
        0,
        0,
        tiled=True,
    )
    feed_sum = jnp.sum(
        feed_parts.reshape(mp_count, own_rows, model_width).astype(jnp.float32), axis=0
    )
    middle = state_own.astype(jnp.float32)
    result = rms_rows(middle + eigen_rates[1][None, :] * (rms_rows(feed_sum) - middle))
    return (live_own.astype(jnp.float32)[:, None] * result).astype(jnp.bfloat16)


def solution(mesh):
    shards = shards_heads if HEADS % mesh.shape["mp"] == 0 else shards_columns
    return jax.shard_map(
        shards,
        mesh=mesh,
        in_specs=(
            P("pages", None),
            P(None, None, "mp"),
            P(),
            P(None, None, "mp"),
            P("mp", None),
            P(),
            P(None, "mp"),
            P(),
            P("pages", None, None),
            P("pages", None, None),
            P(),
            P(),
            P(),
        ),
        out_specs=P(("pages", "mp"), None),
        check_vma=False,
    )
```
